32 devices in a mesh: row: 4 (over y, core), col: 8 (over z, x).
Axes of the slice: x: 2, y: 2, z: 4, core: 2. Of those that a mesh axis runs over, the one named last changes fastest.
Arguments:
- bands: float32 [2, 12, 32, 1024], P(None, None, 'row', 'col'), may hold values from -500 to 500
- directions: float32 [2, 12, 32, 1024], P(None, None, 'row', 'col'), may hold values from -500 to 500
- materials: int32 [32, 1024], P('row', 'col'), may hold values from 0 to 7
- permittivity: float32 [8], replicated, may hold values from 1 to 12
- wavevector: int32 [2], replicated, may hold values from 0 to 15
Outputs:
- basis: float32 [2, 36, 32, 1024], P(None, None, 'row', 'col')
- reduced: float32 [2, 36, 36], replicated
The draws below stay inside these ranges and needn't reach their ends.
All inputs are finite; a program needn't handle non-finite values.
Results may differ from the reference program's by a relative error of at most 0.00018.
Values sent between devices are 32-bit elements; how exact they have to be, the bound alone decides.
No kernel may reach another device: no remote copies, remote signals or barrier semaphores. Data moves between devices by JAX's collectives and lax.ppermute only.
A program may use at most 64 MiB of HBM per device.

```python
import math
import jax
import jax.numpy as jnp
from jax import lax

NB = 12
NMAT = 8
KDEN = 16
NS_STEPS = 5
NR = 32
NC = 1024


def draw_common(key):
    full_shape = (2, 2 * NB + 1, NR, NC)
    row_steps = jnp.arange(NR, dtype=jnp.float32)
    col_steps = jnp.arange(NC, dtype=jnp.float32)
    band_steps = jnp.arange(NB, dtype=jnp.float32)
    samples = jnp.clip(jax.random.normal(key, full_shape, jnp.float32), -4.0, 4.0)
    across = (row_steps + 0.5) / NR
    sideways = (col_steps + 0.5) / NC
    envelope = 3.0 ** (across[:, None] + sideways[None, :])
    column_scale = 10.0 ** (0.5 * band_steps / (NB - 1))
    band_samples = samples[:, :NB]
    direction_samples = samples[:, NB:2 * NB]
    bands = column_scale[None, :, None, None] * envelope[None, None] * (band_samples + 0.5 * jnp.roll(band_samples, -1, axis=1))
    directions = column_scale[::-1][None, :, None, None] * envelope[None, None] * (direction_samples + 0.6 * band_samples)
    return (bands, directions)


def draw_bands(key, part):
    return draw_common(jax.random.fold_in(key, 11))[0].astype(jnp.float32)


def draw_directions(key, part):
    return draw_common(jax.random.fold_in(key, 11))[1].astype(jnp.float32)


def touch_ends(drawn, key, smallest, top_value):
    extent = drawn.shape
    spot = [jax.random.randint(jax.random.fold_in(key, axis), (), 0, extent[axis]) for axis in range(len(extent))]
    drawn = drawn.at[tuple(spot)].set(smallest)
    longest = extent.index(max(extent))
    spot[longest] = (spot[longest] + 1) % extent[longest]
    return drawn.at[tuple(spot)].set(top_value)


def setup_inputs(seed: int = 0) -> dict:
    key_list = jax.random.split(jax.random.key(seed), 6)
    return {
        "bands": draw_bands(jax.random.fold_in(key_list[5], 71), 0),
        "directions": draw_directions(jax.random.fold_in(key_list[5], 71), 0),
        "materials": touch_ends(jax.random.randint(key_list[2], (NR, NC), 0, NMAT), jax.random.fold_in(key_list[2], 1), 0, NMAT - 1).astype(jnp.int32),
        "permittivity": jnp.clip(jnp.exp(jax.random.uniform(key_list[3], (NMAT,), jnp.float32, math.log(1.0), math.log(12.0))), 1.0, 12.0),
        "wavevector": jax.random.randint(key_list[4], (2,), 0, KDEN).astype(jnp.int32),
    }


def rotate(values, phase_angle):
    cosine = jnp.cos(phase_angle)
    sine_part = jnp.sin(phase_angle)
    return jnp.stack([values[0] * cosine - values[1] * sine_part, values[0] * sine_part + values[1] * cosine])

def coupling(stiffness):
    upward = 0.5 * (stiffness + jnp.roll(stiffness, 1, axis=0))
    downward = 0.5 * (stiffness + jnp.roll(stiffness, -1, axis=0))
    leftward = 0.5 * (stiffness + jnp.roll(stiffness, 1, axis=1))
    rightward = 0.5 * (stiffness + jnp.roll(stiffness, -1, axis=1))
    return (upward, downward, leftward, rightward)

def apply_column(column, weights, angle_row, angle_col):
    upward, downward, leftward, rightward = weights
    above_cells = jnp.roll(column, 1, axis=1)
    above_cells = above_cells.at[:, 0].set(rotate(above_cells[:, 0], -angle_row))
    below_cells = jnp.roll(column, -1, axis=1)
    below_cells = below_cells.at[:, -1].set(rotate(below_cells[:, -1], angle_row))
    before = jnp.roll(column, 1, axis=2)
    before = before.at[:, :, 0].set(rotate(before[:, :, 0], -angle_col))
    after_cells = jnp.roll(column, -1, axis=2)
    after_cells = after_cells.at[:, :, -1].set(rotate(after_cells[:, :, -1], angle_col))
    diagonal = upward + downward + leftward + rightward
    return diagonal * column - (upward * above_cells + downward * below_cells + leftward * before + rightward * after_cells)

def operate(field, weights, angle_row, angle_col):
    columns = jnp.moveaxis(field, 1, 0)
    result = lax.map(lambda column: apply_column(column, weights, angle_row, angle_col), columns)
    return jnp.moveaxis(result, 0, 1)

def complex_gram(first_block, second_block):
    highest = lax.Precision.HIGHEST
    first_flat = first_block.reshape(first_block.shape[0], first_block.shape[1], -1)
    second_flat = second_block.reshape(second_block.shape[0], second_block.shape[1], -1)
    real_part = jnp.einsum('pjc,pkc->jk', first_flat, second_flat, precision=highest)
    imag_part = jnp.einsum('jc,kc->jk', first_flat[0], second_flat[1], precision=highest) - jnp.einsum('jc,kc->jk', first_flat[1], second_flat[0], precision=highest)
    return (real_part, imag_part)

def inverse_root(gram_real, gram_imag):
    highest = lax.Precision.HIGHEST
    order_size = gram_real.shape[0]
    upper_half = jnp.concatenate([gram_real, -gram_imag], axis=1)
    lower_half = jnp.concatenate([gram_imag, gram_real], axis=1)
    embedded = jnp.concatenate([upper_half, lower_half], axis=0)
    magnitude = jnp.sqrt(jnp.sum(embedded * embedded))
    identity = jnp.eye(2 * order_size, dtype=embedded.dtype)

    def newton(turn_index, carried):
        current, inverse = carried
        factor = 1.5 * identity - 0.5 * jnp.dot(inverse, current, precision=highest)
        return (jnp.dot(current, factor, precision=highest), jnp.dot(factor, inverse, precision=highest))
    current, inverse = lax.fori_loop(0, NS_STEPS, newton, (embedded / magnitude, identity))
    root_full = inverse / jnp.sqrt(magnitude)
    return (root_full[:order_size, :order_size], root_full[order_size:, :order_size])

def reduce_matrix(root_real, root_imag, ham_real, ham_imag):
    highest = lax.Precision.HIGHEST
    prod_real = jnp.dot(ham_real, root_real, precision=highest) - jnp.dot(ham_imag, root_imag, precision=highest)
    prod_imag = jnp.dot(ham_real, root_imag, precision=highest) + jnp.dot(ham_imag, root_real, precision=highest)
    red_real = jnp.dot(root_real.T, prod_real, precision=highest) + jnp.dot(root_imag.T, prod_imag, precision=highest)
    red_imag = jnp.dot(root_real.T, prod_imag, precision=highest) - jnp.dot(root_imag.T, prod_real, precision=highest)
    return jnp.stack([red_real, red_imag])

def rotate_basis(raw_basis, root_real, root_imag, scale_factor):
    highest = lax.Precision.HIGHEST
    basis_real = jnp.einsum('jrc,jk->krc', raw_basis[0], root_real, precision=highest) - jnp.einsum('jrc,jk->krc', raw_basis[1], root_imag, precision=highest)
    basis_imag = jnp.einsum('jrc,jk->krc', raw_basis[0], root_imag, precision=highest) + jnp.einsum('jrc,jk->krc', raw_basis[1], root_real, precision=highest)
    return scale_factor * jnp.stack([basis_real, basis_imag])

def reference(bands, directions, materials, permittivity, wavevector):
    stiffness = 1.0 / permittivity[materials]
    angle_row = 2.0 * math.pi * wavevector[0].astype(jnp.float32) / KDEN
    angle_col = 2.0 * math.pi * wavevector[1].astype(jnp.float32) / KDEN
    weights = coupling(stiffness)
    diagonal = weights[0] + weights[1] + weights[2] + weights[3]
    applied = operate(bands, weights, angle_row, angle_col)
    numerator = lax.optimization_barrier(jnp.sum(bands * applied, axis=(0, 2, 3)))
    denominator = lax.optimization_barrier(jnp.sum(bands * bands, axis=(0, 2, 3)))
    quotient = numerator / denominator
    precond = (applied - quotient[None, :, None, None] * bands) / diagonal
    raw_basis = jnp.concatenate([bands, precond, directions], axis=1)
    applied_rest = operate(jnp.concatenate([precond, directions], axis=1), weights, angle_row, angle_col)
    applied_raw = jnp.concatenate([applied, applied_rest], axis=1)
    gram_real, gram_imag = complex_gram(raw_basis, raw_basis)
    ham_real, ham_imag = complex_gram(raw_basis, applied_raw)
    root_real, root_imag = inverse_root(gram_real, gram_imag)
    basis = rotate_basis(raw_basis, root_real, root_imag, math.sqrt(NR * NC))
    reduced = reduce_matrix(root_real, root_imag, ham_real, ham_imag)
    return (basis, reduced)
```

```python
import math

import jax
import jax.numpy as jnp
from jax import lax
from jax.sharding import PartitionSpec as P

KDEN = 16
NS_STEPS = 5


def rotate(values, phase_angle):
    cosine = jnp.cos(phase_angle)
    sine_part = jnp.sin(phase_angle)
    return jnp.stack(
        [values[0] * cosine - values[1] * sine_part, values[0] * sine_part + values[1] * cosine]
    )


def stencil(padded, stiff_pad):
    centre = stiff_pad[1:-1, 1:-1]
    upward = 0.5 * (centre + stiff_pad[:-2, 1:-1])
    downward = 0.5 * (centre + stiff_pad[2:, 1:-1])
    leftward = 0.5 * (centre + stiff_pad[1:-1, :-2])
    rightward = 0.5 * (centre + stiff_pad[1:-1, 2:])
    diagonal = upward + downward + leftward + rightward
    inner_cells = padded[:, :, 1:-1, 1:-1]
    neighbours = (
        upward * padded[:, :, :-2, 1:-1]
        + downward * padded[:, :, 2:, 1:-1]
        + leftward * padded[:, :, 1:-1, :-2]
        + rightward * padded[:, :, 1:-1, 2:]
    )
    return (diagonal * inner_cells - neighbours, diagonal)


def complex_gram(first_block, second_block):
    highest = lax.Precision.HIGHEST
    first_flat = first_block.reshape(first_block.shape[0], first_block.shape[1], -1)
    second_flat = second_block.reshape(second_block.shape[0], second_block.shape[1], -1)
    real_part = jnp.einsum("pjc,pkc->jk", first_flat, second_flat, precision=highest)
    imag_part = jnp.einsum(
        "jc,kc->jk", first_flat[0], second_flat[1], precision=highest
    ) - jnp.einsum("jc,kc->jk", first_flat[1], second_flat[0], precision=highest)
    return (real_part, imag_part)


def inverse_root(gram_real, gram_imag):
    highest = lax.Precision.HIGHEST
    order_size = gram_real.shape[0]
    upper_half = jnp.concatenate([gram_real, -gram_imag], axis=1)
    lower_half = jnp.concatenate([gram_imag, gram_real], axis=1)
    embedded = jnp.concatenate([upper_half, lower_half], axis=0)
    magnitude = jnp.sqrt(jnp.sum(embedded * embedded))
    identity = jnp.eye(2 * order_size, dtype=embedded.dtype)

    def newton(turn_index, carried):
        current, inverse = carried
        factor = 1.5 * identity - 0.5 * jnp.dot(inverse, current, precision=highest)
        return (
            jnp.dot(current, factor, precision=highest),
            jnp.dot(factor, inverse, precision=highest),
        )

    current, inverse = lax.fori_loop(0, NS_STEPS, newton, (embedded / magnitude, identity))
    root_full = inverse / jnp.sqrt(magnitude)
    return (root_full[:order_size, :order_size], root_full[order_size:, :order_size])


def reduce_matrix(root_real, root_imag, ham_real, ham_imag):
    highest = lax.Precision.HIGHEST
    prod_real = jnp.dot(ham_real, root_real, precision=highest) - jnp.dot(
        ham_imag, root_imag, precision=highest
    )
    prod_imag = jnp.dot(ham_real, root_imag, precision=highest) + jnp.dot(
        ham_imag, root_real, precision=highest
    )
    red_real = jnp.dot(root_real.T, prod_real, precision=highest) + jnp.dot(
        root_imag.T, prod_imag, precision=highest
    )
    red_imag = jnp.dot(root_real.T, prod_imag, precision=highest) - jnp.dot(
        root_imag.T, prod_real, precision=highest
    )
    return jnp.stack([red_real, red_imag])


def rotate_basis(raw_basis, root_real, root_imag, scale_factor):
    highest = lax.Precision.HIGHEST
    basis_real = jnp.einsum("jrc,jk->krc", raw_basis[0], root_real, precision=highest) - jnp.einsum(
        "jrc,jk->krc", raw_basis[1], root_imag, precision=highest
    )
    basis_imag = jnp.einsum("jrc,jk->krc", raw_basis[0], root_imag, precision=highest) + jnp.einsum(
        "jrc,jk->krc", raw_basis[1], root_real, precision=highest
    )
    return scale_factor * jnp.stack([basis_real, basis_imag])


def project_mixing(mixing, matrix):
    highest = lax.Precision.HIGHEST
    return jnp.dot(mixing.T, jnp.dot(matrix, mixing, precision=highest), precision=highest)


def exchange_rim(cells, axis, dim, width, low_angle, high_angle):
    count = lax.axis_size(axis)
    head = lax.slice_in_dim(cells, 0, width, axis=dim)
    tail = lax.slice_in_dim(cells, cells.shape[dim] - width, cells.shape[dim], axis=dim)
    before = lax.ppermute(tail, axis, [(i, (i + 1) % count) for i in range(count)])
    after = lax.ppermute(head, axis, [((i + 1) % count, i) for i in range(count)])
    return jnp.concatenate(
        [rotate_rim(before, low_angle), cells, rotate_rim(after, high_angle)], axis=dim
    )


def rotate_rim(rim, phase_angle):
    field_part = rim[:-1].reshape((2, -1) + rim.shape[1:])
    turned = rotate(field_part, phase_angle).reshape((-1,) + rim.shape[1:])
    return jnp.concatenate([turned, rim[-1:]], axis=0)


def tree_sum(value, axis):
    count = lax.axis_size(axis)
    if count & (count - 1):
        return lax.psum(value, axis)
    step = 1
    while step < count:
        value = value + lax.ppermute(value, axis, [(i, i ^ step) for i in range(count)])
        step *= 2
    return value


def pack_hermitian(real_part, imag_part):
    order_size = real_part.shape[0]
    upper = jnp.arange(order_size)[:, None] <= jnp.arange(order_size)[None, :]
    return jnp.where(upper, real_part, imag_part)


def unpack_hermitian(packed):
    order_size = packed.shape[0]
    upper = jnp.arange(order_size)[:, None] <= jnp.arange(order_size)[None, :]
    strict_upper = jnp.arange(order_size)[:, None] < jnp.arange(order_size)[None, :]
    real_upper = jnp.where(upper, packed, 0.0)
    real_part = real_upper + jnp.where(strict_upper, packed, 0.0).T
    imag_lower = jnp.where(upper, 0.0, packed)
    return (real_part, imag_lower - imag_lower.T)


def body(bands, directions, materials, permittivity, wavevector):
    band_count = bands.shape[1]
    height = bands.shape[2]
    breadth = bands.shape[3]
    levels = jnp.arange(permittivity.shape[0], dtype=jnp.int32)
    stiffness = jnp.sum(
        jnp.where(
            materials[None] == levels[:, None, None], (1.0 / permittivity)[:, None, None], 0.0
        ),
        axis=0,
    )
    angle_row = 2.0 * math.pi * wavevector[0].astype(jnp.float32) / KDEN
    angle_col = 2.0 * math.pi * wavevector[1].astype(jnp.float32) / KDEN
    row_index = lax.axis_index("row")
    col_index = lax.axis_index("col")
    fields = jnp.concatenate([bands, directions], axis=1)
    packed = jnp.concatenate(
        [fields.reshape(4 * band_count, height, breadth), stiffness[None]], axis=0
    )
    padded = exchange_rim(
        packed,
        "row",
        1,
        2,
        jnp.where(row_index == 0, -angle_row, 0.0),
        jnp.where(row_index == lax.axis_size("row") - 1, angle_row, 0.0),
    )
    padded = exchange_rim(
        padded,
        "col",
        2,
        2,
        jnp.where(col_index == 0, -angle_col, 0.0),
        jnp.where(col_index == lax.axis_size("col") - 1, angle_col, 0.0),
    )
    stiff_wide = padded[-1]
    field_wide = padded[:-1].reshape(2, 2 * band_count, height + 4, breadth + 4)
    band_wide = field_wide[:, :band_count]
    applied_ring, diagonal_ring = stencil(band_wide, stiff_wide)
    stiff_ring = stiff_wide[1:-1, 1:-1]
    scaled_ring = jnp.concatenate(
        [
            applied_ring / diagonal_ring,
            band_wide[:, :, 1:-1, 1:-1] / diagonal_ring,
            field_wide[:, band_count:, 1:-1, 1:-1],
        ],
        axis=1,
    )
    extra_applied = stencil(scaled_ring, stiff_ring)[0]
    applied_cycle = applied_ring[:, :, 1:-1, 1:-1]
    scaled_image = scaled_ring[:, :band_count, 1:-1, 1:-1]
    scaled_bands = scaled_ring[:, band_count : 2 * band_count, 1:-1, 1:-1]
    extended = jnp.concatenate([bands, scaled_image, scaled_bands, directions], axis=1)
    extended_applied = jnp.concatenate([applied_cycle, extra_applied], axis=1)
    local_gram = complex_gram(extended, extended)
    local_ham = complex_gram(extended, extended_applied)
    summed = jnp.stack([pack_hermitian(*local_gram), pack_hermitian(*local_ham)])
    summed = tree_sum(tree_sum(summed, "row"), "col")
    gram_whole, gram_imag_whole = unpack_hermitian(summed[0])
    ham_whole, ham_imag_whole = unpack_hermitian(summed[1])
    quotient = jnp.diagonal(ham_whole)[:band_count] / jnp.diagonal(gram_whole)[:band_count]
    identity = jnp.eye(band_count, dtype=jnp.float32)
    zeros_block = jnp.zeros((band_count, band_count), jnp.float32)
    mixing = jnp.concatenate(
        [
            jnp.concatenate([identity, zeros_block, zeros_block], axis=1),
            jnp.concatenate([zeros_block, identity, zeros_block], axis=1),
            jnp.concatenate([zeros_block, -jnp.diag(quotient), zeros_block], axis=1),
            jnp.concatenate([zeros_block, zeros_block, identity], axis=1),
        ],
        axis=0,
    )
    gram_real = project_mixing(mixing, gram_whole)
    gram_imag = project_mixing(mixing, gram_imag_whole)
    ham_real = project_mixing(mixing, ham_whole)
    ham_imag = project_mixing(mixing, ham_imag_whole)
    precond = scaled_image - quotient[None, :, None, None] * scaled_bands
    raw_basis = jnp.concatenate([bands, precond, directions], axis=1)
    root_real, root_imag = inverse_root(gram_real, gram_imag)
    scale_factor = math.sqrt(height * breadth * lax.axis_size("row") * lax.axis_size("col"))
    basis = rotate_basis(raw_basis, root_real, root_imag, scale_factor)
    reduced = reduce_matrix(root_real, root_imag, ham_real, ham_imag)
    return (basis, reduced)


def solution(mesh):
    placed = (P(None, None, "row", "col"), P(None, None, "row", "col"), P("row", "col"), P(), P())
    return jax.shard_map(
        body,
        mesh=mesh,
        in_specs=placed,
        out_specs=(P(None, None, "row", "col"), P()),
        check_vma=False,
    )
```

```python
import math

import jax
import jax.numpy as jnp
from jax import lax
from jax.sharding import PartitionSpec as P

KDEN = 16
NS_STEPS = 5


def rotate(values, phase_angle):
    cosine = jnp.cos(phase_angle)
    sine_part = jnp.sin(phase_angle)
    return jnp.stack(
        [values[0] * cosine - values[1] * sine_part, values[0] * sine_part + values[1] * cosine]
    )


def stencil(padded, stiff_pad):
    centre = stiff_pad[1:-1, 1:-1]
    upward = 0.5 * (centre + stiff_pad[:-2, 1:-1])
    downward = 0.5 * (centre + stiff_pad[2:, 1:-1])
    leftward = 0.5 * (centre + stiff_pad[1:-1, :-2])
    rightward = 0.5 * (centre + stiff_pad[1:-1, 2:])
    diagonal = upward + downward + leftward + rightward
    inner_cells = padded[:, :, 1:-1, 1:-1]
    neighbours = (
        upward * padded[:, :, :-2, 1:-1]
        + downward * padded[:, :, 2:, 1:-1]
        + leftward * padded[:, :, 1:-1, :-2]
        + rightward * padded[:, :, 1:-1, 2:]
    )
    return (diagonal * inner_cells - neighbours, diagonal)


def complex_gram(first_block, second_block):
    highest = lax.Precision.HIGHEST
    first_flat = first_block.reshape(first_block.shape[0], first_block.shape[1], -1)
    second_flat = second_block.reshape(second_block.shape[0], second_block.shape[1], -1)
    real_part = jnp.einsum("pjc,pkc->jk", first_flat, second_flat, precision=highest)
    imag_part = jnp.einsum(
        "jc,kc->jk", first_flat[0], second_flat[1], precision=highest
    ) - jnp.einsum("jc,kc->jk", first_flat[1], second_flat[0], precision=highest)
    return (real_part, imag_part)


def inverse_root(gram_real, gram_imag):
    highest = lax.Precision.HIGHEST
    order_size = gram_real.shape[0]
    upper_half = jnp.concatenate([gram_real, -gram_imag], axis=1)
    lower_half = jnp.concatenate([gram_imag, gram_real], axis=1)
    embedded = jnp.concatenate([upper_half, lower_half], axis=0)
    magnitude = jnp.sqrt(jnp.sum(embedded * embedded))
    identity = jnp.eye(2 * order_size, dtype=embedded.dtype)

    def newton(turn_index, carried):
        current, inverse = carried
        factor = 1.5 * identity - 0.5 * jnp.dot(inverse, current, precision=highest)
        return (
            jnp.dot(current, factor, precision=highest),
            jnp.dot(factor, inverse, precision=highest),
        )

    current, inverse = lax.fori_loop(0, NS_STEPS, newton, (embedded / magnitude, identity))
    root_full = inverse / jnp.sqrt(magnitude)
    return (root_full[:order_size, :order_size], root_full[order_size:, :order_size])


def reduce_matrix(root_real, root_imag, ham_real, ham_imag):
    highest = lax.Precision.HIGHEST
    prod_real = jnp.dot(ham_real, root_real, precision=highest) - jnp.dot(
        ham_imag, root_imag, precision=highest
    )
    prod_imag = jnp.dot(ham_real, root_imag, precision=highest) + jnp.dot(
        ham_imag, root_real, precision=highest
    )
    red_real = jnp.dot(root_real.T, prod_real, precision=highest) + jnp.dot(
        root_imag.T, prod_imag, precision=highest
    )
    red_imag = jnp.dot(root_real.T, prod_imag, precision=highest) - jnp.dot(
        root_imag.T, prod_real, precision=highest
    )
    return jnp.stack([red_real, red_imag])


def rotate_basis(raw_basis, root_real, root_imag, scale_factor):
    highest = lax.Precision.HIGHEST
    basis_real = jnp.einsum("jrc,jk->krc", raw_basis[0], root_real, precision=highest) - jnp.einsum(
        "jrc,jk->krc", raw_basis[1], root_imag, precision=highest
    )
    basis_imag = jnp.einsum("jrc,jk->krc", raw_basis[0], root_imag, precision=highest) + jnp.einsum(
        "jrc,jk->krc", raw_basis[1], root_real, precision=highest
    )
    return scale_factor * jnp.stack([basis_real, basis_imag])


def project_mixing(mixing, matrix):
    highest = lax.Precision.HIGHEST
    return jnp.dot(mixing.T, jnp.dot(matrix, mixing, precision=highest), precision=highest)


def exchange_rim(cells, axis, dim, width, low_angle, high_angle):
    count = lax.axis_size(axis)
    head = lax.slice_in_dim(cells, 0, width, axis=dim)
    tail = lax.slice_in_dim(cells, cells.shape[dim] - width, cells.shape[dim], axis=dim)
    before = lax.ppermute(tail.reshape(-1), axis, [(i, (i + 1) % count) for i in range(count)])
    after = lax.ppermute(head.reshape(-1), axis, [((i + 1) % count, i) for i in range(count)])
    before = before.reshape(tail.shape)
    after = after.reshape(head.shape)
    return jnp.concatenate(
        [rotate_rim(before, low_angle), cells, rotate_rim(after, high_angle)], axis=dim
    )


def rotate_rim(rim, phase_angle):
    field_part = rim[:-1].reshape((2, -1) + rim.shape[1:])
    turned = rotate(field_part, phase_angle).reshape((-1,) + rim.shape[1:])
    return jnp.concatenate([turned, rim[-1:]], axis=0)


def tree_sum(value, axis):
    count = lax.axis_size(axis)
    if count & (count - 1):
        return lax.psum(value, axis)
    step = 1
    while step < count:
        value = value + lax.ppermute(value, axis, [(i, i ^ step) for i in range(count)])
        step *= 2
    return value


def pack_hermitian(real_part, imag_part):
    order_size = real_part.shape[0]
    upper = jnp.arange(order_size)[:, None] <= jnp.arange(order_size)[None, :]
    return jnp.where(upper, real_part, imag_part)


def unpack_hermitian(packed):
    order_size = packed.shape[0]
    upper = jnp.arange(order_size)[:, None] <= jnp.arange(order_size)[None, :]
    strict_upper = jnp.arange(order_size)[:, None] < jnp.arange(order_size)[None, :]
    real_upper = jnp.where(upper, packed, 0.0)
    real_part = real_upper + jnp.where(strict_upper, packed, 0.0).T
    imag_lower = jnp.where(upper, 0.0, packed)
    return (real_part, imag_lower - imag_lower.T)


def body(bands, directions, materials, permittivity, wavevector):
    band_count = bands.shape[1]
    height = bands.shape[2]
    breadth = bands.shape[3]
    levels = jnp.arange(permittivity.shape[0], dtype=jnp.int32)
    stiffness = jnp.sum(
        jnp.where(
            materials[None] == levels[:, None, None], (1.0 / permittivity)[:, None, None], 0.0
        ),
        axis=0,
    )
    angle_row = 2.0 * math.pi * wavevector[0].astype(jnp.float32) / KDEN
    angle_col = 2.0 * math.pi * wavevector[1].astype(jnp.float32) / KDEN
    row_index = lax.axis_index("row")
    col_index = lax.axis_index("col")
    fields = jnp.concatenate([bands, directions], axis=1)
    packed = jnp.concatenate(
        [fields.reshape(4 * band_count, height, breadth), stiffness[None]], axis=0
    )
    padded = exchange_rim(
        packed,
        "row",
        1,
        2,
        jnp.where(row_index == 0, -angle_row, 0.0),
        jnp.where(row_index == lax.axis_size("row") - 1, angle_row, 0.0),
    )
    padded = exchange_rim(
        padded,
        "col",
        2,
        2,
        jnp.where(col_index == 0, -angle_col, 0.0),
        jnp.where(col_index == lax.axis_size("col") - 1, angle_col, 0.0),
    )
    stiff_wide = padded[-1]
    field_wide = padded[:-1].reshape(2, 2 * band_count, height + 4, breadth + 4)
    band_wide = field_wide[:, :band_count]
    applied_ring, diagonal_ring = stencil(band_wide, stiff_wide)
    stiff_ring = stiff_wide[1:-1, 1:-1]
    scaled_ring = jnp.concatenate(
        [
            applied_ring / diagonal_ring,
            band_wide[:, :, 1:-1, 1:-1] / diagonal_ring,
            field_wide[:, band_count:, 1:-1, 1:-1],
        ],
        axis=1,
    )
    extra_applied = stencil(scaled_ring, stiff_ring)[0]
    applied_cycle = applied_ring[:, :, 1:-1, 1:-1]
    scaled_image = scaled_ring[:, :band_count, 1:-1, 1:-1]
    scaled_bands = scaled_ring[:, band_count : 2 * band_count, 1:-1, 1:-1]
    extended = jnp.concatenate([bands, scaled_image, scaled_bands, directions], axis=1)
    extended_applied = jnp.concatenate([applied_cycle, extra_applied], axis=1)
    local_gram = complex_gram(extended, extended)
    local_ham = complex_gram(extended, extended_applied)
    summed = jnp.stack([pack_hermitian(*local_gram), pack_hermitian(*local_ham)])
    summed = tree_sum(tree_sum(summed.reshape(-1), "row"), "col").reshape(summed.shape)
    gram_whole, gram_imag_whole = unpack_hermitian(summed[0])
    ham_whole, ham_imag_whole = unpack_hermitian(summed[1])
    quotient = jnp.diagonal(ham_whole)[:band_count] / jnp.diagonal(gram_whole)[:band_count]
    identity = jnp.eye(band_count, dtype=jnp.float32)
    zeros_block = jnp.zeros((band_count, band_count), jnp.float32)
    mixing = jnp.concatenate(
        [
            jnp.concatenate([identity, zeros_block, zeros_block], axis=1),
            jnp.concatenate([zeros_block, identity, zeros_block], axis=1),
            jnp.concatenate([zeros_block, -jnp.diag(quotient), zeros_block], axis=1),
            jnp.concatenate([zeros_block, zeros_block, identity], axis=1),
        ],
        axis=0,
    )
    gram_real = project_mixing(mixing, gram_whole)
    gram_imag = project_mixing(mixing, gram_imag_whole)
    ham_real = project_mixing(mixing, ham_whole)
    ham_imag = project_mixing(mixing, ham_imag_whole)
    precond = scaled_image - quotient[None, :, None, None] * scaled_bands
    raw_basis = jnp.concatenate([bands, precond, directions], axis=1)
    root_real, root_imag = inverse_root(gram_real, gram_imag)
    scale_factor = math.sqrt(height * breadth * lax.axis_size("row") * lax.axis_size("col"))
    basis = rotate_basis(raw_basis, root_real, root_imag, scale_factor)
    reduced = reduce_matrix(root_real, root_imag, ham_real, ham_imag)
    return (basis, reduced)


def solution(mesh):
    placed = (P(None, None, "row", "col"), P(None, None, "row", "col"), P("row", "col"), P(), P())
    return jax.shard_map(
        body,
        mesh=mesh,
        in_specs=placed,
        out_specs=(P(None, None, "row", "col"), P()),
        check_vma=False,
    )
```

```python
import functools
import math

import jax
import jax.numpy as jnp
from jax import lax
from jax.experimental import pallas as pl
from jax.experimental.pallas import tpu as pltpu
from jax.sharding import PartitionSpec as P

KDEN = 16
NS_STEPS = 5


def rotate(values, phase_angle):
    cosine = jnp.cos(phase_angle)
    sine_part = jnp.sin(phase_angle)
    return jnp.stack(
        [values[0] * cosine - values[1] * sine_part, values[0] * sine_part + values[1] * cosine]
    )


def stencil(padded, stiff_pad):
    centre = stiff_pad[1:-1, 1:-1]
    upward = 0.5 * (centre + stiff_pad[:-2, 1:-1])
    downward = 0.5 * (centre + stiff_pad[2:, 1:-1])
    leftward = 0.5 * (centre + stiff_pad[1:-1, :-2])
    rightward = 0.5 * (centre + stiff_pad[1:-1, 2:])
    diagonal = upward + downward + leftward + rightward
    inner_cells = padded[:, :, 1:-1, 1:-1]
    neighbours = (
        upward * padded[:, :, :-2, 1:-1]
        + downward * padded[:, :, 2:, 1:-1]
        + leftward * padded[:, :, 1:-1, :-2]
        + rightward * padded[:, :, 1:-1, 2:]
    )
    return (diagonal * inner_cells - neighbours, diagonal)


def complex_gram(first_block, second_block):
    highest = lax.Precision.HIGHEST
    first_flat = first_block.reshape(first_block.shape[0], first_block.shape[1], -1)
    second_flat = second_block.reshape(second_block.shape[0], second_block.shape[1], -1)
    real_part = jnp.einsum("pjc,pkc->jk", first_flat, second_flat, precision=highest)
    imag_part = jnp.einsum(
        "jc,kc->jk", first_flat[0], second_flat[1], precision=highest
    ) - jnp.einsum("jc,kc->jk", first_flat[1], second_flat[0], precision=highest)
    return (real_part, imag_part)


def inverse_root(gram_real, gram_imag):
    highest = lax.Precision.HIGHEST
    order_size = gram_real.shape[0]
    upper_half = jnp.concatenate([gram_real, -gram_imag], axis=1)
    lower_half = jnp.concatenate([gram_imag, gram_real], axis=1)
    embedded = jnp.concatenate([upper_half, lower_half], axis=0)
    magnitude = jnp.sqrt(jnp.sum(embedded * embedded))
    identity = jnp.eye(2 * order_size, dtype=embedded.dtype)

    def newton(turn_index, carried):
        current, inverse = carried
        factor = 1.5 * identity - 0.5 * jnp.dot(inverse, current, precision=highest)
        return (
            jnp.dot(current, factor, precision=highest),
            jnp.dot(factor, inverse, precision=highest),
        )

    current, inverse = lax.fori_loop(0, NS_STEPS, newton, (embedded / magnitude, identity))
    root_full = inverse / jnp.sqrt(magnitude)
    return (root_full[:order_size, :order_size], root_full[order_size:, :order_size])


def reduce_matrix(root_real, root_imag, ham_real, ham_imag):
    highest = lax.Precision.HIGHEST
    prod_real = jnp.dot(ham_real, root_real, precision=highest) - jnp.dot(
        ham_imag, root_imag, precision=highest
    )
    prod_imag = jnp.dot(ham_real, root_imag, precision=highest) + jnp.dot(
        ham_imag, root_real, precision=highest
    )
    red_real = jnp.dot(root_real.T, prod_real, precision=highest) + jnp.dot(
        root_imag.T, prod_imag, precision=highest
    )
    red_imag = jnp.dot(root_real.T, prod_imag, precision=highest) - jnp.dot(
        root_imag.T, prod_real, precision=highest
    )
    return jnp.stack([red_real, red_imag])


def rotate_basis(raw_basis, root_real, root_imag, scale_factor):
    highest = lax.Precision.HIGHEST
    basis_real = jnp.einsum("jrc,jk->krc", raw_basis[0], root_real, precision=highest) - jnp.einsum(
        "jrc,jk->krc", raw_basis[1], root_imag, precision=highest
    )
    basis_imag = jnp.einsum("jrc,jk->krc", raw_basis[0], root_imag, precision=highest) + jnp.einsum(
        "jrc,jk->krc", raw_basis[1], root_real, precision=highest
    )
    return scale_factor * jnp.stack([basis_real, basis_imag])


def project_mixing(mixing, matrix):
    highest = lax.Precision.HIGHEST
    return jnp.dot(mixing.T, jnp.dot(matrix, mixing, precision=highest), precision=highest)


def exchange_rim(cells, axis, dim, width, low_angle, high_angle):
    count = lax.axis_size(axis)
    head = lax.slice_in_dim(cells, 0, width, axis=dim)
    tail = lax.slice_in_dim(cells, cells.shape[dim] - width, cells.shape[dim], axis=dim)
    before = lax.ppermute(tail.reshape(-1), axis, [(i, (i + 1) % count) for i in range(count)])
    after = lax.ppermute(head.reshape(-1), axis, [((i + 1) % count, i) for i in range(count)])
    before = before.reshape(tail.shape)
    after = after.reshape(head.shape)
    return jnp.concatenate(
        [rotate_rim(before, low_angle), cells, rotate_rim(after, high_angle)], axis=dim
    )


def rotate_rim(rim, phase_angle):
    field_part = rim[:-1].reshape((2, -1) + rim.shape[1:])
    turned = rotate(field_part, phase_angle).reshape((-1,) + rim.shape[1:])
    return jnp.concatenate([turned, rim[-1:]], axis=0)


def tree_sum(value, axis):
    count = lax.axis_size(axis)
    if count & (count - 1):
        return lax.psum(value, axis)
    step = 1
    while step < count:
        value = value + lax.ppermute(value, axis, [(i, i ^ step) for i in range(count)])
        step *= 2
    return value


def pack_hermitian(real_part, imag_part):
    order_size = real_part.shape[0]
    upper = jnp.arange(order_size)[:, None] <= jnp.arange(order_size)[None, :]
    return jnp.where(upper, real_part, imag_part)


def unpack_hermitian(packed):
    order_size = packed.shape[0]
    upper = jnp.arange(order_size)[:, None] <= jnp.arange(order_size)[None, :]
    strict_upper = jnp.arange(order_size)[:, None] < jnp.arange(order_size)[None, :]
    real_upper = jnp.where(upper, packed, 0.0)
    real_part = real_upper + jnp.where(strict_upper, packed, 0.0).T
    imag_lower = jnp.where(upper, 0.0, packed)
    return (real_part, imag_lower - imag_lower.T)


def matrix_kernel(packed_ref, mix_ref, red_ref, work_ref, *, band_count):
    highest = lax.Precision.HIGHEST

    def dot(first, second):
        return jnp.dot(first, second, precision=highest, preferred_element_type=jnp.float32)

    size = work_ref.shape[-1]
    ext = packed_ref.shape[-1]
    raw = 3 * band_count
    half = size // 2
    work_ref[...] = jnp.zeros(work_ref.shape, jnp.float32)
    work_ref[0, :ext, :ext] = packed_ref[0]
    work_ref[1, :ext, :ext] = packed_ref[1]
    rows = lax.broadcasted_iota(jnp.int32, (size, size), 0)
    cols = lax.broadcasted_iota(jnp.int32, (size, size), 1)
    upper = rows <= cols
    strict = rows < cols
    eye = rows == cols

    def unpack(packed):
        real_part = jnp.where(upper, packed, 0.0) + jnp.where(strict, packed, 0.0).T
        lower = jnp.where(upper, 0.0, packed)
        return real_part, lower - lower.T

    gram_re, gram_im = unpack(work_ref[0])
    ham_re, ham_im = unpack(work_ref[1])
    band_diag = eye & (rows < band_count)
    quotient = jnp.where(band_diag, ham_re, 0.0) / jnp.where(band_diag, gram_re, 1.0)
    to_row = ((rows == cols + 2 * band_count) & (cols < band_count)).astype(jnp.float32)
    to_col = ((cols == rows + band_count) & (rows < band_count)).astype(jnp.float32)
    shifted = dot(dot(to_row, quotient), to_col)
    kept = (eye & (cols < 2 * band_count)) | (
        (rows == cols + band_count) & (cols >= 2 * band_count) & (cols < raw)
    )
    mixing = kept.astype(jnp.float32) - shifted
    mixing_t = mixing.T
    proj_re = dot(mixing_t, dot(gram_re, mixing))
    proj_im = dot(mixing_t, dot(gram_im, mixing))

    def spread(value, axis):
        return pltpu.roll(value, half, axis)

    embedded = proj_re + spread(spread(proj_re, 0), 1) - spread(proj_im, 1) + spread(proj_im, 0)
    active = (rows < raw) | ((rows >= half) & (rows < half + raw))
    identity = (eye & active).astype(jnp.float32)
    total = jnp.sum(jnp.sum(embedded * embedded, axis=0, keepdims=True), axis=1, keepdims=True)
    magnitude = jnp.sqrt(total)
    current = embedded / magnitude
    inverse = identity
    for _ in range(NS_STEPS):
        factor = 1.5 * identity - 0.5 * dot(inverse, current)
        current, inverse = dot(current, factor), dot(factor, inverse)
    root = inverse / jnp.sqrt(magnitude)
    corner = (rows < raw) & (cols < raw)
    root_re = jnp.where(corner, root, 0.0)
    root_im = jnp.where(corner, spread(root, 0), 0.0)
    mix_re = dot(mixing, root_re)
    mix_im = dot(mixing, root_im)
    image_re = dot(ham_re, mix_re) - dot(ham_im, mix_im)
    image_im = dot(ham_re, mix_im) + dot(ham_im, mix_re)
    mix_re_t = mix_re.T
    mix_im_t = mix_im.T
    mix_ref[0] = mix_re
    mix_ref[1] = mix_im
    red_ref[0] = dot(mix_re_t, image_re) + dot(mix_im_t, image_im)
    red_ref[1] = dot(mix_re_t, image_im) - dot(mix_im_t, image_re)


def matrix_stage(packed, band_count):
    size = 128
    vmem = pl.BlockSpec(memory_space=pltpu.VMEM)
    square = jax.ShapeDtypeStruct((2, size, size), jnp.float32)
    return pl.pallas_call(
        functools.partial(matrix_kernel, band_count=band_count),
        out_shape=(square, square),
        in_specs=[vmem],
        out_specs=(vmem, vmem),
        scratch_shapes=[pltpu.VMEM((2, size, size), jnp.float32)],
    )(packed)


def body(bands, directions, materials, permittivity, wavevector):
    band_count = bands.shape[1]
    height = bands.shape[2]
    breadth = bands.shape[3]
    levels = jnp.arange(permittivity.shape[0], dtype=jnp.int32)
    stiffness = jnp.sum(
        jnp.where(
            materials[None] == levels[:, None, None], (1.0 / permittivity)[:, None, None], 0.0
        ),
        axis=0,
    )
    angle_row = 2.0 * math.pi * wavevector[0].astype(jnp.float32) / KDEN
    angle_col = 2.0 * math.pi * wavevector[1].astype(jnp.float32) / KDEN
    row_index = lax.axis_index("row")
    col_index = lax.axis_index("col")
    fields = jnp.concatenate([bands, directions], axis=1)
    packed = jnp.concatenate(
        [fields.reshape(4 * band_count, height, breadth), stiffness[None]], axis=0
    )
    padded = exchange_rim(
        packed,
        "row",
        1,
        2,
        jnp.where(row_index == 0, -angle_row, 0.0),
        jnp.where(row_index == lax.axis_size("row") - 1, angle_row, 0.0),
    )
    padded = exchange_rim(
        padded,
        "col",
        2,
        2,
        jnp.where(col_index == 0, -angle_col, 0.0),
        jnp.where(col_index == lax.axis_size("col") - 1, angle_col, 0.0),
    )
    stiff_wide = padded[-1]
    field_wide = padded[:-1].reshape(2, 2 * band_count, height + 4, breadth + 4)
    band_wide = field_wide[:, :band_count]
    applied_ring, diagonal_ring = stencil(band_wide, stiff_wide)
    stiff_ring = stiff_wide[1:-1, 1:-1]
    scaled_ring = jnp.concatenate(
        [
            applied_ring / diagonal_ring,
            band_wide[:, :, 1:-1, 1:-1] / diagonal_ring,
            field_wide[:, band_count:, 1:-1, 1:-1],
        ],
        axis=1,
    )
    extra_applied = stencil(scaled_ring, stiff_ring)[0]
    applied_cycle = applied_ring[:, :, 1:-1, 1:-1]
    scaled_image = scaled_ring[:, :band_count, 1:-1, 1:-1]
    scaled_bands = scaled_ring[:, band_count : 2 * band_count, 1:-1, 1:-1]
    extended = jnp.concatenate([bands, scaled_image, scaled_bands, directions], axis=1)
    extended_applied = jnp.concatenate([applied_cycle, extra_applied], axis=1)
    local_gram = complex_gram(extended, extended)
    local_ham = complex_gram(extended, extended_applied)
    summed = jnp.stack([pack_hermitian(*local_gram), pack_hermitian(*local_ham)])
    summed = tree_sum(tree_sum(summed.reshape(-1), "row"), "col").reshape(summed.shape)
    mix, red = matrix_stage(summed, band_count)
    raw_count = 3 * band_count
    ext_count = 4 * band_count
    mix = mix[:, :ext_count, :raw_count]
    reduced = red[:, :raw_count, :raw_count]
    scale_factor = math.sqrt(height * breadth * lax.axis_size("row") * lax.axis_size("col"))
    basis = rotate_basis(extended, mix[0], mix[1], scale_factor)
    return (basis, reduced)


def solution(mesh):
    placed = (P(None, None, "row", "col"), P(None, None, "row", "col"), P("row", "col"), P(), P())
    return jax.shard_map(
        body,
        mesh=mesh,
        in_specs=placed,
        out_specs=(P(None, None, "row", "col"), P()),
        check_vma=False,
    )
```

```python
import functools
import math

import jax
import jax.numpy as jnp
from jax import lax
from jax.experimental import pallas as pl
from jax.experimental.pallas import tpu as pltpu
from jax.sharding import PartitionSpec as P

KDEN = 16
NS_STEPS = 5


def rotate(values, phase_angle):
    cosine = jnp.cos(phase_angle)
    sine_part = jnp.sin(phase_angle)
    return jnp.stack(
        [values[0] * cosine - values[1] * sine_part, values[0] * sine_part + values[1] * cosine]
    )


def stencil(padded, stiff_pad):
    centre = stiff_pad[1:-1, 1:-1]
    upward = 0.5 * (centre + stiff_pad[:-2, 1:-1])
    downward = 0.5 * (centre + stiff_pad[2:, 1:-1])
    leftward = 0.5 * (centre + stiff_pad[1:-1, :-2])
    rightward = 0.5 * (centre + stiff_pad[1:-1, 2:])
    diagonal = upward + downward + leftward + rightward
    inner_cells = padded[:, :, 1:-1, 1:-1]
    neighbours = (
        upward * padded[:, :, :-2, 1:-1]
        + downward * padded[:, :, 2:, 1:-1]
        + leftward * padded[:, :, 1:-1, :-2]
        + rightward * padded[:, :, 1:-1, 2:]
    )
    return (diagonal * inner_cells - neighbours, diagonal)


def complex_gram(first_block, second_block):
    highest = lax.Precision.HIGHEST
    first_flat = first_block.reshape(first_block.shape[0], first_block.shape[1], -1)
    second_flat = second_block.reshape(second_block.shape[0], second_block.shape[1], -1)
    real_part = jnp.einsum("pjc,pkc->jk", first_flat, second_flat, precision=highest)
    imag_part = jnp.einsum(
        "jc,kc->jk", first_flat[0], second_flat[1], precision=highest
    ) - jnp.einsum("jc,kc->jk", first_flat[1], second_flat[0], precision=highest)
    return (real_part, imag_part)


def inverse_root(gram_real, gram_imag):
    highest = lax.Precision.HIGHEST
    order_size = gram_real.shape[0]
    upper_half = jnp.concatenate([gram_real, -gram_imag], axis=1)
    lower_half = jnp.concatenate([gram_imag, gram_real], axis=1)
    embedded = jnp.concatenate([upper_half, lower_half], axis=0)
    magnitude = jnp.sqrt(jnp.sum(embedded * embedded))
    identity = jnp.eye(2 * order_size, dtype=embedded.dtype)

    def newton(turn_index, carried):
        current, inverse = carried
        factor = 1.5 * identity - 0.5 * jnp.dot(inverse, current, precision=highest)
        return (
            jnp.dot(current, factor, precision=highest),
            jnp.dot(factor, inverse, precision=highest),
        )

    current, inverse = lax.fori_loop(0, NS_STEPS, newton, (embedded / magnitude, identity))
    root_full = inverse / jnp.sqrt(magnitude)
    return (root_full[:order_size, :order_size], root_full[order_size:, :order_size])


def reduce_matrix(root_real, root_imag, ham_real, ham_imag):
    highest = lax.Precision.HIGHEST
    prod_real = jnp.dot(ham_real, root_real, precision=highest) - jnp.dot(
        ham_imag, root_imag, precision=highest
    )
    prod_imag = jnp.dot(ham_real, root_imag, precision=highest) + jnp.dot(
        ham_imag, root_real, precision=highest
    )
    red_real = jnp.dot(root_real.T, prod_real, precision=highest) + jnp.dot(
        root_imag.T, prod_imag, precision=highest
    )
    red_imag = jnp.dot(root_real.T, prod_imag, precision=highest) - jnp.dot(
        root_imag.T, prod_real, precision=highest
    )
    return jnp.stack([red_real, red_imag])


def rotate_basis(raw_basis, root_real, root_imag, scale_factor):
    highest = lax.Precision.HIGHEST
    basis_real = jnp.einsum("jrc,jk->krc", raw_basis[0], root_real, precision=highest) - jnp.einsum(
        "jrc,jk->krc", raw_basis[1], root_imag, precision=highest
    )
    basis_imag = jnp.einsum("jrc,jk->krc", raw_basis[0], root_imag, precision=highest) + jnp.einsum(
        "jrc,jk->krc", raw_basis[1], root_real, precision=highest
    )
    return scale_factor * jnp.stack([basis_real, basis_imag])


def project_mixing(mixing, matrix):
    highest = lax.Precision.HIGHEST
    return jnp.dot(mixing.T, jnp.dot(matrix, mixing, precision=highest), precision=highest)


def exchange_rim(cells, axis, dim, width, low_angle, high_angle):
    count = lax.axis_size(axis)
    head = lax.slice_in_dim(cells, 0, width, axis=dim)
    tail = lax.slice_in_dim(cells, cells.shape[dim] - width, cells.shape[dim], axis=dim)
    if count % 2:
        before = lax.ppermute(tail.reshape(-1), axis, [(i, (i + 1) % count) for i in range(count)])
        after = lax.ppermute(head.reshape(-1), axis, [((i + 1) % count, i) for i in range(count)])
    else:
        even = lax.axis_index(axis) % 2 == 0
        first = lax.ppermute(
            jnp.where(even, tail, head).reshape(-1), axis, [(i, i ^ 1) for i in range(count)]
        )
        second = lax.ppermute(
            jnp.where(even, head, tail).reshape(-1),
            axis,
            [(i, (i + 1) % count if i % 2 else (i - 1) % count) for i in range(count)],
        )
        before = jnp.where(even, second, first)
        after = jnp.where(even, first, second)
    before = before.reshape(tail.shape)
    after = after.reshape(head.shape)
    return jnp.concatenate(
        [rotate_rim(before, low_angle), cells, rotate_rim(after, high_angle)], axis=dim
    )


def rotate_rim(rim, phase_angle):
    field_part = rim[:-1].reshape((2, -1) + rim.shape[1:])
    turned = rotate(field_part, phase_angle).reshape((-1,) + rim.shape[1:])
    return jnp.concatenate([turned, rim[-1:]], axis=0)


def tree_sum(value, axis):
    count = lax.axis_size(axis)
    if count & (count - 1):
        return lax.psum(value, axis)
    step = 1
    while step < count:
        value = value + lax.ppermute(value, axis, [(i, i ^ step) for i in range(count)])
        step *= 2
    return value


def pack_hermitian(real_part, imag_part):
    order_size = real_part.shape[0]
    upper = jnp.arange(order_size)[:, None] <= jnp.arange(order_size)[None, :]
    return jnp.where(upper, real_part, imag_part)


def unpack_hermitian(packed):
    order_size = packed.shape[0]
    upper = jnp.arange(order_size)[:, None] <= jnp.arange(order_size)[None, :]
    strict_upper = jnp.arange(order_size)[:, None] < jnp.arange(order_size)[None, :]
    real_upper = jnp.where(upper, packed, 0.0)
    real_part = real_upper + jnp.where(strict_upper, packed, 0.0).T
    imag_lower = jnp.where(upper, 0.0, packed)
    return (real_part, imag_lower - imag_lower.T)


def matrix_kernel(packed_ref, mix_ref, red_ref, work_ref, *, band_count):
    highest = lax.Precision.HIGHEST

    def dot(first, second):
        return jnp.dot(first, second, precision=highest, preferred_element_type=jnp.float32)

    size = work_ref.shape[-1]
    ext = packed_ref.shape[-1]
    raw = 3 * band_count
    half = size // 2
    work_ref[...] = jnp.zeros(work_ref.shape, jnp.float32)
    work_ref[0, :ext, :ext] = packed_ref[0]
    work_ref[1, :ext, :ext] = packed_ref[1]
    rows = lax.broadcasted_iota(jnp.int32, (size, size), 0)
    cols = lax.broadcasted_iota(jnp.int32, (size, size), 1)
    upper = rows <= cols
    strict = rows < cols
    eye = rows == cols

    def unpack(packed):
        real_part = jnp.where(upper, packed, 0.0) + jnp.where(strict, packed, 0.0).T
        lower = jnp.where(upper, 0.0, packed)
        return real_part, lower - lower.T

    gram_re, gram_im = unpack(work_ref[0])
    ham_re, ham_im = unpack(work_ref[1])
    band_diag = eye & (rows < band_count)
    quotient = jnp.where(band_diag, ham_re, 0.0) / jnp.where(band_diag, gram_re, 1.0)
    to_row = ((rows == cols + 2 * band_count) & (cols < band_count)).astype(jnp.float32)
    to_col = ((cols == rows + band_count) & (rows < band_count)).astype(jnp.float32)
    shifted = dot(dot(to_row, quotient), to_col)
    kept = (eye & (cols < 2 * band_count)) | (
        (rows == cols + band_count) & (cols >= 2 * band_count) & (cols < raw)
    )
    mixing = kept.astype(jnp.float32) - shifted
    mixing_t = mixing.T
    proj_re = dot(mixing_t, dot(gram_re, mixing))
    proj_im = dot(mixing_t, dot(gram_im, mixing))

    def spread(value, axis):
        return pltpu.roll(value, half, axis)

    embedded = proj_re + spread(spread(proj_re, 0), 1) - spread(proj_im, 1) + spread(proj_im, 0)
    active = (rows < raw) | ((rows >= half) & (rows < half + raw))
    identity = (eye & active).astype(jnp.float32)
    total = jnp.sum(jnp.sum(embedded * embedded, axis=0, keepdims=True), axis=1, keepdims=True)
    magnitude = jnp.sqrt(total)
    current = embedded / magnitude
    inverse = identity
    for _ in range(NS_STEPS):
        factor = 1.5 * identity - 0.5 * dot(inverse, current)
        current, inverse = dot(current, factor), dot(factor, inverse)
    root = inverse / jnp.sqrt(magnitude)
    corner = (rows < raw) & (cols < raw)
    root_re = jnp.where(corner, root, 0.0)
    root_im = jnp.where(corner, spread(root, 0), 0.0)
    mix_re = dot(mixing, root_re)
    mix_im = dot(mixing, root_im)
    image_re = dot(ham_re, mix_re) - dot(ham_im, mix_im)
    image_im = dot(ham_re, mix_im) + dot(ham_im, mix_re)
    mix_re_t = mix_re.T
    mix_im_t = mix_im.T
    mix_ref[0] = mix_re
    mix_ref[1] = mix_im
    red_ref[0] = dot(mix_re_t, image_re) + dot(mix_im_t, image_im)
    red_ref[1] = dot(mix_re_t, image_im) - dot(mix_im_t, image_re)


def matrix_stage(packed, band_count):
    size = 128
    vmem = pl.BlockSpec(memory_space=pltpu.VMEM)
    square = jax.ShapeDtypeStruct((2, size, size), jnp.float32)
    return pl.pallas_call(
        functools.partial(matrix_kernel, band_count=band_count),
        out_shape=(square, square),
        in_specs=[vmem],
        out_specs=(vmem, vmem),
        scratch_shapes=[pltpu.VMEM((2, size, size), jnp.float32)],
    )(packed)


def body(bands, directions, materials, permittivity, wavevector):
    band_count = bands.shape[1]
    height = bands.shape[2]
    breadth = bands.shape[3]
    levels = jnp.arange(permittivity.shape[0], dtype=jnp.int32)
    stiffness = jnp.sum(
        jnp.where(
            materials[None] == levels[:, None, None], (1.0 / permittivity)[:, None, None], 0.0
        ),
        axis=0,
    )
    angle_row = 2.0 * math.pi * wavevector[0].astype(jnp.float32) / KDEN
    angle_col = 2.0 * math.pi * wavevector[1].astype(jnp.float32) / KDEN
    row_index = lax.axis_index("row")
    col_index = lax.axis_index("col")
    fields = jnp.concatenate([bands, directions], axis=1)
    packed = jnp.concatenate(
        [fields.reshape(4 * band_count, height, breadth), stiffness[None]], axis=0
    )
    padded = exchange_rim(
        packed,
        "row",
        1,
        2,
        jnp.where(row_index == 0, -angle_row, 0.0),
        jnp.where(row_index == lax.axis_size("row") - 1, angle_row, 0.0),
    )
    padded = exchange_rim(
        padded,
        "col",
        2,
        2,
        jnp.where(col_index == 0, -angle_col, 0.0),
        jnp.where(col_index == lax.axis_size("col") - 1, angle_col, 0.0),
    )
    stiff_wide = padded[-1]
    field_wide = padded[:-1].reshape(2, 2 * band_count, height + 4, breadth + 4)
    band_wide = field_wide[:, :band_count]
    applied_ring, diagonal_ring = stencil(band_wide, stiff_wide)
    stiff_ring = stiff_wide[1:-1, 1:-1]
    scaled_ring = jnp.concatenate(
        [
            applied_ring / diagonal_ring,
            band_wide[:, :, 1:-1, 1:-1] / diagonal_ring,
            field_wide[:, band_count:, 1:-1, 1:-1],
        ],
        axis=1,
    )
    extra_applied = stencil(scaled_ring, stiff_ring)[0]
    applied_cycle = applied_ring[:, :, 1:-1, 1:-1]
    scaled_image = scaled_ring[:, :band_count, 1:-1, 1:-1]
    scaled_bands = scaled_ring[:, band_count : 2 * band_count, 1:-1, 1:-1]
    extended = jnp.concatenate([bands, scaled_image, scaled_bands, directions], axis=1)
    extended_applied = jnp.concatenate([applied_cycle, extra_applied], axis=1)
    local_gram = complex_gram(extended, extended)
    local_ham = complex_gram(extended, extended_applied)
    summed = jnp.stack([pack_hermitian(*local_gram), pack_hermitian(*local_ham)])
    summed = tree_sum(tree_sum(summed.reshape(-1), "row"), "col").reshape(summed.shape)
    mix, red = matrix_stage(summed, band_count)
    raw_count = 3 * band_count
    ext_count = 4 * band_count
    mix = mix[:, :ext_count, :raw_count]
    reduced = red[:, :raw_count, :raw_count]
    scale_factor = math.sqrt(height * breadth * lax.axis_size("row") * lax.axis_size("col"))
    basis = rotate_basis(extended, mix[0], mix[1], scale_factor)
    return (basis, reduced)


def solution(mesh):
    placed = (P(None, None, "row", "col"), P(None, None, "row", "col"), P("row", "col"), P(), P())
    return jax.shard_map(
        body,
        mesh=mesh,
        in_specs=placed,
        out_specs=(P(None, None, "row", "col"), P()),
        check_vma=False,
    )
```

```python
import functools
import math

import jax
import jax.numpy as jnp
from jax import lax
from jax.experimental import pallas as pl
from jax.experimental.pallas import tpu as pltpu
from jax.sharding import PartitionSpec as P

KDEN = 16
NS_STEPS = 5


def rotate(values, phase_angle):
    cosine = jnp.cos(phase_angle)
    sine_part = jnp.sin(phase_angle)
    return jnp.stack(
        [values[0] * cosine - values[1] * sine_part, values[0] * sine_part + values[1] * cosine]
    )


def stencil(padded, stiff_pad):
    centre = stiff_pad[1:-1, 1:-1]
    upward = 0.5 * (centre + stiff_pad[:-2, 1:-1])
    downward = 0.5 * (centre + stiff_pad[2:, 1:-1])
    leftward = 0.5 * (centre + stiff_pad[1:-1, :-2])
    rightward = 0.5 * (centre + stiff_pad[1:-1, 2:])
    diagonal = upward + downward + leftward + rightward
    inner_cells = padded[:, :, 1:-1, 1:-1]
    neighbours = (
        upward * padded[:, :, :-2, 1:-1]
        + downward * padded[:, :, 2:, 1:-1]
        + leftward * padded[:, :, 1:-1, :-2]
        + rightward * padded[:, :, 1:-1, 2:]
    )
    return (diagonal * inner_cells - neighbours, diagonal)


def complex_gram(first_block, second_block):
    highest = lax.Precision.HIGHEST
    first_flat = first_block.reshape(first_block.shape[0], first_block.shape[1], -1)
    second_flat = second_block.reshape(second_block.shape[0], second_block.shape[1], -1)
    real_part = jnp.einsum("pjc,pkc->jk", first_flat, second_flat, precision=highest)
    imag_part = jnp.einsum(
        "jc,kc->jk", first_flat[0], second_flat[1], precision=highest
    ) - jnp.einsum("jc,kc->jk", first_flat[1], second_flat[0], precision=highest)
    return (real_part, imag_part)


def inverse_root(gram_real, gram_imag):
    highest = lax.Precision.HIGHEST
    order_size = gram_real.shape[0]
    upper_half = jnp.concatenate([gram_real, -gram_imag], axis=1)
    lower_half = jnp.concatenate([gram_imag, gram_real], axis=1)
    embedded = jnp.concatenate([upper_half, lower_half], axis=0)
    magnitude = jnp.sqrt(jnp.sum(embedded * embedded))
    identity = jnp.eye(2 * order_size, dtype=embedded.dtype)

    def newton(turn_index, carried):
        current, inverse = carried
        factor = 1.5 * identity - 0.5 * jnp.dot(inverse, current, precision=highest)
        return (
            jnp.dot(current, factor, precision=highest),
            jnp.dot(factor, inverse, precision=highest),
        )

    current, inverse = lax.fori_loop(0, NS_STEPS, newton, (embedded / magnitude, identity))
    root_full = inverse / jnp.sqrt(magnitude)
    return (root_full[:order_size, :order_size], root_full[order_size:, :order_size])


def reduce_matrix(root_real, root_imag, ham_real, ham_imag):
    highest = lax.Precision.HIGHEST
    prod_real = jnp.dot(ham_real, root_real, precision=highest) - jnp.dot(
        ham_imag, root_imag, precision=highest
    )
    prod_imag = jnp.dot(ham_real, root_imag, precision=highest) + jnp.dot(
        ham_imag, root_real, precision=highest
    )
    red_real = jnp.dot(root_real.T, prod_real, precision=highest) + jnp.dot(
        root_imag.T, prod_imag, precision=highest
    )
    red_imag = jnp.dot(root_real.T, prod_imag, precision=highest) - jnp.dot(
        root_imag.T, prod_real, precision=highest
    )
    return jnp.stack([red_real, red_imag])


def rotate_basis(raw_basis, root_real, root_imag, scale_factor):
    highest = lax.Precision.HIGHEST
    basis_real = jnp.einsum("jrc,jk->krc", raw_basis[0], root_real, precision=highest) - jnp.einsum(
        "jrc,jk->krc", raw_basis[1], root_imag, precision=highest
    )
    basis_imag = jnp.einsum("jrc,jk->krc", raw_basis[0], root_imag, precision=highest) + jnp.einsum(
        "jrc,jk->krc", raw_basis[1], root_real, precision=highest
    )
    return scale_factor * jnp.stack([basis_real, basis_imag])


def project_mixing(mixing, matrix):
    highest = lax.Precision.HIGHEST
    return jnp.dot(mixing.T, jnp.dot(matrix, mixing, precision=highest), precision=highest)


def exchange_rim(cells, axis, dim, width, low_angle, high_angle):
    count = lax.axis_size(axis)
    head = lax.slice_in_dim(cells, 0, width, axis=dim)
    tail = lax.slice_in_dim(cells, cells.shape[dim] - width, cells.shape[dim], axis=dim)
    if count % 2:
        before = lax.ppermute(tail.reshape(-1), axis, [(i, (i + 1) % count) for i in range(count)])
        after = lax.ppermute(head.reshape(-1), axis, [((i + 1) % count, i) for i in range(count)])
    else:
        even = lax.axis_index(axis) % 2 == 0
        first = lax.ppermute(
            jnp.where(even, tail, head).reshape(-1), axis, [(i, i ^ 1) for i in range(count)]
        )
        second = lax.ppermute(
            jnp.where(even, head, tail).reshape(-1),
            axis,
            [(i, (i + 1) % count if i % 2 else (i - 1) % count) for i in range(count)],
        )
        before = jnp.where(even, second, first)
        after = jnp.where(even, first, second)
    before = before.reshape(tail.shape)
    after = after.reshape(head.shape)
    return jnp.concatenate(
        [rotate_rim(before, low_angle), cells, rotate_rim(after, high_angle)], axis=dim
    )


def rotate_rim(rim, phase_angle):
    field_part = rim[:-1].reshape((2, -1) + rim.shape[1:])
    turned = rotate(field_part, phase_angle).reshape((-1,) + rim.shape[1:])
    return jnp.concatenate([turned, rim[-1:]], axis=0)


def tree_sum(value, axis):
    count = lax.axis_size(axis)
    if count & (count - 1):
        return lax.psum(value, axis)
    step = 1
    while step < count:
        value = value + lax.ppermute(value, axis, [(i, i ^ step) for i in range(count)])
        step *= 2
    return value


def pack_hermitian(real_part, imag_part):
    order_size = real_part.shape[0]
    upper = jnp.arange(order_size)[:, None] <= jnp.arange(order_size)[None, :]
    return jnp.where(upper, real_part, imag_part)


def unpack_hermitian(packed):
    order_size = packed.shape[0]
    upper = jnp.arange(order_size)[:, None] <= jnp.arange(order_size)[None, :]
    strict_upper = jnp.arange(order_size)[:, None] < jnp.arange(order_size)[None, :]
    real_upper = jnp.where(upper, packed, 0.0)
    real_part = real_upper + jnp.where(strict_upper, packed, 0.0).T
    imag_lower = jnp.where(upper, 0.0, packed)
    return (real_part, imag_lower - imag_lower.T)


def matrix_kernel(packed_ref, basis_ref, red_ref, work_ref, *, band_count, scale):
    highest = lax.Precision.HIGHEST

    def dot(first, second):
        return jnp.dot(first, second, precision=highest, preferred_element_type=jnp.float32)

    size = work_ref.shape[-1]
    ext = packed_ref.shape[-1]
    raw = 3 * band_count
    half = size // 2
    work_ref[...] = jnp.zeros(work_ref.shape, jnp.float32)
    work_ref[0, :ext, :ext] = packed_ref[0]
    work_ref[1, :ext, :ext] = packed_ref[1]
    rows = lax.broadcasted_iota(jnp.int32, (size, size), 0)
    cols = lax.broadcasted_iota(jnp.int32, (size, size), 1)
    upper = rows <= cols
    strict = rows < cols
    eye = rows == cols
    corner = (rows < half) & (cols < half)

    def spread(value, axis):
        return pltpu.roll(value, half, axis)

    def embed(real_part, imag_part):
        return real_part + spread(spread(real_part, 0), 1) - spread(imag_part, 1) + spread(imag_part, 0)

    def unpack(packed):
        real_part = jnp.where(upper, packed, 0.0) + jnp.where(strict, packed, 0.0).T
        lower = jnp.where(upper, 0.0, packed)
        return real_part, lower - lower.T

    gram_re, gram_im = unpack(work_ref[0])
    ham_re, ham_im = unpack(work_ref[1])
    band_diag = eye & (rows < band_count)
    quotient = jnp.where(band_diag, ham_re, 0.0) / jnp.where(band_diag, gram_re, 1.0)
    to_row = ((rows == cols + 2 * band_count) & (cols < band_count)).astype(jnp.float32)
    to_col = ((cols == rows + band_count) & (rows < band_count)).astype(jnp.float32)
    shifted = dot(dot(to_row, quotient), to_col)
    kept = (eye & (cols < 2 * band_count)) | (
        (rows == cols + band_count) & (cols >= 2 * band_count) & (cols < raw)
    )
    mixing = kept.astype(jnp.float32) - shifted
    mixing = mixing + spread(spread(mixing, 0), 1)
    embedded = dot(mixing.T, dot(embed(gram_re, gram_im), mixing))
    active = (rows < raw) | ((rows >= half) & (rows < half + raw))
    identity = (eye & active).astype(jnp.float32)
    total = jnp.sum(jnp.sum(embedded * embedded, axis=0, keepdims=True), axis=1, keepdims=True)
    magnitude = jnp.sqrt(total)
    current = embedded / magnitude
    inverse = identity
    for _ in range(NS_STEPS):
        factor = 1.5 * identity - 0.5 * dot(inverse, current)
        current, inverse = dot(current, factor), dot(factor, inverse)
    root = inverse / jnp.sqrt(magnitude)
    root = embed(jnp.where(corner, root, 0.0), jnp.where(corner, spread(root, 0), 0.0))
    rotation = dot(mixing, root)
    red_ref[...] = dot(rotation.T, dot(embed(ham_re, ham_im), rotation))
    rotation = jnp.where(corner | ~((rows < half) | (cols < half)), rotation, -rotation)
    pick_rows = ((rows < ext) & (cols == rows)) | (
        (rows >= ext) & (rows < 2 * ext) & (cols == rows - ext + half)
    )
    pick_cols = ((rows < raw) & (cols == rows)) | (
        (rows >= half) & (rows < half + raw) & (cols == rows - half + raw)
    )
    packed_rotation = dot(pick_rows.astype(jnp.float32), dot(rotation, pick_cols.astype(jnp.float32)))
    basis_ref[...] = scale * packed_rotation


def matrix_stage(packed, band_count, scale):
    size = 128
    vmem = pl.BlockSpec(memory_space=pltpu.VMEM)
    square = jax.ShapeDtypeStruct((size, size), jnp.float32)
    return pl.pallas_call(
        functools.partial(matrix_kernel, band_count=band_count, scale=scale),
        out_shape=(square, square),
        in_specs=[vmem],
        out_specs=(vmem, vmem),
        scratch_shapes=[pltpu.VMEM((2, size, size), jnp.float32)],
    )(packed)


def body(bands, directions, materials, permittivity, wavevector):
    band_count = bands.shape[1]
    height = bands.shape[2]
    breadth = bands.shape[3]
    levels = jnp.arange(permittivity.shape[0], dtype=jnp.int32)
    stiffness = jnp.sum(
        jnp.where(
            materials[None] == levels[:, None, None], (1.0 / permittivity)[:, None, None], 0.0
        ),
        axis=0,
    )
    angle_row = 2.0 * math.pi * wavevector[0].astype(jnp.float32) / KDEN
    angle_col = 2.0 * math.pi * wavevector[1].astype(jnp.float32) / KDEN
    row_index = lax.axis_index("row")
    col_index = lax.axis_index("col")
    fields = jnp.concatenate([bands, directions], axis=1)
    packed = jnp.concatenate(
        [fields.reshape(4 * band_count, height, breadth), stiffness[None]], axis=0
    )
    padded = exchange_rim(
        packed,
        "row",
        1,
        2,
        jnp.where(row_index == 0, -angle_row, 0.0),
        jnp.where(row_index == lax.axis_size("row") - 1, angle_row, 0.0),
    )
    padded = exchange_rim(
        padded,
        "col",
        2,
        2,
        jnp.where(col_index == 0, -angle_col, 0.0),
        jnp.where(col_index == lax.axis_size("col") - 1, angle_col, 0.0),
    )
    stiff_wide = padded[-1]
    field_wide = padded[:-1].reshape(2, 2 * band_count, height + 4, breadth + 4)
    band_wide = field_wide[:, :band_count]
    applied_ring, diagonal_ring = stencil(band_wide, stiff_wide)
    stiff_ring = stiff_wide[1:-1, 1:-1]
    scaled_ring = jnp.concatenate(
        [
            applied_ring / diagonal_ring,
            band_wide[:, :, 1:-1, 1:-1] / diagonal_ring,
            field_wide[:, band_count:, 1:-1, 1:-1],
        ],
        axis=1,
    )
    extra_applied = stencil(scaled_ring, stiff_ring)[0]
    applied_cycle = applied_ring[:, :, 1:-1, 1:-1]
    scaled_image = scaled_ring[:, :band_count, 1:-1, 1:-1]
    scaled_bands = scaled_ring[:, band_count : 2 * band_count, 1:-1, 1:-1]
    extended = jnp.concatenate([bands, scaled_image, scaled_bands, directions], axis=1)
    extended_applied = jnp.concatenate([applied_cycle, extra_applied], axis=1)
    local_gram = complex_gram(extended, extended)
    local_ham = complex_gram(extended, extended_applied)
    summed = jnp.stack([pack_hermitian(*local_gram), pack_hermitian(*local_ham)])
    summed = tree_sum(tree_sum(summed.reshape(-1), "row"), "col").reshape(summed.shape)
    raw_count = 3 * band_count
    ext_count = 4 * band_count
    scale_factor = math.sqrt(height * breadth * lax.axis_size("row") * lax.axis_size("col"))
    mix, red = matrix_stage(summed, band_count, scale_factor)
    half = red.shape[0] // 2
    reduced = jnp.stack([red[:raw_count, :raw_count], red[half : half + raw_count, :raw_count]])
    basis = jnp.einsum(
        "jrc,jk->krc",
        extended.reshape(2 * ext_count, height, breadth),
        mix[: 2 * ext_count, : 2 * raw_count],
        precision=lax.Precision.HIGHEST,
    ).reshape(2, raw_count, height, breadth)
    return (basis, reduced)


def solution(mesh):
    placed = (P(None, None, "row", "col"), P(None, None, "row", "col"), P("row", "col"), P(), P())
    return jax.shard_map(
        body,
        mesh=mesh,
        in_specs=placed,
        out_specs=(P(None, None, "row", "col"), P()),
        check_vma=False,
    )
```

```python
import functools
import math

import jax
import jax.numpy as jnp
from jax import lax
from jax.experimental import pallas as pl
from jax.experimental.pallas import tpu as pltpu
from jax.sharding import PartitionSpec as P

KDEN = 16
NS_STEPS = 5


def rotate(values, phase_angle):
    cosine = jnp.cos(phase_angle)
    sine_part = jnp.sin(phase_angle)
    return jnp.stack(
        [values[0] * cosine - values[1] * sine_part, values[0] * sine_part + values[1] * cosine]
    )


def stencil(padded, stiff_pad):
    centre = stiff_pad[1:-1, 1:-1]
    upward = 0.5 * (centre + stiff_pad[:-2, 1:-1])
    downward = 0.5 * (centre + stiff_pad[2:, 1:-1])
    leftward = 0.5 * (centre + stiff_pad[1:-1, :-2])
    rightward = 0.5 * (centre + stiff_pad[1:-1, 2:])
    diagonal = upward + downward + leftward + rightward
    inner_cells = padded[:, :, 1:-1, 1:-1]
    neighbours = (
        upward * padded[:, :, :-2, 1:-1]
        + downward * padded[:, :, 2:, 1:-1]
        + leftward * padded[:, :, 1:-1, :-2]
        + rightward * padded[:, :, 1:-1, 2:]
    )
    return (diagonal * inner_cells - neighbours, diagonal)


def complex_gram(first_block, second_block):
    highest = lax.Precision.HIGHEST
    first_flat = first_block.reshape(first_block.shape[0], first_block.shape[1], -1)
    second_flat = second_block.reshape(second_block.shape[0], second_block.shape[1], -1)
    real_part = jnp.einsum("pjc,pkc->jk", first_flat, second_flat, precision=highest)
    imag_part = jnp.einsum(
        "jc,kc->jk", first_flat[0], second_flat[1], precision=highest
    ) - jnp.einsum("jc,kc->jk", first_flat[1], second_flat[0], precision=highest)
    return (real_part, imag_part)


def exchange_rim(cells, axis, dim, width, angle):
    count = lax.axis_size(axis)
    index = lax.axis_index(axis)
    head = lax.slice_in_dim(cells, 0, width, axis=dim)
    tail = lax.slice_in_dim(cells, cells.shape[dim] - width, cells.shape[dim], axis=dim)
    head = rotate_rim(head, jnp.where(index == 0, angle, 0.0))
    tail = rotate_rim(tail, jnp.where(index == count - 1, -angle, 0.0))
    if count % 2:
        before = lax.ppermute(tail.reshape(-1), axis, [(i, (i + 1) % count) for i in range(count)])
        after = lax.ppermute(head.reshape(-1), axis, [((i + 1) % count, i) for i in range(count)])
    else:
        even = index % 2 == 0
        first = lax.ppermute(
            jnp.where(even, tail, head).reshape(-1), axis, [(i, i ^ 1) for i in range(count)]
        )
        second = lax.ppermute(
            jnp.where(even, head, tail).reshape(-1),
            axis,
            [(i, (i + 1) % count if i % 2 else (i - 1) % count) for i in range(count)],
        )
        before = jnp.where(even, second, first)
        after = jnp.where(even, first, second)
    before = before.reshape(tail.shape)
    after = after.reshape(head.shape)
    return jnp.concatenate([before, cells, after], axis=dim)


def rotate_rim(rim, phase_angle):
    field_part = rim[:-1].reshape((2, -1) + rim.shape[1:])
    turned = rotate(field_part, phase_angle).reshape((-1,) + rim.shape[1:])
    return jnp.concatenate([turned, rim[-1:]], axis=0)


def tree_sum(value, axis):
    count = lax.axis_size(axis)
    if count & (count - 1):
        return lax.psum(value, axis)
    step = 1
    while step < count:
        value = value + lax.ppermute(value, axis, [(i, i ^ step) for i in range(count)])
        step *= 2
    return value


def pack_hermitian(real_part, imag_part):
    order_size = real_part.shape[0]
    upper = jnp.arange(order_size)[:, None] <= jnp.arange(order_size)[None, :]
    return jnp.where(upper, real_part, imag_part)


def matrix_kernel(packed_ref, basis_ref, red_ref, work_ref, *, band_count, scale):
    highest = lax.Precision.HIGHEST

    def dot(first, second):
        return jnp.dot(first, second, precision=highest, preferred_element_type=jnp.float32)

    size = work_ref.shape[-1]
    raw = 3 * band_count
    half = size // 2
    ext = packed_ref.shape[0]
    work_ref[...] = jnp.zeros(work_ref.shape, jnp.float32)
    work_ref[0, :ext, :] = packed_ref[...]
    rows = lax.broadcasted_iota(jnp.int32, (size, size), 0)
    cols = lax.broadcasted_iota(jnp.int32, (size, size), 1)
    upper = rows <= cols
    strict = rows < cols
    eye = rows == cols
    corner = (rows < half) & (cols < half)

    def spread(value, axis):
        return pltpu.roll(value, half, axis)

    def embed(real_part, imag_part):
        return real_part + spread(spread(real_part, 0), 1) - spread(imag_part, 1) + spread(imag_part, 0)

    def unpack(packed):
        real_part = jnp.where(upper, packed, 0.0) + jnp.where(strict, packed, 0.0).T
        lower = jnp.where(upper, 0.0, packed)
        return real_part, lower - lower.T

    stacked = work_ref[0]
    left = cols < half
    gram_re, gram_im = unpack(jnp.where(left, stacked, 0.0))
    ham_re, ham_im = unpack(jnp.where(left, spread(stacked, 1), 0.0))
    band_diag = eye & (rows < band_count)
    quotient = jnp.where(band_diag, ham_re, 0.0) / jnp.where(band_diag, gram_re, 1.0)
    to_row = ((rows == cols + 2 * band_count) & (cols < band_count)).astype(jnp.float32)
    to_col = ((cols == rows + band_count) & (rows < band_count)).astype(jnp.float32)
    shifted = dot(dot(to_row, quotient), to_col)
    kept = (eye & (cols < 2 * band_count)) | (
        (rows == cols + band_count) & (cols >= 2 * band_count) & (cols < raw)
    )
    mixing = kept.astype(jnp.float32) - shifted
    mixing = mixing + spread(spread(mixing, 0), 1)
    embedded = dot(mixing.T, dot(embed(gram_re, gram_im), mixing))
    active = (rows < raw) | ((rows >= half) & (rows < half + raw))
    identity = (eye & active).astype(jnp.float32)
    total = jnp.sum(jnp.sum(embedded * embedded, axis=0, keepdims=True), axis=1, keepdims=True)
    magnitude = jnp.sqrt(total)
    current = embedded / magnitude
    inverse = identity
    for _ in range(NS_STEPS):
        factor = 1.5 * identity - 0.5 * dot(inverse, current)
        current, inverse = dot(current, factor), dot(factor, inverse)
    root = inverse / jnp.sqrt(magnitude)
    root = embed(jnp.where(corner, root, 0.0), jnp.where(corner, spread(root, 0), 0.0))
    rotation = dot(mixing, root)
    work_ref[1] = dot(rotation.T, dot(embed(ham_re, ham_im), rotation))
    red_ref[0] = work_ref[1, :raw, :raw]
    red_ref[1] = work_ref[1, half : half + raw, :raw]
    rotation = jnp.where(corner | ~((rows < half) | (cols < half)), rotation, -rotation)
    pick_rows = ((rows < ext) & (cols == rows)) | (
        (rows >= ext) & (rows < 2 * ext) & (cols == rows - ext + half)
    )
    pick_cols = ((rows < raw) & (cols == rows)) | (
        (rows >= half) & (rows < half + raw) & (cols == rows - half + raw)
    )
    packed_rotation = dot(pick_rows.astype(jnp.float32), dot(rotation, pick_cols.astype(jnp.float32)))
    work_ref[0] = scale * packed_rotation.T
    basis_ref[...] = work_ref[0, : 2 * raw, : 2 * ext]


def matrix_stage(packed, band_count, scale):
    size = 128
    raw = 3 * band_count
    vmem = pl.BlockSpec(memory_space=pltpu.VMEM)
    return pl.pallas_call(
        functools.partial(matrix_kernel, band_count=band_count, scale=scale),
        out_shape=(
            jax.ShapeDtypeStruct((2 * raw, 2 * packed.shape[0]), jnp.float32),
            jax.ShapeDtypeStruct((2, raw, raw), jnp.float32),
        ),
        in_specs=[vmem],
        out_specs=(vmem, vmem),
        scratch_shapes=[pltpu.VMEM((2, size, size), jnp.float32)],
    )(packed)


def body(bands, directions, materials, permittivity, wavevector):
    band_count = bands.shape[1]
    height = bands.shape[2]
    breadth = bands.shape[3]
    levels = jnp.arange(permittivity.shape[0], dtype=jnp.int32)
    stiffness = jnp.sum(
        jnp.where(
            materials[None] == levels[:, None, None], (1.0 / permittivity)[:, None, None], 0.0
        ),
        axis=0,
    )
    angle_row = 2.0 * math.pi * wavevector[0].astype(jnp.float32) / KDEN
    angle_col = 2.0 * math.pi * wavevector[1].astype(jnp.float32) / KDEN
    fields = jnp.concatenate([bands, directions], axis=1)
    packed = jnp.concatenate(
        [fields.reshape(4 * band_count, height, breadth), stiffness[None]], axis=0
    )
    padded = exchange_rim(packed, "row", 1, 2, angle_row)
    padded = exchange_rim(padded, "col", 2, 2, angle_col)
    stiff_wide = padded[-1]
    field_wide = padded[:-1].reshape(2, 2 * band_count, height + 4, breadth + 4)
    band_wide = field_wide[:, :band_count]
    applied_ring, diagonal_ring = stencil(band_wide, stiff_wide)
    stiff_ring = stiff_wide[1:-1, 1:-1]
    scaled_ring = jnp.concatenate(
        [
            applied_ring / diagonal_ring,
            band_wide[:, :, 1:-1, 1:-1] / diagonal_ring,
            field_wide[:, band_count:, 1:-1, 1:-1],
        ],
        axis=1,
    )
    extra_applied = stencil(scaled_ring, stiff_ring)[0]
    applied_cycle = applied_ring[:, :, 1:-1, 1:-1]
    scaled_image = scaled_ring[:, :band_count, 1:-1, 1:-1]
    scaled_bands = scaled_ring[:, band_count : 2 * band_count, 1:-1, 1:-1]
    extended = jnp.concatenate([bands, scaled_image, scaled_bands, directions], axis=1)
    extended_applied = jnp.concatenate([applied_cycle, extra_applied], axis=1)
    local_gram = complex_gram(extended, extended)
    local_ham = complex_gram(extended, extended_applied)
    ext_count = 4 * band_count
    gap = jnp.zeros((ext_count, 64 - ext_count), jnp.float32)
    summed = jnp.concatenate(
        [pack_hermitian(*local_gram), gap, pack_hermitian(*local_ham), gap], axis=1
    )
    summed = tree_sum(tree_sum(summed, "row"), "col")
    raw_count = 3 * band_count
    scale_factor = math.sqrt(height * breadth * lax.axis_size("row") * lax.axis_size("col"))
    mix, reduced = matrix_stage(summed, band_count, scale_factor)
    basis = jnp.einsum(
        "kj,jrc->krc",
        mix,
        extended.reshape(2 * ext_count, height, breadth),
        precision=lax.Precision.HIGHEST,
    ).reshape(2, raw_count, height, breadth)
    return (basis, reduced)


def solution(mesh):
    placed = (P(None, None, "row", "col"), P(None, None, "row", "col"), P("row", "col"), P(), P())
    return jax.shard_map(
        body,
        mesh=mesh,
        in_specs=placed,
        out_specs=(P(None, None, "row", "col"), P()),
        check_vma=False,
    )
```

```python
import functools
import math

import jax
import jax.numpy as jnp
from jax import lax
from jax.experimental import pallas as pl
from jax.experimental.pallas import tpu as pltpu
from jax.sharding import PartitionSpec as P

KDEN = 16
NS_STEPS = 5


def rotate(values, phase_angle):
    cosine = jnp.cos(phase_angle)
    sine_part = jnp.sin(phase_angle)
    return jnp.stack(
        [values[0] * cosine - values[1] * sine_part, values[0] * sine_part + values[1] * cosine]
    )


def stencil(padded, stiff_pad):
    centre = stiff_pad[1:-1, 1:-1]
    upward = 0.5 * (centre + stiff_pad[:-2, 1:-1])
    downward = 0.5 * (centre + stiff_pad[2:, 1:-1])
    leftward = 0.5 * (centre + stiff_pad[1:-1, :-2])
    rightward = 0.5 * (centre + stiff_pad[1:-1, 2:])
    diagonal = upward + downward + leftward + rightward
    inner_cells = padded[:, :, 1:-1, 1:-1]
    neighbours = (
        upward * padded[:, :, :-2, 1:-1]
        + downward * padded[:, :, 2:, 1:-1]
        + leftward * padded[:, :, 1:-1, :-2]
        + rightward * padded[:, :, 1:-1, 2:]
    )
    return (diagonal * inner_cells - neighbours, diagonal)


def complex_gram(first_block, second_block):
    count = first_block.shape[1]
    first_flat = first_block.reshape((2 * count,) + first_block.shape[2:])
    second_flat = second_block.reshape((2 * count,) + second_block.shape[2:])
    products = jnp.einsum(
        "jrc,krc->jk", first_flat, second_flat, precision=lax.Precision.HIGHEST
    )
    real_part = products[:count, :count] + products[count:, count:]
    imag_part = products[:count, count:] - products[count:, :count]
    return (real_part, imag_part)


def inverse_root(gram_real, gram_imag):
    highest = lax.Precision.HIGHEST
    order_size = gram_real.shape[0]
    upper_half = jnp.concatenate([gram_real, -gram_imag], axis=1)
    lower_half = jnp.concatenate([gram_imag, gram_real], axis=1)
    embedded = jnp.concatenate([upper_half, lower_half], axis=0)
    magnitude = jnp.sqrt(jnp.sum(embedded * embedded))
    identity = jnp.eye(2 * order_size, dtype=embedded.dtype)

    def newton(turn_index, carried):
        current, inverse = carried
        factor = 1.5 * identity - 0.5 * jnp.dot(inverse, current, precision=highest)
        return (
            jnp.dot(current, factor, precision=highest),
            jnp.dot(factor, inverse, precision=highest),
        )

    current, inverse = lax.fori_loop(0, NS_STEPS, newton, (embedded / magnitude, identity))
    root_full = inverse / jnp.sqrt(magnitude)
    return (root_full[:order_size, :order_size], root_full[order_size:, :order_size])


def reduce_matrix(root_real, root_imag, ham_real, ham_imag):
    highest = lax.Precision.HIGHEST
    prod_real = jnp.dot(ham_real, root_real, precision=highest) - jnp.dot(
        ham_imag, root_imag, precision=highest
    )
    prod_imag = jnp.dot(ham_real, root_imag, precision=highest) + jnp.dot(
        ham_imag, root_real, precision=highest
    )
    red_real = jnp.dot(root_real.T, prod_real, precision=highest) + jnp.dot(
        root_imag.T, prod_imag, precision=highest
    )
    red_imag = jnp.dot(root_real.T, prod_imag, precision=highest) - jnp.dot(
        root_imag.T, prod_real, precision=highest
    )
    return jnp.stack([red_real, red_imag])


def rotate_basis(raw_basis, root_real, root_imag, scale_factor):
    highest = lax.Precision.HIGHEST
    basis_real = jnp.einsum("jrc,jk->krc", raw_basis[0], root_real, precision=highest) - jnp.einsum(
        "jrc,jk->krc", raw_basis[1], root_imag, precision=highest
    )
    basis_imag = jnp.einsum("jrc,jk->krc", raw_basis[0], root_imag, precision=highest) + jnp.einsum(
        "jrc,jk->krc", raw_basis[1], root_real, precision=highest
    )
    return scale_factor * jnp.stack([basis_real, basis_imag])


def project_mixing(mixing, matrix):
    highest = lax.Precision.HIGHEST
    return jnp.dot(mixing.T, jnp.dot(matrix, mixing, precision=highest), precision=highest)


def exchange_rim(cells, axis, dim, width, low_angle, high_angle, strips=None):
    count = lax.axis_size(axis)
    if strips is None:
        head = lax.slice_in_dim(cells, 0, width, axis=dim)
        tail = lax.slice_in_dim(cells, cells.shape[dim] - width, cells.shape[dim], axis=dim)
    else:
        head, tail = strips
    if count % 2:
        before = lax.ppermute(tail.reshape(-1), axis, [(i, (i + 1) % count) for i in range(count)])
        after = lax.ppermute(head.reshape(-1), axis, [((i + 1) % count, i) for i in range(count)])
    else:
        even = lax.axis_index(axis) % 2 == 0
        first = lax.ppermute(
            jnp.where(even, tail, head).reshape(-1), axis, [(i, i ^ 1) for i in range(count)]
        )
        second = lax.ppermute(
            jnp.where(even, head, tail).reshape(-1),
            axis,
            [(i, (i + 1) % count if i % 2 else (i - 1) % count) for i in range(count)],
        )
        before = jnp.where(even, second, first)
        after = jnp.where(even, first, second)
    before = before.reshape(tail.shape)
    after = after.reshape(head.shape)
    return jnp.concatenate(
        [rotate_rim(before, low_angle), cells, rotate_rim(after, high_angle)], axis=dim
    )


def rotate_rim(rim, phase_angle):
    field_part = rim[:-1].reshape((2, -1) + rim.shape[1:])
    turned = rotate(field_part, phase_angle).reshape((-1,) + rim.shape[1:])
    return jnp.concatenate([turned, rim[-1:]], axis=0)


def tree_sum(value, axis):
    count = lax.axis_size(axis)
    if count & (count - 1):
        return lax.psum(value, axis)
    step = 1
    while step < count:
        value = value + lax.ppermute(value, axis, [(i, i ^ step) for i in range(count)])
        step *= 2
    return value


def pack_hermitian(real_part, imag_part):
    order_size = real_part.shape[0]
    upper = jnp.arange(order_size)[:, None] <= jnp.arange(order_size)[None, :]
    return jnp.where(upper, real_part, imag_part)


def unpack_hermitian(packed):
    order_size = packed.shape[0]
    upper = jnp.arange(order_size)[:, None] <= jnp.arange(order_size)[None, :]
    strict_upper = jnp.arange(order_size)[:, None] < jnp.arange(order_size)[None, :]
    real_upper = jnp.where(upper, packed, 0.0)
    real_part = real_upper + jnp.where(strict_upper, packed, 0.0).T
    imag_lower = jnp.where(upper, 0.0, packed)
    return (real_part, imag_lower - imag_lower.T)


def matrix_kernel(packed_ref, basis_ref, red_ref, work_ref, *, band_count, scale):
    highest = lax.Precision.HIGHEST

    def dot(first, second):
        return jnp.dot(first, second, precision=highest, preferred_element_type=jnp.float32)

    size = work_ref.shape[-1]
    ext = packed_ref.shape[-1]
    raw = 3 * band_count
    half = size // 2
    work_ref[...] = jnp.zeros(work_ref.shape, jnp.float32)
    work_ref[0, :ext, :ext] = packed_ref[0]
    work_ref[1, :ext, :ext] = packed_ref[1]
    rows = lax.broadcasted_iota(jnp.int32, (size, size), 0)
    cols = lax.broadcasted_iota(jnp.int32, (size, size), 1)
    upper = rows <= cols
    strict = rows < cols
    eye = rows == cols
    corner = (rows < half) & (cols < half)

    def spread(value, axis):
        return pltpu.roll(value, half, axis)

    def embed(real_part, imag_part):
        return real_part + spread(spread(real_part, 0), 1) - spread(imag_part, 1) + spread(imag_part, 0)

    def unpack(packed):
        real_part = jnp.where(upper, packed, 0.0) + jnp.where(strict, packed, 0.0).T
        lower = jnp.where(upper, 0.0, packed)
        return real_part, lower - lower.T

    gram_re, gram_im = unpack(work_ref[0])
    ham_re, ham_im = unpack(work_ref[1])
    band_diag = eye & (rows < band_count)
    quotient = jnp.where(band_diag, ham_re, 0.0) / jnp.where(band_diag, gram_re, 1.0)
    to_row = ((rows == cols + 2 * band_count) & (cols < band_count)).astype(jnp.float32)
    to_col = ((cols == rows + band_count) & (rows < band_count)).astype(jnp.float32)
    shifted = dot(dot(to_row, quotient), to_col)
    kept = (eye & (cols < 2 * band_count)) | (
        (rows == cols + band_count) & (cols >= 2 * band_count) & (cols < raw)
    )
    mixing = kept.astype(jnp.float32) - shifted
    mixing = mixing + spread(spread(mixing, 0), 1)
    embedded = dot(mixing.T, dot(embed(gram_re, gram_im), mixing))
    active = (rows < raw) | ((rows >= half) & (rows < half + raw))
    identity = (eye & active).astype(jnp.float32)
    total = jnp.sum(jnp.sum(embedded * embedded, axis=0, keepdims=True), axis=1, keepdims=True)
    magnitude = jnp.sqrt(total)
    current = embedded / magnitude
    inverse = identity
    for _ in range(NS_STEPS):
        factor = 1.5 * identity - 0.5 * dot(inverse, current)
        current, inverse = dot(current, factor), dot(factor, inverse)
    root = inverse / jnp.sqrt(magnitude)
    root = embed(jnp.where(corner, root, 0.0), jnp.where(corner, spread(root, 0), 0.0))
    rotation = dot(mixing, root)
    red_ref[...] = dot(rotation.T, dot(embed(ham_re, ham_im), rotation))
    rotation = jnp.where(corner | ~((rows < half) | (cols < half)), rotation, -rotation)
    pick_rows = ((rows < ext) & (cols == rows)) | (
        (rows >= ext) & (rows < 2 * ext) & (cols == rows - ext + half)
    )
    pick_cols = ((rows < raw) & (cols == rows)) | (
        (rows >= half) & (rows < half + raw) & (cols == rows - half + raw)
    )
    packed_rotation = dot(pick_rows.astype(jnp.float32), dot(rotation, pick_cols.astype(jnp.float32)))
    basis_ref[...] = scale * packed_rotation


def matrix_stage(packed, band_count, scale):
    size = 128
    vmem = pl.BlockSpec(memory_space=pltpu.VMEM)
    square = jax.ShapeDtypeStruct((size, size), jnp.float32)
    return pl.pallas_call(
        functools.partial(matrix_kernel, band_count=band_count, scale=scale),
        out_shape=(square, square),
        in_specs=[vmem],
        out_specs=(vmem, vmem),
        scratch_shapes=[pltpu.VMEM((2, size, size), jnp.float32)],
    )(packed)


def body(bands, directions, materials, permittivity, wavevector):
    band_count = bands.shape[1]
    height = bands.shape[2]
    breadth = bands.shape[3]
    levels = jnp.arange(permittivity.shape[0], dtype=jnp.int32)

    def stiffness_of(cells):
        return jnp.sum(
            jnp.where(
                cells[None] == levels[:, None, None], (1.0 / permittivity)[:, None, None], 0.0
            ),
            axis=0,
        )

    def strip_of(start, stop):
        field_rows = jnp.concatenate(
            [bands[:, :, start:stop], directions[:, :, start:stop]], axis=1
        ).reshape(4 * band_count, stop - start, breadth)
        return jnp.concatenate([field_rows, stiffness_of(materials[start:stop])[None]], axis=0)

    stiffness = stiffness_of(materials)
    angle_row = 2.0 * math.pi * wavevector[0].astype(jnp.float32) / KDEN
    angle_col = 2.0 * math.pi * wavevector[1].astype(jnp.float32) / KDEN
    row_index = lax.axis_index("row")
    col_index = lax.axis_index("col")
    fields = jnp.concatenate([bands, directions], axis=1)
    packed = jnp.concatenate(
        [fields.reshape(4 * band_count, height, breadth), stiffness[None]], axis=0
    )
    padded = exchange_rim(
        packed,
        "row",
        1,
        2,
        jnp.where(row_index == 0, -angle_row, 0.0),
        jnp.where(row_index == lax.axis_size("row") - 1, angle_row, 0.0),
        (strip_of(0, 2), strip_of(height - 2, height)),
    )
    padded = exchange_rim(
        padded,
        "col",
        2,
        2,
        jnp.where(col_index == 0, -angle_col, 0.0),
        jnp.where(col_index == lax.axis_size("col") - 1, angle_col, 0.0),
    )
    stiff_wide = padded[-1]
    field_wide = padded[:-1].reshape(2, 2 * band_count, height + 4, breadth + 4)
    band_wide = field_wide[:, :band_count]
    applied_ring, diagonal_ring = stencil(band_wide, stiff_wide)
    stiff_ring = stiff_wide[1:-1, 1:-1]
    scaled_ring = jnp.concatenate(
        [
            applied_ring / diagonal_ring,
            band_wide[:, :, 1:-1, 1:-1] / diagonal_ring,
            field_wide[:, band_count:, 1:-1, 1:-1],
        ],
        axis=1,
    )
    extra_applied = stencil(scaled_ring, stiff_ring)[0]
    applied_cycle = applied_ring[:, :, 1:-1, 1:-1]
    scaled_image = scaled_ring[:, :band_count, 1:-1, 1:-1]
    scaled_bands = scaled_ring[:, band_count : 2 * band_count, 1:-1, 1:-1]
    extended = jnp.concatenate([bands, scaled_image, scaled_bands, directions], axis=1)
    extended_applied = jnp.concatenate([applied_cycle, extra_applied], axis=1)
    local_gram = complex_gram(extended, extended)
    local_ham = complex_gram(extended, extended_applied)
    summed = jnp.stack([pack_hermitian(*local_gram), pack_hermitian(*local_ham)])
    summed = tree_sum(tree_sum(summed.reshape(-1), "row"), "col").reshape(summed.shape)
    raw_count = 3 * band_count
    ext_count = 4 * band_count
    scale_factor = math.sqrt(height * breadth * lax.axis_size("row") * lax.axis_size("col"))
    mix, red = matrix_stage(summed, band_count, scale_factor)
    half = red.shape[0] // 2
    reduced = jnp.stack([red[:raw_count, :raw_count], red[half : half + raw_count, :raw_count]])
    basis = jnp.einsum(
        "jrc,jk->krc",
        extended.reshape(2 * ext_count, height, breadth),
        mix[: 2 * ext_count, : 2 * raw_count],
        precision=lax.Precision.HIGHEST,
    ).reshape(2, raw_count, height, breadth)
    return (basis, reduced)


def solution(mesh):
    placed = (P(None, None, "row", "col"), P(None, None, "row", "col"), P("row", "col"), P(), P())
    return jax.shard_map(
        body,
        mesh=mesh,
        in_specs=placed,
        out_specs=(P(None, None, "row", "col"), P()),
        check_vma=False,
    )
```

```python
import functools
import math

import jax
import jax.numpy as jnp
from jax import lax
from jax.experimental import pallas as pl
from jax.experimental.pallas import tpu as pltpu
from jax.sharding import PartitionSpec as P

KDEN = 16
NS_STEPS = 5


def rotate(values, phase_angle):
    cosine = jnp.cos(phase_angle)
    sine_part = jnp.sin(phase_angle)
    return jnp.stack(
        [values[0] * cosine - values[1] * sine_part, values[0] * sine_part + values[1] * cosine]
    )


def stencil(padded, stiff_pad):
    centre = stiff_pad[1:-1, 1:-1]
    upward = 0.5 * (centre + stiff_pad[:-2, 1:-1])
    downward = 0.5 * (centre + stiff_pad[2:, 1:-1])
    leftward = 0.5 * (centre + stiff_pad[1:-1, :-2])
    rightward = 0.5 * (centre + stiff_pad[1:-1, 2:])
    diagonal = upward + downward + leftward + rightward
    inner_cells = padded[:, :, 1:-1, 1:-1]
    neighbours = (
        upward * padded[:, :, :-2, 1:-1]
        + downward * padded[:, :, 2:, 1:-1]
        + leftward * padded[:, :, 1:-1, :-2]
        + rightward * padded[:, :, 1:-1, 2:]
    )
    return (diagonal * inner_cells - neighbours, diagonal)


def complex_gram(first_block, second_block):
    count = first_block.shape[1]
    first_flat = first_block.reshape((2 * count,) + first_block.shape[2:])
    second_flat = second_block.reshape((2 * count,) + second_block.shape[2:])
    products = jnp.einsum(
        "jrc,krc->jk", first_flat, second_flat, precision=lax.Precision.HIGHEST
    )
    real_part = products[:count, :count] + products[count:, count:]
    imag_part = products[:count, count:] - products[count:, :count]
    return (real_part, imag_part)


def inverse_root(gram_real, gram_imag):
    highest = lax.Precision.HIGHEST
    order_size = gram_real.shape[0]
    upper_half = jnp.concatenate([gram_real, -gram_imag], axis=1)
    lower_half = jnp.concatenate([gram_imag, gram_real], axis=1)
    embedded = jnp.concatenate([upper_half, lower_half], axis=0)
    magnitude = jnp.sqrt(jnp.sum(embedded * embedded))
    identity = jnp.eye(2 * order_size, dtype=embedded.dtype)

    def newton(turn_index, carried):
        current, inverse = carried
        factor = 1.5 * identity - 0.5 * jnp.dot(inverse, current, precision=highest)
        return (
            jnp.dot(current, factor, precision=highest),
            jnp.dot(factor, inverse, precision=highest),
        )

    current, inverse = lax.fori_loop(0, NS_STEPS, newton, (embedded / magnitude, identity))
    root_full = inverse / jnp.sqrt(magnitude)
    return (root_full[:order_size, :order_size], root_full[order_size:, :order_size])


def reduce_matrix(root_real, root_imag, ham_real, ham_imag):
    highest = lax.Precision.HIGHEST
    prod_real = jnp.dot(ham_real, root_real, precision=highest) - jnp.dot(
        ham_imag, root_imag, precision=highest
    )
    prod_imag = jnp.dot(ham_real, root_imag, precision=highest) + jnp.dot(
        ham_imag, root_real, precision=highest
    )
    red_real = jnp.dot(root_real.T, prod_real, precision=highest) + jnp.dot(
        root_imag.T, prod_imag, precision=highest
    )
    red_imag = jnp.dot(root_real.T, prod_imag, precision=highest) - jnp.dot(
        root_imag.T, prod_real, precision=highest
    )
    return jnp.stack([red_real, red_imag])


def rotate_basis(raw_basis, root_real, root_imag, scale_factor):
    highest = lax.Precision.HIGHEST
    basis_real = jnp.einsum("jrc,jk->krc", raw_basis[0], root_real, precision=highest) - jnp.einsum(
        "jrc,jk->krc", raw_basis[1], root_imag, precision=highest
    )
    basis_imag = jnp.einsum("jrc,jk->krc", raw_basis[0], root_imag, precision=highest) + jnp.einsum(
        "jrc,jk->krc", raw_basis[1], root_real, precision=highest
    )
    return scale_factor * jnp.stack([basis_real, basis_imag])


def project_mixing(mixing, matrix):
    highest = lax.Precision.HIGHEST
    return jnp.dot(mixing.T, jnp.dot(matrix, mixing, precision=highest), precision=highest)


def exchange_rim(cells, axis, dim, width, strips=None):
    count = lax.axis_size(axis)
    if strips is None:
        head = lax.slice_in_dim(cells, 0, width, axis=dim)
        tail = lax.slice_in_dim(cells, cells.shape[dim] - width, cells.shape[dim], axis=dim)
    else:
        head, tail = strips
    if count % 2:
        before = lax.ppermute(tail.reshape(-1), axis, [(i, (i + 1) % count) for i in range(count)])
        after = lax.ppermute(head.reshape(-1), axis, [((i + 1) % count, i) for i in range(count)])
    else:
        even = lax.axis_index(axis) % 2 == 0
        first = lax.ppermute(
            jnp.where(even, tail, head).reshape(-1), axis, [(i, i ^ 1) for i in range(count)]
        )
        second = lax.ppermute(
            jnp.where(even, head, tail).reshape(-1),
            axis,
            [(i, (i + 1) % count if i % 2 else (i - 1) % count) for i in range(count)],
        )
        before = jnp.where(even, second, first)
        after = jnp.where(even, first, second)
    before = before.reshape(tail.shape)
    after = after.reshape(head.shape)
    return jnp.concatenate([before, cells, after], axis=dim)


def tree_sum(value, axis):
    count = lax.axis_size(axis)
    if count & (count - 1):
        return lax.psum(value, axis)
    step = 1
    while step < count:
        value = value + lax.ppermute(value, axis, [(i, i ^ step) for i in range(count)])
        step *= 2
    return value


def pack_hermitian(real_part, imag_part):
    order_size = real_part.shape[0]
    upper = jnp.arange(order_size)[:, None] <= jnp.arange(order_size)[None, :]
    return jnp.where(upper, real_part, imag_part)


def unpack_hermitian(packed):
    order_size = packed.shape[0]
    upper = jnp.arange(order_size)[:, None] <= jnp.arange(order_size)[None, :]
    strict_upper = jnp.arange(order_size)[:, None] < jnp.arange(order_size)[None, :]
    real_upper = jnp.where(upper, packed, 0.0)
    real_part = real_upper + jnp.where(strict_upper, packed, 0.0).T
    imag_lower = jnp.where(upper, 0.0, packed)
    return (real_part, imag_lower - imag_lower.T)


def matrix_kernel(packed_ref, basis_ref, red_ref, work_ref, *, band_count, scale):
    highest = lax.Precision.HIGHEST

    def dot(first, second):
        return jnp.dot(first, second, precision=highest, preferred_element_type=jnp.float32)

    size = work_ref.shape[-1]
    ext = packed_ref.shape[-1]
    raw = 3 * band_count
    half = size // 2
    work_ref[...] = jnp.zeros(work_ref.shape, jnp.float32)
    work_ref[0, :ext, :ext] = packed_ref[0]
    work_ref[1, :ext, :ext] = packed_ref[1]
    rows = lax.broadcasted_iota(jnp.int32, (size, size), 0)
    cols = lax.broadcasted_iota(jnp.int32, (size, size), 1)
    upper = rows <= cols
    strict = rows < cols
    eye = rows == cols
    corner = (rows < half) & (cols < half)

    def spread(value, axis):
        return pltpu.roll(value, half, axis)

    def embed(real_part, imag_part):
        return real_part + spread(spread(real_part, 0), 1) - spread(imag_part, 1) + spread(imag_part, 0)

    def unpack(packed):
        real_part = jnp.where(upper, packed, 0.0) + jnp.where(strict, packed, 0.0).T
        lower = jnp.where(upper, 0.0, packed)
        return real_part, lower - lower.T

    gram_re, gram_im = unpack(work_ref[0])
    ham_re, ham_im = unpack(work_ref[1])
    band_diag = eye & (rows < band_count)
    quotient = jnp.where(band_diag, ham_re, 0.0) / jnp.where(band_diag, gram_re, 1.0)
    to_row = ((rows == cols + 2 * band_count) & (cols < band_count)).astype(jnp.float32)
    to_col = ((cols == rows + band_count) & (rows < band_count)).astype(jnp.float32)
    shifted = dot(dot(to_row, quotient), to_col)
    kept = (eye & (cols < 2 * band_count)) | (
        (rows == cols + band_count) & (cols >= 2 * band_count) & (cols < raw)
    )
    mixing = kept.astype(jnp.float32) - shifted
    mixing = mixing + spread(spread(mixing, 0), 1)
    embedded = dot(mixing.T, dot(embed(gram_re, gram_im), mixing))
    active = (rows < raw) | ((rows >= half) & (rows < half + raw))
    identity = (eye & active).astype(jnp.float32)
    total = jnp.sum(jnp.sum(embedded * embedded, axis=0, keepdims=True), axis=1, keepdims=True)
    magnitude = jnp.sqrt(total)
    current = embedded / magnitude
    inverse = identity
    for _ in range(NS_STEPS):
        factor = 1.5 * identity - 0.5 * dot(inverse, current)
        current, inverse = dot(current, factor), dot(factor, inverse)
    root = inverse / jnp.sqrt(magnitude)
    root = embed(jnp.where(corner, root, 0.0), jnp.where(corner, spread(root, 0), 0.0))
    rotation = dot(mixing, root)
    red_ref[...] = dot(rotation.T, dot(embed(ham_re, ham_im), rotation))
    rotation = jnp.where(corner | ~((rows < half) | (cols < half)), rotation, -rotation)
    pick_rows = ((rows < ext) & (cols == rows)) | (
        (rows >= ext) & (rows < 2 * ext) & (cols == rows - ext + half)
    )
    pick_cols = ((rows < raw) & (cols == rows)) | (
        (rows >= half) & (rows < half + raw) & (cols == rows - half + raw)
    )
    packed_rotation = dot(pick_rows.astype(jnp.float32), dot(rotation, pick_cols.astype(jnp.float32)))
    basis_ref[...] = scale * packed_rotation


def matrix_stage(packed, band_count, scale):
    size = 128
    vmem = pl.BlockSpec(memory_space=pltpu.VMEM)
    square = jax.ShapeDtypeStruct((size, size), jnp.float32)
    return pl.pallas_call(
        functools.partial(matrix_kernel, band_count=band_count, scale=scale),
        out_shape=(square, square),
        in_specs=[vmem],
        out_specs=(vmem, vmem),
        scratch_shapes=[pltpu.VMEM((2, size, size), jnp.float32)],
    )(packed)


def body(bands, directions, materials, permittivity, wavevector):
    band_count = bands.shape[1]
    height = bands.shape[2]
    breadth = bands.shape[3]
    levels = jnp.arange(permittivity.shape[0], dtype=jnp.int32)

    def stiffness_of(cells):
        return jnp.sum(
            jnp.where(
                cells[None] == levels[:, None, None], (1.0 / permittivity)[:, None, None], 0.0
            ),
            axis=0,
        )

    def strip_of(start, stop):
        field_rows = jnp.concatenate(
            [bands[:, :, start:stop], directions[:, :, start:stop]], axis=1
        ).reshape(4 * band_count, stop - start, breadth)
        return jnp.concatenate([field_rows, stiffness_of(materials[start:stop])[None]], axis=0)

    stiffness = stiffness_of(materials)
    angle_row = 2.0 * math.pi * wavevector[0].astype(jnp.float32) / KDEN
    angle_col = 2.0 * math.pi * wavevector[1].astype(jnp.float32) / KDEN
    row_index = lax.axis_index("row")
    col_index = lax.axis_index("col")
    fields = jnp.concatenate([bands, directions], axis=1)
    packed = jnp.concatenate(
        [fields.reshape(4 * band_count, height, breadth), stiffness[None]], axis=0
    )
    padded = exchange_rim(packed, "row", 1, 2, (strip_of(0, 2), strip_of(height - 2, height)))
    padded = exchange_rim(padded, "col", 2, 2)
    stiff_wide = padded[-1]
    field_wide = padded[:-1].reshape(2, 2 * band_count, height + 4, breadth + 4)
    row_place = jnp.arange(height + 4)
    col_place = jnp.arange(breadth + 4)
    row_phase = jnp.where(row_place < 2, jnp.where(row_index == 0, -angle_row, 0.0), 0.0) + jnp.where(
        row_place >= height + 2, jnp.where(row_index == lax.axis_size("row") - 1, angle_row, 0.0), 0.0
    )
    col_phase = jnp.where(col_place < 2, jnp.where(col_index == 0, -angle_col, 0.0), 0.0) + jnp.where(
        col_place >= breadth + 2, jnp.where(col_index == lax.axis_size("col") - 1, angle_col, 0.0), 0.0
    )
    field_wide = rotate(field_wide, row_phase[:, None] + col_phase[None, :])
    band_wide = field_wide[:, :band_count]
    applied_ring, diagonal_ring = stencil(band_wide, stiff_wide)
    stiff_ring = stiff_wide[1:-1, 1:-1]
    scaled_ring = jnp.concatenate(
        [
            applied_ring / diagonal_ring,
            band_wide[:, :, 1:-1, 1:-1] / diagonal_ring,
            field_wide[:, band_count:, 1:-1, 1:-1],
        ],
        axis=1,
    )
    extra_applied = stencil(scaled_ring, stiff_ring)[0]
    applied_cycle = applied_ring[:, :, 1:-1, 1:-1]
    scaled_image = scaled_ring[:, :band_count, 1:-1, 1:-1]
    scaled_bands = scaled_ring[:, band_count : 2 * band_count, 1:-1, 1:-1]
    extended = jnp.concatenate([bands, scaled_image, scaled_bands, directions], axis=1)
    extended_applied = jnp.concatenate([applied_cycle, extra_applied], axis=1)
    local_gram = complex_gram(extended, extended)
    local_ham = complex_gram(extended, extended_applied)
    summed = jnp.stack([pack_hermitian(*local_gram), pack_hermitian(*local_ham)])
    summed = tree_sum(tree_sum(summed.reshape(-1), "row"), "col").reshape(summed.shape)
    raw_count = 3 * band_count
    ext_count = 4 * band_count
    scale_factor = math.sqrt(height * breadth * lax.axis_size("row") * lax.axis_size("col"))
    mix, red = matrix_stage(summed, band_count, scale_factor)
    half = red.shape[0] // 2
    reduced = jnp.stack([red[:raw_count, :raw_count], red[half : half + raw_count, :raw_count]])
    basis = jnp.einsum(
        "jrc,jk->krc",
        extended.reshape(2 * ext_count, height, breadth),
        mix[: 2 * ext_count, : 2 * raw_count],
        precision=lax.Precision.HIGHEST,
    ).reshape(2, raw_count, height, breadth)
    return (basis, reduced)


def solution(mesh):
    placed = (P(None, None, "row", "col"), P(None, None, "row", "col"), P("row", "col"), P(), P())
    return jax.shard_map(
        body,
        mesh=mesh,
        in_specs=placed,
        out_specs=(P(None, None, "row", "col"), P()),
        check_vma=False,
    )
```

```python
import functools
import math

import jax
import jax.numpy as jnp
from jax import lax
from jax.experimental import pallas as pl
from jax.experimental.pallas import tpu as pltpu
from jax.sharding import PartitionSpec as P

KDEN = 16
NS_STEPS = 5


def rotate(values, phase_angle):
    cosine = jnp.cos(phase_angle)
    sine_part = jnp.sin(phase_angle)
    return jnp.stack(
        [values[0] * cosine - values[1] * sine_part, values[0] * sine_part + values[1] * cosine]
    )


def stencil(padded, stiff_pad):
    centre = stiff_pad[1:-1, 1:-1]
    upward = 0.5 * (centre + stiff_pad[:-2, 1:-1])
    downward = 0.5 * (centre + stiff_pad[2:, 1:-1])
    leftward = 0.5 * (centre + stiff_pad[1:-1, :-2])
    rightward = 0.5 * (centre + stiff_pad[1:-1, 2:])
    diagonal = upward + downward + leftward + rightward
    inner_cells = padded[:, :, 1:-1, 1:-1]
    neighbours = (
        upward * padded[:, :, :-2, 1:-1]
        + downward * padded[:, :, 2:, 1:-1]
        + leftward * padded[:, :, 1:-1, :-2]
        + rightward * padded[:, :, 1:-1, 2:]
    )
    return (diagonal * inner_cells - neighbours, diagonal)


def complex_gram(first_block, second_block):
    count = first_block.shape[1]
    first_flat = first_block.reshape((2 * count,) + first_block.shape[2:])
    second_flat = second_block.reshape((2 * count,) + second_block.shape[2:])
    products = jnp.einsum(
        "jrc,krc->jk", first_flat, second_flat, precision=lax.Precision.HIGHEST
    )
    real_part = products[:count, :count] + products[count:, count:]
    imag_part = products[:count, count:] - products[count:, :count]
    return (real_part, imag_part)


def inverse_root(gram_real, gram_imag):
    highest = lax.Precision.HIGHEST
    order_size = gram_real.shape[0]
    upper_half = jnp.concatenate([gram_real, -gram_imag], axis=1)
    lower_half = jnp.concatenate([gram_imag, gram_real], axis=1)
    embedded = jnp.concatenate([upper_half, lower_half], axis=0)
    magnitude = jnp.sqrt(jnp.sum(embedded * embedded))
    identity = jnp.eye(2 * order_size, dtype=embedded.dtype)

    def newton(turn_index, carried):
        current, inverse = carried
        factor = 1.5 * identity - 0.5 * jnp.dot(inverse, current, precision=highest)
        return (
            jnp.dot(current, factor, precision=highest),
            jnp.dot(factor, inverse, precision=highest),
        )

    current, inverse = lax.fori_loop(0, NS_STEPS, newton, (embedded / magnitude, identity))
    root_full = inverse / jnp.sqrt(magnitude)
    return (root_full[:order_size, :order_size], root_full[order_size:, :order_size])


def reduce_matrix(root_real, root_imag, ham_real, ham_imag):
    highest = lax.Precision.HIGHEST
    prod_real = jnp.dot(ham_real, root_real, precision=highest) - jnp.dot(
        ham_imag, root_imag, precision=highest
    )
    prod_imag = jnp.dot(ham_real, root_imag, precision=highest) + jnp.dot(
        ham_imag, root_real, precision=highest
    )
    red_real = jnp.dot(root_real.T, prod_real, precision=highest) + jnp.dot(
        root_imag.T, prod_imag, precision=highest
    )
    red_imag = jnp.dot(root_real.T, prod_imag, precision=highest) - jnp.dot(
        root_imag.T, prod_real, precision=highest
    )
    return jnp.stack([red_real, red_imag])


def rotate_basis(raw_basis, root_real, root_imag, scale_factor):
    highest = lax.Precision.HIGHEST
    basis_real = jnp.einsum("jrc,jk->krc", raw_basis[0], root_real, precision=highest) - jnp.einsum(
        "jrc,jk->krc", raw_basis[1], root_imag, precision=highest
    )
    basis_imag = jnp.einsum("jrc,jk->krc", raw_basis[0], root_imag, precision=highest) + jnp.einsum(
        "jrc,jk->krc", raw_basis[1], root_real, precision=highest
    )
    return scale_factor * jnp.stack([basis_real, basis_imag])


def project_mixing(mixing, matrix):
    highest = lax.Precision.HIGHEST
    return jnp.dot(mixing.T, jnp.dot(matrix, mixing, precision=highest), precision=highest)


def exchange_rim(cells, axis, dim, width, strips=None):
    count = lax.axis_size(axis)
    if strips is None:
        head = lax.slice_in_dim(cells, 0, width, axis=dim)
        tail = lax.slice_in_dim(cells, cells.shape[dim] - width, cells.shape[dim], axis=dim)
    else:
        head, tail = strips
    if count % 2:
        before = lax.ppermute(tail.reshape(-1), axis, [(i, (i + 1) % count) for i in range(count)])
        after = lax.ppermute(head.reshape(-1), axis, [((i + 1) % count, i) for i in range(count)])
    else:
        even = lax.axis_index(axis) % 2 == 0
        first = lax.ppermute(
            jnp.where(even, tail, head).reshape(-1), axis, [(i, i ^ 1) for i in range(count)]
        )
        second = lax.ppermute(
            jnp.where(even, head, tail).reshape(-1),
            axis,
            [(i, (i + 1) % count if i % 2 else (i - 1) % count) for i in range(count)],
        )
        before = jnp.where(even, second, first)
        after = jnp.where(even, first, second)
    before = before.reshape(tail.shape)
    after = after.reshape(head.shape)
    return jnp.concatenate([before, cells, after], axis=dim)


def tree_sum(value, axis):
    count = lax.axis_size(axis)
    if count & (count - 1):
        return lax.psum(value, axis)
    step = 1
    while step < count:
        value = value + lax.ppermute(value, axis, [(i, i ^ step) for i in range(count)])
        step *= 2
    return value


def pack_hermitian(real_part, imag_part):
    order_size = real_part.shape[0]
    upper = jnp.arange(order_size)[:, None] <= jnp.arange(order_size)[None, :]
    return jnp.where(upper, real_part, imag_part)


def unpack_hermitian(packed):
    order_size = packed.shape[0]
    upper = jnp.arange(order_size)[:, None] <= jnp.arange(order_size)[None, :]
    strict_upper = jnp.arange(order_size)[:, None] < jnp.arange(order_size)[None, :]
    real_upper = jnp.where(upper, packed, 0.0)
    real_part = real_upper + jnp.where(strict_upper, packed, 0.0).T
    imag_lower = jnp.where(upper, 0.0, packed)
    return (real_part, imag_lower - imag_lower.T)


def matrix_kernel(packed_ref, basis_ref, red_ref, work_ref, *, band_count, scale):
    highest = lax.Precision.HIGHEST

    def dot(first, second):
        return jnp.dot(first, second, precision=highest, preferred_element_type=jnp.float32)

    size = work_ref.shape[-1]
    ext = packed_ref.shape[-1]
    raw = 3 * band_count
    half = size // 2
    work_ref[...] = jnp.zeros(work_ref.shape, jnp.float32)
    work_ref[0, :ext, :ext] = packed_ref[0]
    work_ref[1, :ext, :ext] = packed_ref[1]
    rows = lax.broadcasted_iota(jnp.int32, (size, size), 0)
    cols = lax.broadcasted_iota(jnp.int32, (size, size), 1)
    upper = rows <= cols
    strict = rows < cols
    eye = rows == cols
    corner = (rows < half) & (cols < half)

    def spread(value, axis):
        return pltpu.roll(value, half, axis)

    def embed(real_part, imag_part):
        return real_part + spread(spread(real_part, 0), 1) - spread(imag_part, 1) + spread(imag_part, 0)

    def unpack(packed):
        real_part = jnp.where(upper, packed, 0.0) + jnp.where(strict, packed, 0.0).T
        lower = jnp.where(upper, 0.0, packed)
        return real_part, lower - lower.T

    gram_re, gram_im = unpack(work_ref[0])
    ham_re, ham_im = unpack(work_ref[1])
    band_diag = eye & (rows < band_count)
    quotient = jnp.where(band_diag, ham_re, 0.0) / jnp.where(band_diag, gram_re, 1.0)
    to_row = ((rows == cols + 2 * band_count) & (cols < band_count)).astype(jnp.float32)
    to_col = ((cols == rows + band_count) & (rows < band_count)).astype(jnp.float32)
    shifted = dot(dot(to_row, quotient), to_col)
    kept = (eye & (cols < 2 * band_count)) | (
        (rows == cols + band_count) & (cols >= 2 * band_count) & (cols < raw)
    )
    mixing = kept.astype(jnp.float32) - shifted
    mixing = mixing + spread(spread(mixing, 0), 1)
    embedded = dot(mixing.T, dot(embed(gram_re, gram_im), mixing))
    active = (rows < raw) | ((rows >= half) & (rows < half + raw))
    identity = (eye & active).astype(jnp.float32)
    total = jnp.sum(jnp.sum(embedded * embedded, axis=0, keepdims=True), axis=1, keepdims=True)
    magnitude = jnp.sqrt(total)
    current = embedded / magnitude
    inverse = identity
    for _ in range(NS_STEPS):
        factor = 1.5 * identity - 0.5 * dot(inverse, current)
        current, inverse = dot(current, factor), dot(factor, inverse)
    root = inverse / jnp.sqrt(magnitude)
    root = embed(jnp.where(corner, root, 0.0), jnp.where(corner, spread(root, 0), 0.0))
    rotation = dot(mixing, root)
    red_ref[...] = dot(rotation.T, dot(embed(ham_re, ham_im), rotation))
    rotation = jnp.where(corner | ~((rows < half) | (cols < half)), rotation, -rotation)
    pick_rows = ((rows < ext) & (cols == rows)) | (
        (rows >= ext) & (rows < 2 * ext) & (cols == rows - ext + half)
    )
    pick_cols = ((rows < raw) & (cols == rows)) | (
        (rows >= half) & (rows < half + raw) & (cols == rows - half + raw)
    )
    packed_rotation = dot(pick_rows.astype(jnp.float32), dot(rotation, pick_cols.astype(jnp.float32)))
    basis_ref[...] = scale * packed_rotation


def matrix_stage(packed, band_count, scale):
    size = 128
    vmem = pl.BlockSpec(memory_space=pltpu.VMEM)
    square = jax.ShapeDtypeStruct((size, size), jnp.float32)
    return pl.pallas_call(
        functools.partial(matrix_kernel, band_count=band_count, scale=scale),
        out_shape=(square, square),
        in_specs=[vmem],
        out_specs=(vmem, vmem),
        scratch_shapes=[pltpu.VMEM((2, size, size), jnp.float32)],
    )(packed)


def body(bands, directions, materials, permittivity, wavevector):
    band_count = bands.shape[1]
    height = bands.shape[2]
    breadth = bands.shape[3]
    levels = jnp.arange(permittivity.shape[0], dtype=jnp.int32)

    def stiffness_of(cells):
        return jnp.sum(
            jnp.where(
                cells[None] == levels.astype(jnp.float32)[:, None, None],
                (1.0 / permittivity)[:, None, None],
                0.0,
            ),
            axis=0,
        )

    def strip_of(start, stop):
        field_rows = jnp.concatenate(
            [bands[:, :, start:stop], directions[:, :, start:stop]], axis=1
        ).reshape(4 * band_count, stop - start, breadth)
        return jnp.concatenate([field_rows, material_grid[None, start:stop]], axis=0)

    material_grid = materials.astype(jnp.float32)
    angle_row = 2.0 * math.pi * wavevector[0].astype(jnp.float32) / KDEN
    angle_col = 2.0 * math.pi * wavevector[1].astype(jnp.float32) / KDEN
    row_index = lax.axis_index("row")
    col_index = lax.axis_index("col")
    fields = jnp.concatenate([bands, directions], axis=1)
    packed = jnp.concatenate(
        [fields.reshape(4 * band_count, height, breadth), material_grid[None]], axis=0
    )
    padded = exchange_rim(packed, "row", 1, 2, (strip_of(0, 2), strip_of(height - 2, height)))
    padded = exchange_rim(padded, "col", 2, 2)
    stiff_wide = stiffness_of(padded[-1])
    field_wide = padded[:-1].reshape(2, 2 * band_count, height + 4, breadth + 4)
    row_place = jnp.arange(height + 4)
    col_place = jnp.arange(breadth + 4)
    row_phase = jnp.where(row_place < 2, jnp.where(row_index == 0, -angle_row, 0.0), 0.0) + jnp.where(
        row_place >= height + 2, jnp.where(row_index == lax.axis_size("row") - 1, angle_row, 0.0), 0.0
    )
    col_phase = jnp.where(col_place < 2, jnp.where(col_index == 0, -angle_col, 0.0), 0.0) + jnp.where(
        col_place >= breadth + 2, jnp.where(col_index == lax.axis_size("col") - 1, angle_col, 0.0), 0.0
    )
    field_wide = rotate(field_wide, row_phase[:, None] + col_phase[None, :])
    band_wide = field_wide[:, :band_count]
    applied_ring, diagonal_ring = stencil(band_wide, stiff_wide)
    stiff_ring = stiff_wide[1:-1, 1:-1]
    scaled_ring = jnp.concatenate(
        [
            applied_ring / diagonal_ring,
            band_wide[:, :, 1:-1, 1:-1] / diagonal_ring,
            field_wide[:, band_count:, 1:-1, 1:-1],
        ],
        axis=1,
    )
    extra_applied = stencil(scaled_ring, stiff_ring)[0]
    applied_cycle = applied_ring[:, :, 1:-1, 1:-1]
    scaled_image = scaled_ring[:, :band_count, 1:-1, 1:-1]
    scaled_bands = scaled_ring[:, band_count : 2 * band_count, 1:-1, 1:-1]
    extended = jnp.concatenate([bands, scaled_image, scaled_bands, directions], axis=1)
    extended_applied = jnp.concatenate([applied_cycle, extra_applied], axis=1)
    local_gram = complex_gram(extended, extended)
    local_ham = complex_gram(extended, extended_applied)
    summed = jnp.stack([pack_hermitian(*local_gram), pack_hermitian(*local_ham)])
    summed = tree_sum(tree_sum(summed.reshape(-1), "row"), "col").reshape(summed.shape)
    raw_count = 3 * band_count
    ext_count = 4 * band_count
    scale_factor = math.sqrt(height * breadth * lax.axis_size("row") * lax.axis_size("col"))
    mix, red = matrix_stage(summed, band_count, scale_factor)
    half = red.shape[0] // 2
    reduced = jnp.stack([red[:raw_count, :raw_count], red[half : half + raw_count, :raw_count]])
    basis = jnp.einsum(
        "jrc,jk->krc",
        extended.reshape(2 * ext_count, height, breadth),
        mix[: 2 * ext_count, : 2 * raw_count],
        precision=lax.Precision.HIGHEST,
    ).reshape(2, raw_count, height, breadth)
    return (basis, reduced)


def solution(mesh):
    placed = (P(None, None, "row", "col"), P(None, None, "row", "col"), P("row", "col"), P(), P())
    return jax.shard_map(
        body,
        mesh=mesh,
        in_specs=placed,
        out_specs=(P(None, None, "row", "col"), P()),
        check_vma=False,
    )
```

```python
import functools
import math

import jax
import jax.numpy as jnp
from jax import lax
from jax.experimental import pallas as pl
from jax.experimental.pallas import tpu as pltpu
from jax.sharding import PartitionSpec as P

KDEN = 16
NS_STEPS = 5


def rotate(values, phase_angle):
    cosine = jnp.cos(phase_angle)
    sine_part = jnp.sin(phase_angle)
    return jnp.stack(
        [values[0] * cosine - values[1] * sine_part, values[0] * sine_part + values[1] * cosine]
    )


def stencil(padded, stiff_pad):
    centre = stiff_pad[1:-1, 1:-1]
    upward = 0.5 * (centre + stiff_pad[:-2, 1:-1])
    downward = 0.5 * (centre + stiff_pad[2:, 1:-1])
    leftward = 0.5 * (centre + stiff_pad[1:-1, :-2])
    rightward = 0.5 * (centre + stiff_pad[1:-1, 2:])
    diagonal = upward + downward + leftward + rightward
    inner_cells = padded[:, :, 1:-1, 1:-1]
    neighbours = (
        upward * padded[:, :, :-2, 1:-1]
        + downward * padded[:, :, 2:, 1:-1]
        + leftward * padded[:, :, 1:-1, :-2]
        + rightward * padded[:, :, 1:-1, 2:]
    )
    return (diagonal * inner_cells - neighbours, diagonal)


def complex_gram(first_block, second_block):
    count = first_block.shape[1]
    first_flat = first_block.reshape((2 * count,) + first_block.shape[2:])
    second_flat = second_block.reshape((2 * count,) + second_block.shape[2:])
    products = jnp.einsum(
        "jrc,krc->jk", first_flat, second_flat, precision=lax.Precision.HIGHEST
    )
    real_part = products[:count, :count] + products[count:, count:]
    imag_part = products[:count, count:] - products[count:, :count]
    return (real_part, imag_part)


def inverse_root(gram_real, gram_imag):
    highest = lax.Precision.HIGHEST
    order_size = gram_real.shape[0]
    upper_half = jnp.concatenate([gram_real, -gram_imag], axis=1)
    lower_half = jnp.concatenate([gram_imag, gram_real], axis=1)
    embedded = jnp.concatenate([upper_half, lower_half], axis=0)
    magnitude = jnp.sqrt(jnp.sum(embedded * embedded))
    identity = jnp.eye(2 * order_size, dtype=embedded.dtype)

    def newton(turn_index, carried):
        current, inverse = carried
        factor = 1.5 * identity - 0.5 * jnp.dot(inverse, current, precision=highest)
        return (
            jnp.dot(current, factor, precision=highest),
            jnp.dot(factor, inverse, precision=highest),
        )

    current, inverse = lax.fori_loop(0, NS_STEPS, newton, (embedded / magnitude, identity))
    root_full = inverse / jnp.sqrt(magnitude)
    return (root_full[:order_size, :order_size], root_full[order_size:, :order_size])


def reduce_matrix(root_real, root_imag, ham_real, ham_imag):
    highest = lax.Precision.HIGHEST
    prod_real = jnp.dot(ham_real, root_real, precision=highest) - jnp.dot(
        ham_imag, root_imag, precision=highest
    )
    prod_imag = jnp.dot(ham_real, root_imag, precision=highest) + jnp.dot(
        ham_imag, root_real, precision=highest
    )
    red_real = jnp.dot(root_real.T, prod_real, precision=highest) + jnp.dot(
        root_imag.T, prod_imag, precision=highest
    )
    red_imag = jnp.dot(root_real.T, prod_imag, precision=highest) - jnp.dot(
        root_imag.T, prod_real, precision=highest
    )
    return jnp.stack([red_real, red_imag])


def rotate_basis(raw_basis, root_real, root_imag, scale_factor):
    highest = lax.Precision.HIGHEST
    basis_real = jnp.einsum("jrc,jk->krc", raw_basis[0], root_real, precision=highest) - jnp.einsum(
        "jrc,jk->krc", raw_basis[1], root_imag, precision=highest
    )
    basis_imag = jnp.einsum("jrc,jk->krc", raw_basis[0], root_imag, precision=highest) + jnp.einsum(
        "jrc,jk->krc", raw_basis[1], root_real, precision=highest
    )
    return scale_factor * jnp.stack([basis_real, basis_imag])


def project_mixing(mixing, matrix):
    highest = lax.Precision.HIGHEST
    return jnp.dot(mixing.T, jnp.dot(matrix, mixing, precision=highest), precision=highest)


def exchange_rim(cells, axis, dim, width, strips=None):
    count = lax.axis_size(axis)
    if strips is None:
        head = lax.slice_in_dim(cells, 0, width, axis=dim)
        tail = lax.slice_in_dim(cells, cells.shape[dim] - width, cells.shape[dim], axis=dim)
    else:
        head, tail = strips
    if count % 2:
        before = lax.ppermute(tail.reshape(-1), axis, [(i, (i + 1) % count) for i in range(count)])
        after = lax.ppermute(head.reshape(-1), axis, [((i + 1) % count, i) for i in range(count)])
    else:
        even = lax.axis_index(axis) % 2 == 0
        first = lax.ppermute(
            jnp.where(even, tail, head).reshape(-1), axis, [(i, i ^ 1) for i in range(count)]
        )
        second = lax.ppermute(
            jnp.where(even, head, tail).reshape(-1),
            axis,
            [(i, (i + 1) % count if i % 2 else (i - 1) % count) for i in range(count)],
        )
        before = jnp.where(even, second, first)
        after = jnp.where(even, first, second)
    before = before.reshape(tail.shape)
    after = after.reshape(head.shape)
    return jnp.concatenate([before, cells, after], axis=dim)


def tree_sum(value, axis):
    count = lax.axis_size(axis)
    if count & (count - 1):
        return lax.psum(value, axis)
    step = 1
    while step < count:
        value = value + lax.ppermute(value, axis, [(i, i ^ step) for i in range(count)])
        step *= 2
    return value


def pack_hermitian(real_part, imag_part):
    order_size = real_part.shape[0]
    upper = jnp.arange(order_size)[:, None] <= jnp.arange(order_size)[None, :]
    return jnp.where(upper, real_part, imag_part)


def unpack_hermitian(packed):
    order_size = packed.shape[0]
    upper = jnp.arange(order_size)[:, None] <= jnp.arange(order_size)[None, :]
    strict_upper = jnp.arange(order_size)[:, None] < jnp.arange(order_size)[None, :]
    real_upper = jnp.where(upper, packed, 0.0)
    real_part = real_upper + jnp.where(strict_upper, packed, 0.0).T
    imag_lower = jnp.where(upper, 0.0, packed)
    return (real_part, imag_lower - imag_lower.T)


def matrix_kernel(packed_ref, field_ref, basis_ref, red_ref, work_ref, *, band_count, scale):
    highest = lax.Precision.HIGHEST

    def dot(first, second):
        return jnp.dot(first, second, precision=highest, preferred_element_type=jnp.float32)

    size = work_ref.shape[-1]
    ext = packed_ref.shape[-1]
    raw = 3 * band_count
    half = size // 2
    work_ref[...] = jnp.zeros(work_ref.shape, jnp.float32)
    work_ref[0, :ext, :ext] = packed_ref[0]
    work_ref[1, :ext, :ext] = packed_ref[1]
    rows = lax.broadcasted_iota(jnp.int32, (size, size), 0)
    cols = lax.broadcasted_iota(jnp.int32, (size, size), 1)
    upper = rows <= cols
    strict = rows < cols
    eye = rows == cols
    corner = (rows < half) & (cols < half)

    def spread(value, axis):
        return pltpu.roll(value, half, axis)

    def embed(real_part, imag_part):
        return real_part + spread(spread(real_part, 0), 1) - spread(imag_part, 1) + spread(imag_part, 0)

    def unpack(packed):
        real_part = jnp.where(upper, packed, 0.0) + jnp.where(strict, packed, 0.0).T
        lower = jnp.where(upper, 0.0, packed)
        return real_part, lower - lower.T

    gram_re, gram_im = unpack(work_ref[0])
    ham_re, ham_im = unpack(work_ref[1])
    band_diag = eye & (rows < band_count)
    quotient = jnp.where(band_diag, ham_re, 0.0) / jnp.where(band_diag, gram_re, 1.0)
    to_row = ((rows == cols + 2 * band_count) & (cols < band_count)).astype(jnp.float32)
    to_col = ((cols == rows + band_count) & (rows < band_count)).astype(jnp.float32)
    shifted = dot(dot(to_row, quotient), to_col)
    kept = (eye & (cols < 2 * band_count)) | (
        (rows == cols + band_count) & (cols >= 2 * band_count) & (cols < raw)
    )
    mixing = kept.astype(jnp.float32) - shifted
    mixing = mixing + spread(spread(mixing, 0), 1)
    embedded = dot(mixing.T, dot(embed(gram_re, gram_im), mixing))
    active = (rows < raw) | ((rows >= half) & (rows < half + raw))
    identity = (eye & active).astype(jnp.float32)
    total = jnp.sum(jnp.sum(embedded * embedded, axis=0, keepdims=True), axis=1, keepdims=True)
    magnitude = jnp.sqrt(total)
    current = embedded / magnitude
    inverse = identity
    for _ in range(NS_STEPS):
        factor = 1.5 * identity - 0.5 * dot(inverse, current)
        current, inverse = dot(current, factor), dot(factor, inverse)
    root = inverse / jnp.sqrt(magnitude)
    root = embed(jnp.where(corner, root, 0.0), jnp.where(corner, spread(root, 0), 0.0))
    rotation = dot(mixing, root)
    red_ref[...] = dot(rotation.T, dot(embed(ham_re, ham_im), rotation))
    rotation = jnp.where(corner | ~((rows < half) | (cols < half)), rotation, -rotation)
    pick_rows = ((rows < ext) & (cols == rows)) | (
        (rows >= ext) & (rows < 2 * ext) & (cols == rows - ext + half)
    )
    pick_cols = ((rows < raw) & (cols == rows)) | (
        (rows >= half) & (rows < half + raw) & (cols == rows - half + raw)
    )
    packed_rotation = dot(pick_rows.astype(jnp.float32), dot(rotation, pick_cols.astype(jnp.float32)))
    work_ref[0] = scale * packed_rotation.T
    rotation_t = work_ref[0, : 2 * raw, : 2 * ext]
    for row in range(field_ref.shape[1]):
        basis_ref[:, row, :] = dot(rotation_t, field_ref[:, row, :])


def matrix_stage(packed, fields, band_count, scale):
    size = 128
    raw = 3 * band_count
    vmem = pl.BlockSpec(memory_space=pltpu.VMEM)
    return pl.pallas_call(
        functools.partial(matrix_kernel, band_count=band_count, scale=scale),
        out_shape=(
            jax.ShapeDtypeStruct((2 * raw,) + fields.shape[1:], jnp.float32),
            jax.ShapeDtypeStruct((size, size), jnp.float32),
        ),
        in_specs=[vmem, vmem],
        out_specs=(vmem, vmem),
        scratch_shapes=[pltpu.VMEM((2, size, size), jnp.float32)],
    )(packed, fields)


def body(bands, directions, materials, permittivity, wavevector):
    band_count = bands.shape[1]
    height = bands.shape[2]
    breadth = bands.shape[3]
    levels = jnp.arange(permittivity.shape[0], dtype=jnp.int32)

    def stiffness_of(cells):
        return jnp.sum(
            jnp.where(
                cells[None] == levels.astype(jnp.float32)[:, None, None],
                (1.0 / permittivity)[:, None, None],
                0.0,
            ),
            axis=0,
        )

    def strip_of(start, stop):
        field_rows = jnp.concatenate(
            [bands[:, :, start:stop], directions[:, :, start:stop]], axis=1
        ).reshape(4 * band_count, stop - start, breadth)
        return jnp.concatenate([field_rows, material_grid[None, start:stop]], axis=0)

    material_grid = materials.astype(jnp.float32)
    angle_row = 2.0 * math.pi * wavevector[0].astype(jnp.float32) / KDEN
    angle_col = 2.0 * math.pi * wavevector[1].astype(jnp.float32) / KDEN
    row_index = lax.axis_index("row")
    col_index = lax.axis_index("col")
    fields = jnp.concatenate([bands, directions], axis=1)
    packed = jnp.concatenate(
        [fields.reshape(4 * band_count, height, breadth), material_grid[None]], axis=0
    )
    padded = exchange_rim(packed, "row", 1, 2, (strip_of(0, 2), strip_of(height - 2, height)))
    padded = exchange_rim(padded, "col", 2, 2)
    stiff_wide = stiffness_of(padded[-1])
    field_wide = padded[:-1].reshape(2, 2 * band_count, height + 4, breadth + 4)
    row_place = jnp.arange(height + 4)
    col_place = jnp.arange(breadth + 4)
    row_phase = jnp.where(row_place < 2, jnp.where(row_index == 0, -angle_row, 0.0), 0.0) + jnp.where(
        row_place >= height + 2, jnp.where(row_index == lax.axis_size("row") - 1, angle_row, 0.0), 0.0
    )
    col_phase = jnp.where(col_place < 2, jnp.where(col_index == 0, -angle_col, 0.0), 0.0) + jnp.where(
        col_place >= breadth + 2, jnp.where(col_index == lax.axis_size("col") - 1, angle_col, 0.0), 0.0
    )
    field_wide = rotate(field_wide, row_phase[:, None] + col_phase[None, :])
    band_wide = field_wide[:, :band_count]
    applied_ring, diagonal_ring = stencil(band_wide, stiff_wide)
    stiff_ring = stiff_wide[1:-1, 1:-1]
    scaled_ring = jnp.concatenate(
        [
            applied_ring / diagonal_ring,
            band_wide[:, :, 1:-1, 1:-1] / diagonal_ring,
            field_wide[:, band_count:, 1:-1, 1:-1],
        ],
        axis=1,
    )
    extra_applied = stencil(scaled_ring, stiff_ring)[0]
    applied_cycle = applied_ring[:, :, 1:-1, 1:-1]
    scaled_image = scaled_ring[:, :band_count, 1:-1, 1:-1]
    scaled_bands = scaled_ring[:, band_count : 2 * band_count, 1:-1, 1:-1]
    extended = jnp.concatenate([bands, scaled_image, scaled_bands, directions], axis=1)
    extended_applied = jnp.concatenate([applied_cycle, extra_applied], axis=1)
    local_gram = complex_gram(extended, extended)
    local_ham = complex_gram(extended, extended_applied)
    summed = jnp.stack([pack_hermitian(*local_gram), pack_hermitian(*local_ham)])
    summed = tree_sum(tree_sum(summed.reshape(-1), "row"), "col").reshape(summed.shape)
    raw_count = 3 * band_count
    ext_count = 4 * band_count
    scale_factor = math.sqrt(height * breadth * lax.axis_size("row") * lax.axis_size("col"))
    basis, red = matrix_stage(
        summed, extended.reshape(2 * ext_count, height, breadth), band_count, scale_factor
    )
    half = red.shape[0] // 2
    reduced = jnp.stack([red[:raw_count, :raw_count], red[half : half + raw_count, :raw_count]])
    basis = basis.reshape(2, raw_count, height, breadth)
    return (basis, reduced)


def solution(mesh):
    placed = (P(None, None, "row", "col"), P(None, None, "row", "col"), P("row", "col"), P(), P())
    return jax.shard_map(
        body,
        mesh=mesh,
        in_specs=placed,
        out_specs=(P(None, None, "row", "col"), P()),
        check_vma=False,
    )
```

```python
import functools
import math

import jax
import jax.numpy as jnp
from jax import lax
from jax.experimental import pallas as pl
from jax.experimental.pallas import tpu as pltpu
from jax.sharding import PartitionSpec as P

KDEN = 16
NS_STEPS = 5


def rotate(values, phase_angle):
    cosine = jnp.cos(phase_angle)
    sine_part = jnp.sin(phase_angle)
    return jnp.stack(
        [values[0] * cosine - values[1] * sine_part, values[0] * sine_part + values[1] * cosine]
    )


def stencil(padded, stiff_pad):
    centre = stiff_pad[1:-1, 1:-1]
    upward = 0.5 * (centre + stiff_pad[:-2, 1:-1])
    downward = 0.5 * (centre + stiff_pad[2:, 1:-1])
    leftward = 0.5 * (centre + stiff_pad[1:-1, :-2])
    rightward = 0.5 * (centre + stiff_pad[1:-1, 2:])
    diagonal = upward + downward + leftward + rightward
    inner_cells = padded[:, :, 1:-1, 1:-1]
    neighbours = (
        upward * padded[:, :, :-2, 1:-1]
        + downward * padded[:, :, 2:, 1:-1]
        + leftward * padded[:, :, 1:-1, :-2]
        + rightward * padded[:, :, 1:-1, 2:]
    )
    return (diagonal * inner_cells - neighbours, diagonal)


def complex_gram(first_block, second_block):
    count = first_block.shape[1]
    first_flat = first_block.reshape((2 * count,) + first_block.shape[2:])
    second_flat = second_block.reshape((2 * count,) + second_block.shape[2:])
    products = jnp.einsum(
        "jrc,krc->jk", first_flat, second_flat, precision=lax.Precision.HIGHEST
    )
    real_part = products[:count, :count] + products[count:, count:]
    imag_part = products[:count, count:] - products[count:, :count]
    return (real_part, imag_part)


def inverse_root(gram_real, gram_imag):
    highest = lax.Precision.HIGHEST
    order_size = gram_real.shape[0]
    upper_half = jnp.concatenate([gram_real, -gram_imag], axis=1)
    lower_half = jnp.concatenate([gram_imag, gram_real], axis=1)
    embedded = jnp.concatenate([upper_half, lower_half], axis=0)
    magnitude = jnp.sqrt(jnp.sum(embedded * embedded))
    identity = jnp.eye(2 * order_size, dtype=embedded.dtype)

    def newton(turn_index, carried):
        current, inverse = carried
        factor = 1.5 * identity - 0.5 * jnp.dot(inverse, current, precision=highest)
        return (
            jnp.dot(current, factor, precision=highest),
            jnp.dot(factor, inverse, precision=highest),
        )

    current, inverse = lax.fori_loop(0, NS_STEPS, newton, (embedded / magnitude, identity))
    root_full = inverse / jnp.sqrt(magnitude)
    return (root_full[:order_size, :order_size], root_full[order_size:, :order_size])


def reduce_matrix(root_real, root_imag, ham_real, ham_imag):
    highest = lax.Precision.HIGHEST
    prod_real = jnp.dot(ham_real, root_real, precision=highest) - jnp.dot(
        ham_imag, root_imag, precision=highest
    )
    prod_imag = jnp.dot(ham_real, root_imag, precision=highest) + jnp.dot(
        ham_imag, root_real, precision=highest
    )
    red_real = jnp.dot(root_real.T, prod_real, precision=highest) + jnp.dot(
        root_imag.T, prod_imag, precision=highest
    )
    red_imag = jnp.dot(root_real.T, prod_imag, precision=highest) - jnp.dot(
        root_imag.T, prod_real, precision=highest
    )
    return jnp.stack([red_real, red_imag])


def rotate_basis(raw_basis, root_real, root_imag, scale_factor):
    highest = lax.Precision.HIGHEST
    basis_real = jnp.einsum("jrc,jk->krc", raw_basis[0], root_real, precision=highest) - jnp.einsum(
        "jrc,jk->krc", raw_basis[1], root_imag, precision=highest
    )
    basis_imag = jnp.einsum("jrc,jk->krc", raw_basis[0], root_imag, precision=highest) + jnp.einsum(
        "jrc,jk->krc", raw_basis[1], root_real, precision=highest
    )
    return scale_factor * jnp.stack([basis_real, basis_imag])


def project_mixing(mixing, matrix):
    highest = lax.Precision.HIGHEST
    return jnp.dot(mixing.T, jnp.dot(matrix, mixing, precision=highest), precision=highest)


def exchange_rim(cells, axis, dim, width, strips=None):
    count = lax.axis_size(axis)
    if strips is None:
        head = lax.slice_in_dim(cells, 0, width, axis=dim)
        tail = lax.slice_in_dim(cells, cells.shape[dim] - width, cells.shape[dim], axis=dim)
    else:
        head, tail = strips
    if count % 2:
        before = lax.ppermute(tail.reshape(-1), axis, [(i, (i + 1) % count) for i in range(count)])
        after = lax.ppermute(head.reshape(-1), axis, [((i + 1) % count, i) for i in range(count)])
    else:
        even = lax.axis_index(axis) % 2 == 0
        first = lax.ppermute(
            jnp.where(even, tail, head).reshape(-1), axis, [(i, i ^ 1) for i in range(count)]
        )
        second = lax.ppermute(
            jnp.where(even, head, tail).reshape(-1),
            axis,
            [(i, (i + 1) % count if i % 2 else (i - 1) % count) for i in range(count)],
        )
        before = jnp.where(even, second, first)
        after = jnp.where(even, first, second)
    before = before.reshape(tail.shape)
    after = after.reshape(head.shape)
    return jnp.concatenate([before, cells, after], axis=dim)


def tree_sum(value, axis):
    count = lax.axis_size(axis)
    if count & (count - 1):
        return lax.psum(value, axis)
    step = 1
    while step < count:
        value = value + lax.ppermute(value, axis, [(i, i ^ step) for i in range(count)])
        step *= 2
    return value


def pack_hermitian(real_part, imag_part):
    order_size = real_part.shape[0]
    upper = jnp.arange(order_size)[:, None] <= jnp.arange(order_size)[None, :]
    return jnp.where(upper, real_part, imag_part)


def unpack_hermitian(packed):
    order_size = packed.shape[0]
    upper = jnp.arange(order_size)[:, None] <= jnp.arange(order_size)[None, :]
    strict_upper = jnp.arange(order_size)[:, None] < jnp.arange(order_size)[None, :]
    real_upper = jnp.where(upper, packed, 0.0)
    real_part = real_upper + jnp.where(strict_upper, packed, 0.0).T
    imag_lower = jnp.where(upper, 0.0, packed)
    return (real_part, imag_lower - imag_lower.T)


def matrix_kernel(packed_ref, field_ref, basis_ref, red_ref, work_ref, *, band_count, scale):
    highest = lax.Precision.HIGHEST

    def dot(first, second):
        return jnp.dot(first, second, precision=highest, preferred_element_type=jnp.float32)

    size = work_ref.shape[-1]
    ext = packed_ref.shape[-1]
    raw = 3 * band_count
    half = size // 2
    work_ref[...] = jnp.zeros(work_ref.shape, jnp.float32)
    work_ref[0, :ext, :ext] = packed_ref[0]
    work_ref[1, :ext, :ext] = packed_ref[1]
    rows = lax.broadcasted_iota(jnp.int32, (size, size), 0)
    cols = lax.broadcasted_iota(jnp.int32, (size, size), 1)
    upper = rows <= cols
    strict = rows < cols
    eye = rows == cols
    corner = (rows < half) & (cols < half)

    def spread(value, axis):
        return pltpu.roll(value, half, axis)

    def embed(real_part, imag_part):
        return real_part + spread(spread(real_part, 0), 1) - spread(imag_part, 1) + spread(imag_part, 0)

    def unpack(packed):
        real_part = jnp.where(upper, packed, 0.0) + jnp.where(strict, packed, 0.0).T
        lower = jnp.where(upper, 0.0, packed)
        return real_part, lower - lower.T

    gram_re, gram_im = unpack(work_ref[0])
    ham_re, ham_im = unpack(work_ref[1])
    band_diag = eye & (rows < band_count)
    quotient = jnp.where(band_diag, ham_re, 0.0) / jnp.where(band_diag, gram_re, 1.0)
    to_row = ((rows == cols + 2 * band_count) & (cols < band_count)).astype(jnp.float32)
    to_col = ((cols == rows + band_count) & (rows < band_count)).astype(jnp.float32)
    shifted = dot(dot(to_row, quotient), to_col)
    kept = (eye & (cols < 2 * band_count)) | (
        (rows == cols + band_count) & (cols >= 2 * band_count) & (cols < raw)
    )
    mixing = kept.astype(jnp.float32) - shifted
    mixing = mixing + spread(spread(mixing, 0), 1)
    embedded = dot(mixing.T, dot(embed(gram_re, gram_im), mixing))
    active = (rows < raw) | ((rows >= half) & (rows < half + raw))
    identity = (eye & active).astype(jnp.float32)
    total = jnp.sum(jnp.sum(embedded * embedded, axis=0, keepdims=True), axis=1, keepdims=True)
    magnitude = jnp.sqrt(total)
    current = embedded / magnitude
    inverse = identity
    for _ in range(NS_STEPS):
        factor = 1.5 * identity - 0.5 * dot(inverse, current)
        current, inverse = dot(current, factor), dot(factor, inverse)
    root = inverse / jnp.sqrt(magnitude)
    root = embed(jnp.where(corner, root, 0.0), jnp.where(corner, spread(root, 0), 0.0))
    rotation = dot(mixing, root)
    work_ref[1] = dot(rotation.T, dot(embed(ham_re, ham_im), rotation))
    red_ref[:, 0, :] = work_ref[1, :raw, :raw]
    red_ref[:, 1, :] = work_ref[1, half : half + raw, :raw]
    rotation = jnp.where(corner | ~((rows < half) | (cols < half)), rotation, -rotation)
    pick_rows = ((rows < ext) & (cols == rows)) | (
        (rows >= ext) & (rows < 2 * ext) & (cols == rows - ext + half)
    )
    pick_cols = ((rows < raw) & (cols == rows)) | (
        (rows >= half) & (rows < half + raw) & (cols == rows - half + raw)
    )
    packed_rotation = dot(pick_rows.astype(jnp.float32), dot(rotation, pick_cols.astype(jnp.float32)))
    work_ref[0] = scale * packed_rotation.T
    rotation_t = work_ref[0, : 2 * raw, : 2 * ext]
    for row in range(field_ref.shape[1]):
        basis_ref[:, row, :] = dot(rotation_t, field_ref[:, row, :])


def matrix_stage(packed, fields, band_count, scale):
    size = 128
    raw = 3 * band_count
    vmem = pl.BlockSpec(memory_space=pltpu.VMEM)
    return pl.pallas_call(
        functools.partial(matrix_kernel, band_count=band_count, scale=scale),
        out_shape=(
            jax.ShapeDtypeStruct((2 * raw,) + fields.shape[1:], jnp.float32),
            jax.ShapeDtypeStruct((raw, 2, raw), jnp.float32),
        ),
        in_specs=[vmem, vmem],
        out_specs=(vmem, vmem),
        scratch_shapes=[pltpu.VMEM((2, size, size), jnp.float32)],
    )(packed, fields)


def body(bands, directions, materials, permittivity, wavevector):
    band_count = bands.shape[1]
    height = bands.shape[2]
    breadth = bands.shape[3]
    levels = jnp.arange(permittivity.shape[0], dtype=jnp.int32)

    def stiffness_of(cells):
        return jnp.sum(
            jnp.where(
                cells[None] == levels.astype(jnp.float32)[:, None, None],
                (1.0 / permittivity)[:, None, None],
                0.0,
            ),
            axis=0,
        )

    def strip_of(start, stop):
        field_rows = jnp.concatenate(
            [bands[:, :, start:stop], directions[:, :, start:stop]], axis=1
        ).reshape(4 * band_count, stop - start, breadth)
        return jnp.concatenate([field_rows, material_grid[None, start:stop]], axis=0)

    material_grid = materials.astype(jnp.float32)
    angle_row = 2.0 * math.pi * wavevector[0].astype(jnp.float32) / KDEN
    angle_col = 2.0 * math.pi * wavevector[1].astype(jnp.float32) / KDEN
    row_index = lax.axis_index("row")
    col_index = lax.axis_index("col")
    fields = jnp.concatenate([bands, directions], axis=1)
    packed = jnp.concatenate(
        [fields.reshape(4 * band_count, height, breadth), material_grid[None]], axis=0
    )
    padded = exchange_rim(packed, "row", 1, 2, (strip_of(0, 2), strip_of(height - 2, height)))
    padded = exchange_rim(padded, "col", 2, 2)
    stiff_wide = stiffness_of(padded[-1])
    field_wide = padded[:-1].reshape(2, 2 * band_count, height + 4, breadth + 4)
    row_place = jnp.arange(height + 4)
    col_place = jnp.arange(breadth + 4)
    row_phase = jnp.where(row_place < 2, jnp.where(row_index == 0, -angle_row, 0.0), 0.0) + jnp.where(
        row_place >= height + 2, jnp.where(row_index == lax.axis_size("row") - 1, angle_row, 0.0), 0.0
    )
    col_phase = jnp.where(col_place < 2, jnp.where(col_index == 0, -angle_col, 0.0), 0.0) + jnp.where(
        col_place >= breadth + 2, jnp.where(col_index == lax.axis_size("col") - 1, angle_col, 0.0), 0.0
    )
    field_wide = rotate(field_wide, row_phase[:, None] + col_phase[None, :])
    band_wide = field_wide[:, :band_count]
    applied_ring, diagonal_ring = stencil(band_wide, stiff_wide)
    stiff_ring = stiff_wide[1:-1, 1:-1]
    scaled_ring = jnp.concatenate(
        [
            applied_ring / diagonal_ring,
            band_wide[:, :, 1:-1, 1:-1] / diagonal_ring,
            field_wide[:, band_count:, 1:-1, 1:-1],
        ],
        axis=1,
    )
    extra_applied = stencil(scaled_ring, stiff_ring)[0]
    applied_cycle = applied_ring[:, :, 1:-1, 1:-1]
    scaled_image = scaled_ring[:, :band_count, 1:-1, 1:-1]
    scaled_bands = scaled_ring[:, band_count : 2 * band_count, 1:-1, 1:-1]
    extended = jnp.concatenate([bands, scaled_image, scaled_bands, directions], axis=1)
    extended_applied = jnp.concatenate([applied_cycle, extra_applied], axis=1)
    local_gram = complex_gram(extended, extended)
    local_ham = complex_gram(extended, extended_applied)
    summed = jnp.stack([pack_hermitian(*local_gram), pack_hermitian(*local_ham)])
    summed = tree_sum(tree_sum(summed.reshape(-1), "row"), "col").reshape(summed.shape)
    raw_count = 3 * band_count
    ext_count = 4 * band_count
    scale_factor = math.sqrt(height * breadth * lax.axis_size("row") * lax.axis_size("col"))
    basis, red = matrix_stage(
        summed, extended.reshape(2 * ext_count, height, breadth), band_count, scale_factor
    )
    reduced = jnp.transpose(red, (1, 0, 2))
    basis = basis.reshape(2, raw_count, height, breadth)
    return (basis, reduced)


def solution(mesh):
    placed = (P(None, None, "row", "col"), P(None, None, "row", "col"), P("row", "col"), P(), P())
    return jax.shard_map(
        body,
        mesh=mesh,
        in_specs=placed,
        out_specs=(P(None, None, "row", "col"), P()),
        check_vma=False,
    )
```

```python
import functools
import math

import jax
import jax.numpy as jnp
from jax import lax
from jax.experimental import pallas as pl
from jax.experimental.pallas import tpu as pltpu
from jax.sharding import PartitionSpec as P

KDEN = 16
NS_STEPS = 5


def rotate(values, phase_angle):
    cosine = jnp.cos(phase_angle)
    sine_part = jnp.sin(phase_angle)
    return jnp.stack(
        [values[0] * cosine - values[1] * sine_part, values[0] * sine_part + values[1] * cosine]
    )


def stencil(padded, stiff_pad):
    centre = stiff_pad[1:-1, 1:-1]
    upward = 0.5 * (centre + stiff_pad[:-2, 1:-1])
    downward = 0.5 * (centre + stiff_pad[2:, 1:-1])
    leftward = 0.5 * (centre + stiff_pad[1:-1, :-2])
    rightward = 0.5 * (centre + stiff_pad[1:-1, 2:])
    diagonal = upward + downward + leftward + rightward
    inner_cells = padded[:, :, 1:-1, 1:-1]
    neighbours = (
        upward * padded[:, :, :-2, 1:-1]
        + downward * padded[:, :, 2:, 1:-1]
        + leftward * padded[:, :, 1:-1, :-2]
        + rightward * padded[:, :, 1:-1, 2:]
    )
    return (diagonal * inner_cells - neighbours, diagonal)


def complex_gram(first_block, second_block):
    count = first_block.shape[1]
    first_flat = first_block.reshape((2 * count,) + first_block.shape[2:])
    second_flat = second_block.reshape((2 * count,) + second_block.shape[2:])
    products = jnp.einsum(
        "jrc,krc->jk", first_flat, second_flat, precision=lax.Precision.HIGHEST
    )
    real_part = products[:count, :count] + products[count:, count:]
    imag_part = products[:count, count:] - products[count:, :count]
    return (real_part, imag_part)


def inverse_root(gram_real, gram_imag):
    highest = lax.Precision.HIGHEST
    order_size = gram_real.shape[0]
    upper_half = jnp.concatenate([gram_real, -gram_imag], axis=1)
    lower_half = jnp.concatenate([gram_imag, gram_real], axis=1)
    embedded = jnp.concatenate([upper_half, lower_half], axis=0)
    magnitude = jnp.sqrt(jnp.sum(embedded * embedded))
    identity = jnp.eye(2 * order_size, dtype=embedded.dtype)

    def newton(turn_index, carried):
        current, inverse = carried
        factor = 1.5 * identity - 0.5 * jnp.dot(inverse, current, precision=highest)
        return (
            jnp.dot(current, factor, precision=highest),
            jnp.dot(factor, inverse, precision=highest),
        )

    current, inverse = lax.fori_loop(0, NS_STEPS, newton, (embedded / magnitude, identity))
    root_full = inverse / jnp.sqrt(magnitude)
    return (root_full[:order_size, :order_size], root_full[order_size:, :order_size])


def reduce_matrix(root_real, root_imag, ham_real, ham_imag):
    highest = lax.Precision.HIGHEST
    prod_real = jnp.dot(ham_real, root_real, precision=highest) - jnp.dot(
        ham_imag, root_imag, precision=highest
    )
    prod_imag = jnp.dot(ham_real, root_imag, precision=highest) + jnp.dot(
        ham_imag, root_real, precision=highest
    )
    red_real = jnp.dot(root_real.T, prod_real, precision=highest) + jnp.dot(
        root_imag.T, prod_imag, precision=highest
    )
    red_imag = jnp.dot(root_real.T, prod_imag, precision=highest) - jnp.dot(
        root_imag.T, prod_real, precision=highest
    )
    return jnp.stack([red_real, red_imag])


def rotate_basis(raw_basis, root_real, root_imag, scale_factor):
    highest = lax.Precision.HIGHEST
    basis_real = jnp.einsum("jrc,jk->krc", raw_basis[0], root_real, precision=highest) - jnp.einsum(
        "jrc,jk->krc", raw_basis[1], root_imag, precision=highest
    )
    basis_imag = jnp.einsum("jrc,jk->krc", raw_basis[0], root_imag, precision=highest) + jnp.einsum(
        "jrc,jk->krc", raw_basis[1], root_real, precision=highest
    )
    return scale_factor * jnp.stack([basis_real, basis_imag])


def project_mixing(mixing, matrix):
    highest = lax.Precision.HIGHEST
    return jnp.dot(mixing.T, jnp.dot(matrix, mixing, precision=highest), precision=highest)


def exchange_rim(cells, axis, dim, width, strips=None):
    count = lax.axis_size(axis)
    if strips is None:
        head = lax.slice_in_dim(cells, 0, width, axis=dim)
        tail = lax.slice_in_dim(cells, cells.shape[dim] - width, cells.shape[dim], axis=dim)
    else:
        head, tail = strips
    if count % 2:
        before = lax.ppermute(tail.reshape(-1), axis, [(i, (i + 1) % count) for i in range(count)])
        after = lax.ppermute(head.reshape(-1), axis, [((i + 1) % count, i) for i in range(count)])
    else:
        even = lax.axis_index(axis) % 2 == 0
        first = lax.ppermute(
            jnp.where(even, tail, head).reshape(-1), axis, [(i, i ^ 1) for i in range(count)]
        )
        second = lax.ppermute(
            jnp.where(even, head, tail).reshape(-1),
            axis,
            [(i, (i + 1) % count if i % 2 else (i - 1) % count) for i in range(count)],
        )
        before = jnp.where(even, second, first)
        after = jnp.where(even, first, second)
    before = before.reshape(tail.shape)
    after = after.reshape(head.shape)
    return jnp.concatenate([before, cells, after], axis=dim)


def tree_sum(value, axis):
    count = lax.axis_size(axis)
    if count & (count - 1):
        return lax.psum(value, axis)
    step = 1
    while step < count:
        value = value + lax.ppermute(value, axis, [(i, i ^ step) for i in range(count)])
        step *= 2
    return value


def pack_hermitian(real_part, imag_part):
    order_size = real_part.shape[0]
    upper = jnp.arange(order_size)[:, None] <= jnp.arange(order_size)[None, :]
    return jnp.where(upper, real_part, imag_part)


def unpack_hermitian(packed):
    order_size = packed.shape[0]
    upper = jnp.arange(order_size)[:, None] <= jnp.arange(order_size)[None, :]
    strict_upper = jnp.arange(order_size)[:, None] < jnp.arange(order_size)[None, :]
    real_upper = jnp.where(upper, packed, 0.0)
    real_part = real_upper + jnp.where(strict_upper, packed, 0.0).T
    imag_lower = jnp.where(upper, 0.0, packed)
    return (real_part, imag_lower - imag_lower.T)


def matrix_kernel(packed_ref, field_ref, basis_ref, red_ref, work_ref, *, band_count, scale):
    highest = lax.Precision.HIGHEST

    def dot(first, second):
        return jnp.dot(first, second, precision=highest, preferred_element_type=jnp.float32)

    size = work_ref.shape[-1]
    ext = packed_ref.shape[-1]
    raw = 3 * band_count
    half = size // 2
    work_ref[...] = jnp.zeros(work_ref.shape, jnp.float32)
    work_ref[0, :ext, :ext] = packed_ref[0]
    work_ref[1, :ext, :ext] = packed_ref[1]
    rows = lax.broadcasted_iota(jnp.int32, (size, size), 0)
    cols = lax.broadcasted_iota(jnp.int32, (size, size), 1)
    upper = rows <= cols
    strict = rows < cols
    eye = rows == cols
    corner = (rows < half) & (cols < half)

    def spread(value, axis):
        return pltpu.roll(value, half, axis)

    def embed(real_part, imag_part):
        return real_part + spread(spread(real_part, 0), 1) - spread(imag_part, 1) + spread(imag_part, 0)

    def unpack(packed):
        real_part = jnp.where(upper, packed, 0.0) + jnp.where(strict, packed, 0.0).T
        lower = jnp.where(upper, 0.0, packed)
        return real_part, lower - lower.T

    gram_re, gram_im = unpack(work_ref[0])
    ham_re, ham_im = unpack(work_ref[1])
    band_diag = eye & (rows < band_count)
    quotient = jnp.where(band_diag, ham_re, 0.0) / jnp.where(band_diag, gram_re, 1.0)
    to_row = ((rows == cols + 2 * band_count) & (cols < band_count)).astype(jnp.float32)
    to_col = ((cols == rows + band_count) & (rows < band_count)).astype(jnp.float32)
    shifted = dot(dot(to_row, quotient), to_col)
    kept = (eye & (cols < 2 * band_count)) | (
        (rows == cols + band_count) & (cols >= 2 * band_count) & (cols < raw)
    )
    mixing = kept.astype(jnp.float32) - shifted
    mixing = mixing + spread(spread(mixing, 0), 1)
    embedded = dot(mixing.T, dot(embed(gram_re, gram_im), mixing))
    active = (rows < raw) | ((rows >= half) & (rows < half + raw))
    identity = (eye & active).astype(jnp.float32)
    total = jnp.sum(jnp.sum(embedded * embedded, axis=0, keepdims=True), axis=1, keepdims=True)
    magnitude = jnp.sqrt(total)
    current = embedded / magnitude
    inverse = identity
    for _ in range(NS_STEPS):
        factor = 1.5 * identity - 0.5 * dot(inverse, current)
        current, inverse = dot(current, factor), dot(factor, inverse)
    root = inverse / jnp.sqrt(magnitude)
    root = embed(jnp.where(corner, root, 0.0), jnp.where(corner, spread(root, 0), 0.0))
    rotation = dot(mixing, root)
    work_ref[1] = dot(rotation.T, dot(embed(ham_re, ham_im), rotation))
    red_ref[:, 0, :] = work_ref[1, :raw, :raw]
    red_ref[:, 1, :] = work_ref[1, half : half + raw, :raw]
    rotation = jnp.where(corner | ~((rows < half) | (cols < half)), rotation, -rotation)
    pick_rows = ((rows < ext) & (cols == rows)) | (
        (rows >= ext) & (rows < 2 * ext) & (cols == rows - ext + half)
    )
    pick_cols = ((rows < raw) & (cols == rows)) | (
        (rows >= half) & (rows < half + raw) & (cols == rows - half + raw)
    )
    packed_rotation = dot(pick_rows.astype(jnp.float32), dot(rotation, pick_cols.astype(jnp.float32)))
    work_ref[0] = scale * packed_rotation.T
    rotation_t = work_ref[0, : 2 * raw, : 2 * ext]
    for row in range(field_ref.shape[1]):
        basis_ref[:, row, :] = dot(rotation_t, field_ref[:, row, :])


def matrix_stage(packed, fields, band_count, scale):
    size = 128
    raw = 3 * band_count
    vmem = pl.BlockSpec(memory_space=pltpu.VMEM)
    return pl.pallas_call(
        functools.partial(matrix_kernel, band_count=band_count, scale=scale),
        out_shape=(
            jax.ShapeDtypeStruct((2 * raw,) + fields.shape[1:], jnp.float32),
            jax.ShapeDtypeStruct((raw, 2, raw), jnp.float32),
        ),
        in_specs=[vmem, vmem],
        out_specs=(vmem, vmem),
        scratch_shapes=[pltpu.VMEM((2, size, size), jnp.float32)],
    )(packed, fields)


def body(bands, directions, materials, permittivity, wavevector):
    band_count = bands.shape[1]
    height = bands.shape[2]
    breadth = bands.shape[3]
    levels = jnp.arange(permittivity.shape[0], dtype=jnp.int32)

    def stiffness_of(cells):
        return jnp.sum(
            jnp.where(
                cells[None] == levels.astype(jnp.float32)[:, None, None],
                (1.0 / permittivity)[:, None, None],
                0.0,
            ),
            axis=0,
        )

    def strip_of(start, stop):
        field_rows = jnp.concatenate(
            [bands[:, :, start:stop], directions[:, :, start:stop]], axis=1
        ).reshape(4 * band_count, stop - start, breadth)
        material_rows = materials[start:stop].astype(jnp.float32)
        return jnp.concatenate([field_rows, material_rows[None]], axis=0)

    material_grid = materials.astype(jnp.float32)
    angle_row = 2.0 * math.pi * wavevector[0].astype(jnp.float32) / KDEN
    angle_col = 2.0 * math.pi * wavevector[1].astype(jnp.float32) / KDEN
    row_index = lax.axis_index("row")
    col_index = lax.axis_index("col")
    fields = jnp.concatenate([bands, directions], axis=1)
    packed = jnp.concatenate(
        [fields.reshape(4 * band_count, height, breadth), material_grid[None]], axis=0
    )
    padded = exchange_rim(packed, "row", 1, 2, (strip_of(0, 2), strip_of(height - 2, height)))
    padded = exchange_rim(padded, "col", 2, 2)
    stiff_wide = stiffness_of(padded[-1])
    field_wide = padded[:-1].reshape(2, 2 * band_count, height + 4, breadth + 4)
    row_place = jnp.arange(height + 4)
    col_place = jnp.arange(breadth + 4)
    row_phase = jnp.where(row_place < 2, jnp.where(row_index == 0, -angle_row, 0.0), 0.0) + jnp.where(
        row_place >= height + 2, jnp.where(row_index == lax.axis_size("row") - 1, angle_row, 0.0), 0.0
    )
    col_phase = jnp.where(col_place < 2, jnp.where(col_index == 0, -angle_col, 0.0), 0.0) + jnp.where(
        col_place >= breadth + 2, jnp.where(col_index == lax.axis_size("col") - 1, angle_col, 0.0), 0.0
    )
    field_wide = rotate(field_wide, row_phase[:, None] + col_phase[None, :])
    band_wide = field_wide[:, :band_count]
    applied_ring, diagonal_ring = stencil(band_wide, stiff_wide)
    stiff_ring = stiff_wide[1:-1, 1:-1]
    scaled_ring = jnp.concatenate(
        [
            applied_ring / diagonal_ring,
            band_wide[:, :, 1:-1, 1:-1] / diagonal_ring,
            field_wide[:, band_count:, 1:-1, 1:-1],
        ],
        axis=1,
    )
    extra_applied = stencil(scaled_ring, stiff_ring)[0]
    applied_cycle = applied_ring[:, :, 1:-1, 1:-1]
    scaled_image = scaled_ring[:, :band_count, 1:-1, 1:-1]
    scaled_bands = scaled_ring[:, band_count : 2 * band_count, 1:-1, 1:-1]
    extended = jnp.concatenate([bands, scaled_image, scaled_bands, directions], axis=1)
    extended_applied = jnp.concatenate([applied_cycle, extra_applied], axis=1)
    local_gram = complex_gram(extended, extended)
    local_ham = complex_gram(extended, extended_applied)
    summed = jnp.stack([pack_hermitian(*local_gram), pack_hermitian(*local_ham)])
    summed = tree_sum(tree_sum(summed.reshape(-1), "row"), "col").reshape(summed.shape)
    raw_count = 3 * band_count
    ext_count = 4 * band_count
    scale_factor = math.sqrt(height * breadth * lax.axis_size("row") * lax.axis_size("col"))
    basis, red = matrix_stage(
        summed, extended.reshape(2 * ext_count, height, breadth), band_count, scale_factor
    )
    reduced = jnp.transpose(red, (1, 0, 2))
    basis = basis.reshape(2, raw_count, height, breadth)
    return (basis, reduced)


def solution(mesh):
    placed = (P(None, None, "row", "col"), P(None, None, "row", "col"), P("row", "col"), P(), P())
    return jax.shard_map(
        body,
        mesh=mesh,
        in_specs=placed,
        out_specs=(P(None, None, "row", "col"), P()),
        check_vma=False,
    )
```

```python
import functools
import math

import jax
import jax.numpy as jnp
from jax import lax
from jax.experimental import pallas as pl
from jax.experimental.pallas import tpu as pltpu
from jax.sharding import PartitionSpec as P

KDEN = 16
NS_STEPS = 5


def rotate(values, phase_angle):
    cosine = jnp.cos(phase_angle)
    sine_part = jnp.sin(phase_angle)
    return jnp.stack(
        [values[0] * cosine - values[1] * sine_part, values[0] * sine_part + values[1] * cosine]
    )


def stencil(padded, stiff_pad):
    centre = stiff_pad[1:-1, 1:-1]
    upward = 0.5 * (centre + stiff_pad[:-2, 1:-1])
    downward = 0.5 * (centre + stiff_pad[2:, 1:-1])
    leftward = 0.5 * (centre + stiff_pad[1:-1, :-2])
    rightward = 0.5 * (centre + stiff_pad[1:-1, 2:])
    diagonal = upward + downward + leftward + rightward
    inner_cells = padded[:, :, 1:-1, 1:-1]
    neighbours = (
        upward * padded[:, :, :-2, 1:-1]
        + downward * padded[:, :, 2:, 1:-1]
        + leftward * padded[:, :, 1:-1, :-2]
        + rightward * padded[:, :, 1:-1, 2:]
    )
    return (diagonal * inner_cells - neighbours, diagonal)


def complex_gram(first_block, second_block):
    count = first_block.shape[1]
    first_flat = first_block.reshape((2 * count,) + first_block.shape[2:])
    second_flat = second_block.reshape((2 * count,) + second_block.shape[2:])
    products = jnp.einsum(
        "jrc,krc->jk", first_flat, second_flat, precision=lax.Precision.HIGHEST
    )
    real_part = products[:count, :count] + products[count:, count:]
    imag_part = products[:count, count:] - products[count:, :count]
    return (real_part, imag_part)


def inverse_root(gram_real, gram_imag):
    highest = lax.Precision.HIGHEST
    order_size = gram_real.shape[0]
    upper_half = jnp.concatenate([gram_real, -gram_imag], axis=1)
    lower_half = jnp.concatenate([gram_imag, gram_real], axis=1)
    embedded = jnp.concatenate([upper_half, lower_half], axis=0)
    magnitude = jnp.sqrt(jnp.sum(embedded * embedded))
    identity = jnp.eye(2 * order_size, dtype=embedded.dtype)

    def newton(turn_index, carried):
        current, inverse = carried
        factor = 1.5 * identity - 0.5 * jnp.dot(inverse, current, precision=highest)
        return (
            jnp.dot(current, factor, precision=highest),
            jnp.dot(factor, inverse, precision=highest),
        )

    current, inverse = lax.fori_loop(0, NS_STEPS, newton, (embedded / magnitude, identity))
    root_full = inverse / jnp.sqrt(magnitude)
    return (root_full[:order_size, :order_size], root_full[order_size:, :order_size])


def reduce_matrix(root_real, root_imag, ham_real, ham_imag):
    highest = lax.Precision.HIGHEST
    prod_real = jnp.dot(ham_real, root_real, precision=highest) - jnp.dot(
        ham_imag, root_imag, precision=highest
    )
    prod_imag = jnp.dot(ham_real, root_imag, precision=highest) + jnp.dot(
        ham_imag, root_real, precision=highest
    )
    red_real = jnp.dot(root_real.T, prod_real, precision=highest) + jnp.dot(
        root_imag.T, prod_imag, precision=highest
    )
    red_imag = jnp.dot(root_real.T, prod_imag, precision=highest) - jnp.dot(
        root_imag.T, prod_real, precision=highest
    )
    return jnp.stack([red_real, red_imag])


def rotate_basis(raw_basis, root_real, root_imag, scale_factor):
    highest = lax.Precision.HIGHEST
    basis_real = jnp.einsum("jrc,jk->krc", raw_basis[0], root_real, precision=highest) - jnp.einsum(
        "jrc,jk->krc", raw_basis[1], root_imag, precision=highest
    )
    basis_imag = jnp.einsum("jrc,jk->krc", raw_basis[0], root_imag, precision=highest) + jnp.einsum(
        "jrc,jk->krc", raw_basis[1], root_real, precision=highest
    )
    return scale_factor * jnp.stack([basis_real, basis_imag])


def project_mixing(mixing, matrix):
    highest = lax.Precision.HIGHEST
    return jnp.dot(mixing.T, jnp.dot(matrix, mixing, precision=highest), precision=highest)


def exchange_rim(cells, axis, dim, width, strips=None):
    count = lax.axis_size(axis)
    if strips is None:
        head = lax.slice_in_dim(cells, 0, width, axis=dim)
        tail = lax.slice_in_dim(cells, cells.shape[dim] - width, cells.shape[dim], axis=dim)
    else:
        head, tail = strips
    if count % 2:
        before = lax.ppermute(tail.reshape(-1), axis, [(i, (i + 1) % count) for i in range(count)])
        after = lax.ppermute(head.reshape(-1), axis, [((i + 1) % count, i) for i in range(count)])
    else:
        even = lax.axis_index(axis) % 2 == 0
        both = jnp.concatenate([head.reshape(-1), tail.reshape(-1)])
        first = lax.ppermute(both, axis, [(i, i ^ 1) for i in range(count)])
        second = lax.ppermute(
            both, axis, [(i, (i + 1) % count if i % 2 else (i - 1) % count) for i in range(count)]
        )
        split = head.size
        before = jnp.where(even, second[split:], first[split:])
        after = jnp.where(even, first[:split], second[:split])
    before = before.reshape(tail.shape)
    after = after.reshape(head.shape)
    return jnp.concatenate([before, cells, after], axis=dim)


def tree_sum(value, axis):
    count = lax.axis_size(axis)
    if count & (count - 1):
        return lax.psum(value, axis)
    step = 1
    while step < count:
        value = value + lax.ppermute(value, axis, [(i, i ^ step) for i in range(count)])
        step *= 2
    return value


def pack_hermitian(real_part, imag_part):
    order_size = real_part.shape[0]
    upper = jnp.arange(order_size)[:, None] <= jnp.arange(order_size)[None, :]
    return jnp.where(upper, real_part, imag_part)


def unpack_hermitian(packed):
    order_size = packed.shape[0]
    upper = jnp.arange(order_size)[:, None] <= jnp.arange(order_size)[None, :]
    strict_upper = jnp.arange(order_size)[:, None] < jnp.arange(order_size)[None, :]
    real_upper = jnp.where(upper, packed, 0.0)
    real_part = real_upper + jnp.where(strict_upper, packed, 0.0).T
    imag_lower = jnp.where(upper, 0.0, packed)
    return (real_part, imag_lower - imag_lower.T)


def matrix_kernel(packed_ref, field_ref, basis_ref, red_ref, work_ref, *, band_count, scale):
    highest = lax.Precision.HIGHEST

    def dot(first, second):
        return jnp.dot(first, second, precision=highest, preferred_element_type=jnp.float32)

    size = work_ref.shape[-1]
    ext = packed_ref.shape[-1]
    raw = 3 * band_count
    half = size // 2
    work_ref[...] = jnp.zeros(work_ref.shape, jnp.float32)
    work_ref[0, :ext, :ext] = packed_ref[0]
    work_ref[1, :ext, :ext] = packed_ref[1]
    rows = lax.broadcasted_iota(jnp.int32, (size, size), 0)
    cols = lax.broadcasted_iota(jnp.int32, (size, size), 1)
    upper = rows <= cols
    strict = rows < cols
    eye = rows == cols
    corner = (rows < half) & (cols < half)

    def spread(value, axis):
        return pltpu.roll(value, half, axis)

    def embed(real_part, imag_part):
        return real_part + spread(spread(real_part, 0), 1) - spread(imag_part, 1) + spread(imag_part, 0)

    def unpack(packed):
        real_part = jnp.where(upper, packed, 0.0) + jnp.where(strict, packed, 0.0).T
        lower = jnp.where(upper, 0.0, packed)
        return real_part, lower - lower.T

    gram_re, gram_im = unpack(work_ref[0])
    ham_re, ham_im = unpack(work_ref[1])
    band_diag = eye & (rows < band_count)
    quotient = jnp.where(band_diag, ham_re, 0.0) / jnp.where(band_diag, gram_re, 1.0)
    to_row = ((rows == cols + 2 * band_count) & (cols < band_count)).astype(jnp.float32)
    to_col = ((cols == rows + band_count) & (rows < band_count)).astype(jnp.float32)
    shifted = dot(dot(to_row, quotient), to_col)
    kept = (eye & (cols < 2 * band_count)) | (
        (rows == cols + band_count) & (cols >= 2 * band_count) & (cols < raw)
    )
    mixing = kept.astype(jnp.float32) - shifted
    mixing = mixing + spread(spread(mixing, 0), 1)
    embedded = dot(mixing.T, dot(embed(gram_re, gram_im), mixing))
    active = (rows < raw) | ((rows >= half) & (rows < half + raw))
    identity = (eye & active).astype(jnp.float32)
    total = jnp.sum(jnp.sum(embedded * embedded, axis=0, keepdims=True), axis=1, keepdims=True)
    magnitude = jnp.sqrt(total)
    current = embedded / magnitude
    inverse = identity
    for _ in range(NS_STEPS):
        factor = 1.5 * identity - 0.5 * dot(inverse, current)
        current, inverse = dot(current, factor), dot(factor, inverse)
    root = inverse / jnp.sqrt(magnitude)
    root = embed(jnp.where(corner, root, 0.0), jnp.where(corner, spread(root, 0), 0.0))
    rotation = dot(mixing, root)
    work_ref[1] = dot(rotation.T, dot(embed(ham_re, ham_im), rotation))
    red_ref[:, 0, :] = work_ref[1, :raw, :raw]
    red_ref[:, 1, :] = work_ref[1, half : half + raw, :raw]
    rotation = jnp.where(corner | ~((rows < half) | (cols < half)), rotation, -rotation)
    pick_rows = ((rows < ext) & (cols == rows)) | (
        (rows >= ext) & (rows < 2 * ext) & (cols == rows - ext + half)
    )
    pick_cols = ((rows < raw) & (cols == rows)) | (
        (rows >= half) & (rows < half + raw) & (cols == rows - half + raw)
    )
    packed_rotation = dot(pick_rows.astype(jnp.float32), dot(rotation, pick_cols.astype(jnp.float32)))
    work_ref[0] = scale * packed_rotation.T
    rotation_t = work_ref[0, : 2 * raw, : 2 * ext]
    for row in range(field_ref.shape[1]):
        basis_ref[:, row, :] = dot(rotation_t, field_ref[:, row, :])


def matrix_stage(packed, fields, band_count, scale):
    size = 128
    raw = 3 * band_count
    vmem = pl.BlockSpec(memory_space=pltpu.VMEM)
    return pl.pallas_call(
        functools.partial(matrix_kernel, band_count=band_count, scale=scale),
        out_shape=(
            jax.ShapeDtypeStruct((2 * raw,) + fields.shape[1:], jnp.float32),
            jax.ShapeDtypeStruct((raw, 2, raw), jnp.float32),
        ),
        in_specs=[vmem, vmem],
        out_specs=(vmem, vmem),
        scratch_shapes=[pltpu.VMEM((2, size, size), jnp.float32)],
    )(packed, fields)


def body(bands, directions, materials, permittivity, wavevector):
    band_count = bands.shape[1]
    height = bands.shape[2]
    breadth = bands.shape[3]
    levels = jnp.arange(permittivity.shape[0], dtype=jnp.int32)

    def stiffness_of(cells):
        return jnp.sum(
            jnp.where(
                cells[None] == levels.astype(jnp.float32)[:, None, None],
                (1.0 / permittivity)[:, None, None],
                0.0,
            ),
            axis=0,
        )

    def strip_of(start, stop):
        field_rows = jnp.concatenate(
            [bands[:, :, start:stop], directions[:, :, start:stop]], axis=1
        ).reshape(4 * band_count, stop - start, breadth)
        return jnp.concatenate([field_rows, material_grid[None, start:stop]], axis=0)

    material_grid = materials.astype(jnp.float32)
    angle_row = 2.0 * math.pi * wavevector[0].astype(jnp.float32) / KDEN
    angle_col = 2.0 * math.pi * wavevector[1].astype(jnp.float32) / KDEN
    row_index = lax.axis_index("row")
    col_index = lax.axis_index("col")
    fields = jnp.concatenate([bands, directions], axis=1)
    packed = jnp.concatenate(
        [fields.reshape(4 * band_count, height, breadth), material_grid[None]], axis=0
    )
    padded = exchange_rim(packed, "row", 1, 2, (strip_of(0, 2), strip_of(height - 2, height)))
    padded = exchange_rim(padded, "col", 2, 2)
    stiff_wide = stiffness_of(padded[-1])
    field_wide = padded[:-1].reshape(2, 2 * band_count, height + 4, breadth + 4)
    row_place = jnp.arange(height + 4)
    col_place = jnp.arange(breadth + 4)
    row_phase = jnp.where(row_place < 2, jnp.where(row_index == 0, -angle_row, 0.0), 0.0) + jnp.where(
        row_place >= height + 2, jnp.where(row_index == lax.axis_size("row") - 1, angle_row, 0.0), 0.0
    )
    col_phase = jnp.where(col_place < 2, jnp.where(col_index == 0, -angle_col, 0.0), 0.0) + jnp.where(
        col_place >= breadth + 2, jnp.where(col_index == lax.axis_size("col") - 1, angle_col, 0.0), 0.0
    )
    field_wide = rotate(field_wide, row_phase[:, None] + col_phase[None, :])
    band_wide = field_wide[:, :band_count]
    applied_ring, diagonal_ring = stencil(band_wide, stiff_wide)
    stiff_ring = stiff_wide[1:-1, 1:-1]
    scaled_ring = jnp.concatenate(
        [
            applied_ring / diagonal_ring,
            band_wide[:, :, 1:-1, 1:-1] / diagonal_ring,
            field_wide[:, band_count:, 1:-1, 1:-1],
        ],
        axis=1,
    )
    extra_applied = stencil(scaled_ring, stiff_ring)[0]
    applied_cycle = applied_ring[:, :, 1:-1, 1:-1]
    scaled_image = scaled_ring[:, :band_count, 1:-1, 1:-1]
    scaled_bands = scaled_ring[:, band_count : 2 * band_count, 1:-1, 1:-1]
    extended = jnp.concatenate([bands, scaled_image, scaled_bands, directions], axis=1)
    extended_applied = jnp.concatenate([applied_cycle, extra_applied], axis=1)
    local_gram = complex_gram(extended, extended)
    local_ham = complex_gram(extended, extended_applied)
    summed = jnp.stack([pack_hermitian(*local_gram), pack_hermitian(*local_ham)])
    summed = tree_sum(tree_sum(summed.reshape(-1), "row"), "col").reshape(summed.shape)
    raw_count = 3 * band_count
    ext_count = 4 * band_count
    scale_factor = math.sqrt(height * breadth * lax.axis_size("row") * lax.axis_size("col"))
    basis, red = matrix_stage(
        summed, extended.reshape(2 * ext_count, height, breadth), band_count, scale_factor
    )
    reduced = jnp.transpose(red, (1, 0, 2))
    basis = basis.reshape(2, raw_count, height, breadth)
    return (basis, reduced)


def solution(mesh):
    placed = (P(None, None, "row", "col"), P(None, None, "row", "col"), P("row", "col"), P(), P())
    return jax.shard_map(
        body,
        mesh=mesh,
        in_specs=placed,
        out_specs=(P(None, None, "row", "col"), P()),
        check_vma=False,
    )
```

```python
import functools
import math

import jax
import jax.numpy as jnp
from jax import lax
from jax.experimental import pallas as pl
from jax.experimental.pallas import tpu as pltpu
from jax.sharding import PartitionSpec as P

KDEN = 16
NS_STEPS = 5


def rotate(values, phase_angle):
    cosine = jnp.cos(phase_angle)
    sine_part = jnp.sin(phase_angle)
    return jnp.stack(
        [values[0] * cosine - values[1] * sine_part, values[0] * sine_part + values[1] * cosine]
    )


def stencil(padded, stiff_pad):
    centre = stiff_pad[1:-1, 1:-1]
    upward = 0.5 * (centre + stiff_pad[:-2, 1:-1])
    downward = 0.5 * (centre + stiff_pad[2:, 1:-1])
    leftward = 0.5 * (centre + stiff_pad[1:-1, :-2])
    rightward = 0.5 * (centre + stiff_pad[1:-1, 2:])
    diagonal = upward + downward + leftward + rightward
    inner_cells = padded[:, :, 1:-1, 1:-1]
    neighbours = (
        upward * padded[:, :, :-2, 1:-1]
        + downward * padded[:, :, 2:, 1:-1]
        + leftward * padded[:, :, 1:-1, :-2]
        + rightward * padded[:, :, 1:-1, 2:]
    )
    return (diagonal * inner_cells - neighbours, diagonal)


def complex_gram(first_block, second_block):
    count = first_block.shape[1]
    first_flat = first_block.reshape((2 * count,) + first_block.shape[2:])
    second_flat = second_block.reshape((2 * count,) + second_block.shape[2:])
    products = jnp.einsum(
        "jrc,krc->jk", first_flat, second_flat, precision=lax.Precision.HIGHEST
    )
    real_part = products[:count, :count] + products[count:, count:]
    imag_part = products[:count, count:] - products[count:, :count]
    return (real_part, imag_part)


def inverse_root(gram_real, gram_imag):
    highest = lax.Precision.HIGHEST
    order_size = gram_real.shape[0]
    upper_half = jnp.concatenate([gram_real, -gram_imag], axis=1)
    lower_half = jnp.concatenate([gram_imag, gram_real], axis=1)
    embedded = jnp.concatenate([upper_half, lower_half], axis=0)
    magnitude = jnp.sqrt(jnp.sum(embedded * embedded))
    identity = jnp.eye(2 * order_size, dtype=embedded.dtype)

    def newton(turn_index, carried):
        current, inverse = carried
        factor = 1.5 * identity - 0.5 * jnp.dot(inverse, current, precision=highest)
        return (
            jnp.dot(current, factor, precision=highest),
            jnp.dot(factor, inverse, precision=highest),
        )

    current, inverse = lax.fori_loop(0, NS_STEPS, newton, (embedded / magnitude, identity))
    root_full = inverse / jnp.sqrt(magnitude)
    return (root_full[:order_size, :order_size], root_full[order_size:, :order_size])


def reduce_matrix(root_real, root_imag, ham_real, ham_imag):
    highest = lax.Precision.HIGHEST
    prod_real = jnp.dot(ham_real, root_real, precision=highest) - jnp.dot(
        ham_imag, root_imag, precision=highest
    )
    prod_imag = jnp.dot(ham_real, root_imag, precision=highest) + jnp.dot(
        ham_imag, root_real, precision=highest
    )
    red_real = jnp.dot(root_real.T, prod_real, precision=highest) + jnp.dot(
        root_imag.T, prod_imag, precision=highest
    )
    red_imag = jnp.dot(root_real.T, prod_imag, precision=highest) - jnp.dot(
        root_imag.T, prod_real, precision=highest
    )
    return jnp.stack([red_real, red_imag])


def rotate_basis(raw_basis, root_real, root_imag, scale_factor):
    highest = lax.Precision.HIGHEST
    basis_real = jnp.einsum("jrc,jk->krc", raw_basis[0], root_real, precision=highest) - jnp.einsum(
        "jrc,jk->krc", raw_basis[1], root_imag, precision=highest
    )
    basis_imag = jnp.einsum("jrc,jk->krc", raw_basis[0], root_imag, precision=highest) + jnp.einsum(
        "jrc,jk->krc", raw_basis[1], root_real, precision=highest
    )
    return scale_factor * jnp.stack([basis_real, basis_imag])


def project_mixing(mixing, matrix):
    highest = lax.Precision.HIGHEST
    return jnp.dot(mixing.T, jnp.dot(matrix, mixing, precision=highest), precision=highest)


def exchange_rim(cells, axis, dim, width, strips=None):
    count = lax.axis_size(axis)
    if strips is None:
        head = lax.slice_in_dim(cells, 0, width, axis=dim)
        tail = lax.slice_in_dim(cells, cells.shape[dim] - width, cells.shape[dim], axis=dim)
    else:
        head, tail = strips
    if count % 2:
        before = lax.ppermute(tail.reshape(-1), axis, [(i, (i + 1) % count) for i in range(count)])
        after = lax.ppermute(head.reshape(-1), axis, [((i + 1) % count, i) for i in range(count)])
    else:
        even = lax.axis_index(axis) % 2 == 0
        first = lax.ppermute(
            jnp.where(even, tail, head).reshape(-1), axis, [(i, i ^ 1) for i in range(count)]
        )
        second = lax.ppermute(
            jnp.where(even, head, tail).reshape(-1),
            axis,
            [(i, (i + 1) % count if i % 2 else (i - 1) % count) for i in range(count)],
        )
        before = jnp.where(even, second, first)
        after = jnp.where(even, first, second)
    before = before.reshape(tail.shape)
    after = after.reshape(head.shape)
    return jnp.concatenate([before, cells, after], axis=dim)


def tree_sum(value, axis):
    count = lax.axis_size(axis)
    if count & (count - 1):
        return lax.psum(value, axis)
    step = 1
    while step < count:
        value = value + lax.ppermute(value, axis, [(i, i ^ step) for i in range(count)])
        step *= 2
    return value


def pack_hermitian(real_part, imag_part):
    order_size = real_part.shape[0]
    upper = jnp.arange(order_size)[:, None] <= jnp.arange(order_size)[None, :]
    return jnp.where(upper, real_part, imag_part)


def unpack_hermitian(packed):
    order_size = packed.shape[0]
    upper = jnp.arange(order_size)[:, None] <= jnp.arange(order_size)[None, :]
    strict_upper = jnp.arange(order_size)[:, None] < jnp.arange(order_size)[None, :]
    real_upper = jnp.where(upper, packed, 0.0)
    real_part = real_upper + jnp.where(strict_upper, packed, 0.0).T
    imag_lower = jnp.where(upper, 0.0, packed)
    return (real_part, imag_lower - imag_lower.T)


def matrix_kernel(packed_ref, field_ref, basis_ref, red_ref, work_ref, *, band_count, scale):
    highest = lax.Precision.HIGHEST

    def dot(first, second):
        return jnp.dot(first, second, precision=highest, preferred_element_type=jnp.float32)

    size = work_ref.shape[-1]
    ext = packed_ref.shape[-1]
    raw = 3 * band_count
    half = size // 2
    work_ref[...] = jnp.zeros(work_ref.shape, jnp.float32)
    work_ref[0, :ext, :ext] = packed_ref[0]
    work_ref[1, :ext, :ext] = packed_ref[1]
    rows = lax.broadcasted_iota(jnp.int32, (size, size), 0)
    cols = lax.broadcasted_iota(jnp.int32, (size, size), 1)
    upper = rows <= cols
    strict = rows < cols
    eye = rows == cols
    corner = (rows < half) & (cols < half)

    def spread(value, axis):
        return pltpu.roll(value, half, axis)

    def embed(real_part, imag_part):
        return real_part + spread(spread(real_part, 0), 1) - spread(imag_part, 1) + spread(imag_part, 0)

    def unpack(packed):
        real_part = jnp.where(upper, packed, 0.0) + jnp.where(strict, packed, 0.0).T
        lower = jnp.where(upper, 0.0, packed)
        return real_part, lower - lower.T

    gram_re, gram_im = unpack(work_ref[0])
    ham_re, ham_im = unpack(work_ref[1])
    band_diag = eye & (rows < band_count)
    quotient = jnp.where(band_diag, ham_re, 0.0) / jnp.where(band_diag, gram_re, 1.0)
    to_row = ((rows == cols + 2 * band_count) & (cols < band_count)).astype(jnp.float32)
    to_col = ((cols == rows + band_count) & (rows < band_count)).astype(jnp.float32)
    shifted = dot(dot(to_row, quotient), to_col)
    kept = (eye & (cols < 2 * band_count)) | (
        (rows == cols + band_count) & (cols >= 2 * band_count) & (cols < raw)
    )
    mixing = kept.astype(jnp.float32) - shifted
    mixing = mixing + spread(spread(mixing, 0), 1)
    embedded = dot(mixing.T, dot(embed(gram_re, gram_im), mixing))
    active = (rows < raw) | ((rows >= half) & (rows < half + raw))
    identity = (eye & active).astype(jnp.float32)
    total = jnp.sum(jnp.sum(embedded * embedded, axis=0, keepdims=True), axis=1, keepdims=True)
    magnitude = jnp.sqrt(total)
    current = embedded / magnitude
    inverse = identity
    for _ in range(NS_STEPS):
        factor = 1.5 * identity - 0.5 * dot(inverse, current)
        both = dot(factor, jnp.concatenate([current, inverse], axis=1))
        current, inverse = both[:, :size], both[:, size:]
    root = inverse / jnp.sqrt(magnitude)
    root = embed(jnp.where(corner, root, 0.0), jnp.where(corner, spread(root, 0), 0.0))
    rotation = dot(mixing, root)
    work_ref[1] = dot(rotation.T, dot(embed(ham_re, ham_im), rotation))
    red_ref[:, 0, :] = work_ref[1, :raw, :raw]
    red_ref[:, 1, :] = work_ref[1, half : half + raw, :raw]
    rotation = jnp.where(corner | ~((rows < half) | (cols < half)), rotation, -rotation)
    pick_rows = ((rows < ext) & (cols == rows)) | (
        (rows >= ext) & (rows < 2 * ext) & (cols == rows - ext + half)
    )
    pick_cols = ((rows < raw) & (cols == rows)) | (
        (rows >= half) & (rows < half + raw) & (cols == rows - half + raw)
    )
    packed_rotation = dot(pick_rows.astype(jnp.float32), dot(rotation, pick_cols.astype(jnp.float32)))
    work_ref[0] = scale * packed_rotation.T
    rotation_t = work_ref[0, : 2 * raw, : 2 * ext]
    lanes = field_ref.shape[2]
    row_count = field_ref.shape[1]
    rotated = dot(
        rotation_t, jnp.concatenate([field_ref[:, row, :] for row in range(row_count)], axis=1)
    )
    for row in range(row_count):
        basis_ref[:, row, :] = rotated[:, row * lanes : (row + 1) * lanes]


def matrix_stage(packed, fields, band_count, scale):
    size = 128
    raw = 3 * band_count
    vmem = pl.BlockSpec(memory_space=pltpu.VMEM)
    return pl.pallas_call(
        functools.partial(matrix_kernel, band_count=band_count, scale=scale),
        out_shape=(
            jax.ShapeDtypeStruct((2 * raw,) + fields.shape[1:], jnp.float32),
            jax.ShapeDtypeStruct((raw, 2, raw), jnp.float32),
        ),
        in_specs=[vmem, vmem],
        out_specs=(vmem, vmem),
        scratch_shapes=[pltpu.VMEM((2, size, size), jnp.float32)],
    )(packed, fields)


def body(bands, directions, materials, permittivity, wavevector):
    band_count = bands.shape[1]
    height = bands.shape[2]
    breadth = bands.shape[3]
    levels = jnp.arange(permittivity.shape[0], dtype=jnp.int32)

    def stiffness_of(cells):
        return jnp.sum(
            jnp.where(
                cells[None] == levels.astype(jnp.float32)[:, None, None],
                (1.0 / permittivity)[:, None, None],
                0.0,
            ),
            axis=0,
        )

    def strip_of(start, stop):
        field_rows = jnp.concatenate(
            [bands[:, :, start:stop], directions[:, :, start:stop]], axis=1
        ).reshape(4 * band_count, stop - start, breadth)
        return jnp.concatenate([field_rows, material_grid[None, start:stop]], axis=0)

    material_grid = materials.astype(jnp.float32)
    angle_row = 2.0 * math.pi * wavevector[0].astype(jnp.float32) / KDEN
    angle_col = 2.0 * math.pi * wavevector[1].astype(jnp.float32) / KDEN
    row_index = lax.axis_index("row")
    col_index = lax.axis_index("col")
    fields = jnp.concatenate([bands, directions], axis=1)
    packed = jnp.concatenate(
        [fields.reshape(4 * band_count, height, breadth), material_grid[None]], axis=0
    )
    padded = exchange_rim(packed, "row", 1, 2, (strip_of(0, 2), strip_of(height - 2, height)))
    padded = exchange_rim(padded, "col", 2, 2)
    stiff_wide = stiffness_of(padded[-1])
    field_wide = padded[:-1].reshape(2, 2 * band_count, height + 4, breadth + 4)
    row_place = jnp.arange(height + 4)
    col_place = jnp.arange(breadth + 4)
    row_phase = jnp.where(row_place < 2, jnp.where(row_index == 0, -angle_row, 0.0), 0.0) + jnp.where(
        row_place >= height + 2, jnp.where(row_index == lax.axis_size("row") - 1, angle_row, 0.0), 0.0
    )
    col_phase = jnp.where(col_place < 2, jnp.where(col_index == 0, -angle_col, 0.0), 0.0) + jnp.where(
        col_place >= breadth + 2, jnp.where(col_index == lax.axis_size("col") - 1, angle_col, 0.0), 0.0
    )
    field_wide = rotate(field_wide, row_phase[:, None] + col_phase[None, :])
    band_wide = field_wide[:, :band_count]
    applied_ring, diagonal_ring = stencil(band_wide, stiff_wide)
    stiff_ring = stiff_wide[1:-1, 1:-1]
    scaled_ring = jnp.concatenate(
        [
            applied_ring / diagonal_ring,
            band_wide[:, :, 1:-1, 1:-1] / diagonal_ring,
            field_wide[:, band_count:, 1:-1, 1:-1],
        ],
        axis=1,
    )
    extra_applied = stencil(scaled_ring, stiff_ring)[0]
    applied_cycle = applied_ring[:, :, 1:-1, 1:-1]
    scaled_image = scaled_ring[:, :band_count, 1:-1, 1:-1]
    scaled_bands = scaled_ring[:, band_count : 2 * band_count, 1:-1, 1:-1]
    extended = jnp.concatenate([bands, scaled_image, scaled_bands, directions], axis=1)
    extended_applied = jnp.concatenate([applied_cycle, extra_applied], axis=1)
    local_gram = complex_gram(extended, extended)
    local_ham = complex_gram(extended, extended_applied)
    summed = jnp.stack([pack_hermitian(*local_gram), pack_hermitian(*local_ham)])
    summed = tree_sum(tree_sum(summed.reshape(-1), "row"), "col").reshape(summed.shape)
    raw_count = 3 * band_count
    ext_count = 4 * band_count
    scale_factor = math.sqrt(height * breadth * lax.axis_size("row") * lax.axis_size("col"))
    basis, red = matrix_stage(
        summed, extended.reshape(2 * ext_count, height, breadth), band_count, scale_factor
    )
    reduced = jnp.transpose(red, (1, 0, 2))
    basis = basis.reshape(2, raw_count, height, breadth)
    return (basis, reduced)


def solution(mesh):
    placed = (P(None, None, "row", "col"), P(None, None, "row", "col"), P("row", "col"), P(), P())
    return jax.shard_map(
        body,
        mesh=mesh,
        in_specs=placed,
        out_specs=(P(None, None, "row", "col"), P()),
        check_vma=False,
    )
```

```python
import functools
import math

import jax
import jax.numpy as jnp
from jax import lax
from jax.experimental import pallas as pl
from jax.experimental.pallas import tpu as pltpu
from jax.sharding import PartitionSpec as P

KDEN = 16
NS_STEPS = 5


def rotate(values, phase_angle):
    cosine = jnp.cos(phase_angle)
    sine_part = jnp.sin(phase_angle)
    return jnp.stack(
        [values[0] * cosine - values[1] * sine_part, values[0] * sine_part + values[1] * cosine]
    )


def stencil(padded, stiff_pad):
    centre = stiff_pad[1:-1, 1:-1]
    upward = 0.5 * (centre + stiff_pad[:-2, 1:-1])
    downward = 0.5 * (centre + stiff_pad[2:, 1:-1])
    leftward = 0.5 * (centre + stiff_pad[1:-1, :-2])
    rightward = 0.5 * (centre + stiff_pad[1:-1, 2:])
    diagonal = upward + downward + leftward + rightward
    inner_cells = padded[:, :, 1:-1, 1:-1]
    neighbours = (
        upward * padded[:, :, :-2, 1:-1]
        + downward * padded[:, :, 2:, 1:-1]
        + leftward * padded[:, :, 1:-1, :-2]
        + rightward * padded[:, :, 1:-1, 2:]
    )
    return (diagonal * inner_cells - neighbours, diagonal)


def complex_gram(first_block, second_block):
    count = first_block.shape[1]
    first_flat = first_block.reshape((2 * count,) + first_block.shape[2:])
    second_flat = second_block.reshape((2 * count,) + second_block.shape[2:])
    products = jnp.einsum(
        "jrc,krc->jk", first_flat, second_flat, precision=lax.Precision.HIGHEST
    )
    real_part = products[:count, :count] + products[count:, count:]
    imag_part = products[:count, count:] - products[count:, :count]
    return (real_part, imag_part)


def inverse_root(gram_real, gram_imag):
    highest = lax.Precision.HIGHEST
    order_size = gram_real.shape[0]
    upper_half = jnp.concatenate([gram_real, -gram_imag], axis=1)
    lower_half = jnp.concatenate([gram_imag, gram_real], axis=1)
    embedded = jnp.concatenate([upper_half, lower_half], axis=0)
    magnitude = jnp.sqrt(jnp.sum(embedded * embedded))
    identity = jnp.eye(2 * order_size, dtype=embedded.dtype)

    def newton(turn_index, carried):
        current, inverse = carried
        factor = 1.5 * identity - 0.5 * jnp.dot(inverse, current, precision=highest)
        return (
            jnp.dot(current, factor, precision=highest),
            jnp.dot(factor, inverse, precision=highest),
        )

    current, inverse = lax.fori_loop(0, NS_STEPS, newton, (embedded / magnitude, identity))
    root_full = inverse / jnp.sqrt(magnitude)
    return (root_full[:order_size, :order_size], root_full[order_size:, :order_size])


def reduce_matrix(root_real, root_imag, ham_real, ham_imag):
    highest = lax.Precision.HIGHEST
    prod_real = jnp.dot(ham_real, root_real, precision=highest) - jnp.dot(
        ham_imag, root_imag, precision=highest
    )
    prod_imag = jnp.dot(ham_real, root_imag, precision=highest) + jnp.dot(
        ham_imag, root_real, precision=highest
    )
    red_real = jnp.dot(root_real.T, prod_real, precision=highest) + jnp.dot(
        root_imag.T, prod_imag, precision=highest
    )
    red_imag = jnp.dot(root_real.T, prod_imag, precision=highest) - jnp.dot(
        root_imag.T, prod_real, precision=highest
    )
    return jnp.stack([red_real, red_imag])


def rotate_basis(raw_basis, root_real, root_imag, scale_factor):
    highest = lax.Precision.HIGHEST
    basis_real = jnp.einsum("jrc,jk->krc", raw_basis[0], root_real, precision=highest) - jnp.einsum(
        "jrc,jk->krc", raw_basis[1], root_imag, precision=highest
    )
    basis_imag = jnp.einsum("jrc,jk->krc", raw_basis[0], root_imag, precision=highest) + jnp.einsum(
        "jrc,jk->krc", raw_basis[1], root_real, precision=highest
    )
    return scale_factor * jnp.stack([basis_real, basis_imag])


def project_mixing(mixing, matrix):
    highest = lax.Precision.HIGHEST
    return jnp.dot(mixing.T, jnp.dot(matrix, mixing, precision=highest), precision=highest)


def exchange_rim(cells, axis, dim, width, strips=None, angle=None):
    count = lax.axis_size(axis)
    if strips is None:
        head = lax.slice_in_dim(cells, 0, width, axis=dim)
        tail = lax.slice_in_dim(cells, cells.shape[dim] - width, cells.shape[dim], axis=dim)
    else:
        head, tail = strips
    if count % 2:
        before = lax.ppermute(tail.reshape(-1), axis, [(i, (i + 1) % count) for i in range(count)])
        after = lax.ppermute(head.reshape(-1), axis, [((i + 1) % count, i) for i in range(count)])
    else:
        even = lax.axis_index(axis) % 2 == 0
        first = lax.ppermute(
            jnp.where(even, tail, head).reshape(-1), axis, [(i, i ^ 1) for i in range(count)]
        )
        second = lax.ppermute(
            jnp.where(even, head, tail).reshape(-1),
            axis,
            [(i, (i + 1) % count if i % 2 else (i - 1) % count) for i in range(count)],
        )
        before = jnp.where(even, second, first)
        after = jnp.where(even, first, second)
    if angle is not None:
        index = lax.axis_index(axis)
        before = turn_flat(before, jnp.where(index == 0, -angle, 0.0), cells.shape[0])
        after = turn_flat(after, jnp.where(index == count - 1, angle, 0.0), cells.shape[0])
    before = before.reshape(tail.shape)
    after = after.reshape(head.shape)
    return jnp.concatenate([before, cells, after], axis=dim)


def turn_flat(flat, phase_angle, channels):
    share = flat.shape[0] // channels
    half = (channels - 1) // 2 * share
    turned = rotate(jnp.stack([flat[:half], flat[half : 2 * half]]), phase_angle)
    return jnp.concatenate([turned[0], turned[1], flat[2 * half :]])


def tree_sum(value, axis):
    count = lax.axis_size(axis)
    if count & (count - 1):
        return lax.psum(value, axis)
    step = 1
    while step < count:
        value = value + lax.ppermute(value, axis, [(i, i ^ step) for i in range(count)])
        step *= 2
    return value


def pack_hermitian(real_part, imag_part):
    order_size = real_part.shape[0]
    upper = jnp.arange(order_size)[:, None] <= jnp.arange(order_size)[None, :]
    return jnp.where(upper, real_part, imag_part)


def unpack_hermitian(packed):
    order_size = packed.shape[0]
    upper = jnp.arange(order_size)[:, None] <= jnp.arange(order_size)[None, :]
    strict_upper = jnp.arange(order_size)[:, None] < jnp.arange(order_size)[None, :]
    real_upper = jnp.where(upper, packed, 0.0)
    real_part = real_upper + jnp.where(strict_upper, packed, 0.0).T
    imag_lower = jnp.where(upper, 0.0, packed)
    return (real_part, imag_lower - imag_lower.T)


def matrix_kernel(packed_ref, field_ref, basis_ref, red_ref, work_ref, *, band_count, scale):
    highest = lax.Precision.HIGHEST

    def dot(first, second):
        return jnp.dot(first, second, precision=highest, preferred_element_type=jnp.float32)

    size = work_ref.shape[-1]
    ext = packed_ref.shape[-1]
    raw = 3 * band_count
    half = size // 2
    work_ref[...] = jnp.zeros(work_ref.shape, jnp.float32)
    work_ref[0, :ext, :ext] = packed_ref[0]
    work_ref[1, :ext, :ext] = packed_ref[1]
    rows = lax.broadcasted_iota(jnp.int32, (size, size), 0)
    cols = lax.broadcasted_iota(jnp.int32, (size, size), 1)
    upper = rows <= cols
    strict = rows < cols
    eye = rows == cols
    corner = (rows < half) & (cols < half)

    def spread(value, axis):
        return pltpu.roll(value, half, axis)

    def embed(real_part, imag_part):
        return real_part + spread(spread(real_part, 0), 1) - spread(imag_part, 1) + spread(imag_part, 0)

    def unpack(packed):
        real_part = jnp.where(upper, packed, 0.0) + jnp.where(strict, packed, 0.0).T
        lower = jnp.where(upper, 0.0, packed)
        return real_part, lower - lower.T

    gram_re, gram_im = unpack(work_ref[0])
    ham_re, ham_im = unpack(work_ref[1])
    band_diag = eye & (rows < band_count)
    quotient = jnp.where(band_diag, ham_re, 0.0) / jnp.where(band_diag, gram_re, 1.0)
    to_row = ((rows == cols + 2 * band_count) & (cols < band_count)).astype(jnp.float32)
    to_col = ((cols == rows + band_count) & (rows < band_count)).astype(jnp.float32)
    shifted = dot(dot(to_row, quotient), to_col)
    kept = (eye & (cols < 2 * band_count)) | (
        (rows == cols + band_count) & (cols >= 2 * band_count) & (cols < raw)
    )
    mixing = kept.astype(jnp.float32) - shifted
    mixing = mixing + spread(spread(mixing, 0), 1)
    embedded = dot(mixing.T, dot(embed(gram_re, gram_im), mixing))
    active = (rows < raw) | ((rows >= half) & (rows < half + raw))
    identity = (eye & active).astype(jnp.float32)
    total = jnp.sum(jnp.sum(embedded * embedded, axis=0, keepdims=True), axis=1, keepdims=True)
    magnitude = jnp.sqrt(total)
    current = embedded / magnitude
    inverse = identity
    for _ in range(NS_STEPS):
        factor = 1.5 * identity - 0.5 * dot(inverse, current)
        current, inverse = dot(current, factor), dot(factor, inverse)
    root = inverse / jnp.sqrt(magnitude)
    root = embed(jnp.where(corner, root, 0.0), jnp.where(corner, spread(root, 0), 0.0))
    rotation = dot(mixing, root)
    work_ref[1] = dot(rotation.T, dot(embed(ham_re, ham_im), rotation))
    red_ref[:, 0, :] = work_ref[1, :raw, :raw]
    red_ref[:, 1, :] = work_ref[1, half : half + raw, :raw]
    rotation = jnp.where(corner | ~((rows < half) | (cols < half)), rotation, -rotation)
    pick_rows = ((rows < ext) & (cols == rows)) | (
        (rows >= ext) & (rows < 2 * ext) & (cols == rows - ext + half)
    )
    pick_cols = ((rows < raw) & (cols == rows)) | (
        (rows >= half) & (rows < half + raw) & (cols == rows - half + raw)
    )
    packed_rotation = dot(pick_rows.astype(jnp.float32), dot(rotation, pick_cols.astype(jnp.float32)))
    work_ref[0] = scale * packed_rotation.T
    rotation_t = work_ref[0, : 2 * raw, : 2 * ext]
    for row in range(field_ref.shape[1]):
        basis_ref[:, row, :] = dot(rotation_t, field_ref[:, row, :])


def matrix_stage(packed, fields, band_count, scale):
    size = 128
    raw = 3 * band_count
    vmem = pl.BlockSpec(memory_space=pltpu.VMEM)
    return pl.pallas_call(
        functools.partial(matrix_kernel, band_count=band_count, scale=scale),
        out_shape=(
            jax.ShapeDtypeStruct((2 * raw,) + fields.shape[1:], jnp.float32),
            jax.ShapeDtypeStruct((raw, 2, raw), jnp.float32),
        ),
        in_specs=[vmem, vmem],
        out_specs=(vmem, vmem),
        scratch_shapes=[pltpu.VMEM((2, size, size), jnp.float32)],
    )(packed, fields)


def body(bands, directions, materials, permittivity, wavevector):
    band_count = bands.shape[1]
    height = bands.shape[2]
    breadth = bands.shape[3]
    levels = jnp.arange(permittivity.shape[0], dtype=jnp.int32)

    def stiffness_of(cells):
        return jnp.sum(
            jnp.where(
                cells[None] == levels.astype(jnp.float32)[:, None, None],
                (1.0 / permittivity)[:, None, None],
                0.0,
            ),
            axis=0,
        )

    def strip_of(start, stop):
        field_rows = jnp.concatenate(
            [bands[:, :, start:stop], directions[:, :, start:stop]], axis=1
        ).reshape(4 * band_count, stop - start, breadth)
        return jnp.concatenate([field_rows, material_grid[None, start:stop]], axis=0)

    material_grid = materials.astype(jnp.float32)
    angle_row = 2.0 * math.pi * wavevector[0].astype(jnp.float32) / KDEN
    angle_col = 2.0 * math.pi * wavevector[1].astype(jnp.float32) / KDEN
    fields = jnp.concatenate([bands, directions], axis=1)
    packed = jnp.concatenate(
        [fields.reshape(4 * band_count, height, breadth), material_grid[None]], axis=0
    )
    padded = exchange_rim(
        packed, "row", 1, 2, (strip_of(0, 2), strip_of(height - 2, height)), angle_row
    )
    padded = exchange_rim(padded, "col", 2, 2, angle=angle_col)
    stiff_wide = stiffness_of(padded[-1])
    field_wide = padded[:-1].reshape(2, 2 * band_count, height + 4, breadth + 4)
    band_wide = field_wide[:, :band_count]
    applied_ring, diagonal_ring = stencil(band_wide, stiff_wide)
    stiff_ring = stiff_wide[1:-1, 1:-1]
    scaled_ring = jnp.concatenate(
        [
            applied_ring / diagonal_ring,
            band_wide[:, :, 1:-1, 1:-1] / diagonal_ring,
            field_wide[:, band_count:, 1:-1, 1:-1],
        ],
        axis=1,
    )
    extra_applied = stencil(scaled_ring, stiff_ring)[0]
    applied_cycle = applied_ring[:, :, 1:-1, 1:-1]
    scaled_image = scaled_ring[:, :band_count, 1:-1, 1:-1]
    scaled_bands = scaled_ring[:, band_count : 2 * band_count, 1:-1, 1:-1]
    extended = jnp.concatenate([bands, scaled_image, scaled_bands, directions], axis=1)
    extended_applied = jnp.concatenate([applied_cycle, extra_applied], axis=1)
    local_gram = complex_gram(extended, extended)
    local_ham = complex_gram(extended, extended_applied)
    summed = jnp.stack([pack_hermitian(*local_gram), pack_hermitian(*local_ham)])
    summed = tree_sum(tree_sum(summed.reshape(-1), "row"), "col").reshape(summed.shape)
    raw_count = 3 * band_count
    ext_count = 4 * band_count
    scale_factor = math.sqrt(height * breadth * lax.axis_size("row") * lax.axis_size("col"))
    basis, red = matrix_stage(
        summed, extended.reshape(2 * ext_count, height, breadth), band_count, scale_factor
    )
    reduced = jnp.transpose(red, (1, 0, 2))
    basis = basis.reshape(2, raw_count, height, breadth)
    return (basis, reduced)


def solution(mesh):
    placed = (P(None, None, "row", "col"), P(None, None, "row", "col"), P("row", "col"), P(), P())
    return jax.shard_map(
        body,
        mesh=mesh,
        in_specs=placed,
        out_specs=(P(None, None, "row", "col"), P()),
        check_vma=False,
    )
```

```python
import functools
import math

import jax
import jax.numpy as jnp
from jax import lax
from jax.experimental import pallas as pl
from jax.experimental.pallas import tpu as pltpu
from jax.sharding import PartitionSpec as P

KDEN = 16
NS_STEPS = 5


def rotate(values, phase_angle):
    cosine = jnp.cos(phase_angle)
    sine_part = jnp.sin(phase_angle)
    return jnp.stack(
        [values[0] * cosine - values[1] * sine_part, values[0] * sine_part + values[1] * cosine]
    )


def stencil(padded, stiff_pad):
    centre = stiff_pad[1:-1, 1:-1]
    upward = 0.5 * (centre + stiff_pad[:-2, 1:-1])
    downward = 0.5 * (centre + stiff_pad[2:, 1:-1])
    leftward = 0.5 * (centre + stiff_pad[1:-1, :-2])
    rightward = 0.5 * (centre + stiff_pad[1:-1, 2:])
    diagonal = upward + downward + leftward + rightward
    inner_cells = padded[:, :, 1:-1, 1:-1]
    neighbours = (
        upward * padded[:, :, :-2, 1:-1]
        + downward * padded[:, :, 2:, 1:-1]
        + leftward * padded[:, :, 1:-1, :-2]
        + rightward * padded[:, :, 1:-1, 2:]
    )
    return (diagonal * inner_cells - neighbours, diagonal)


def combine_parts(products, count):
    real_part = products[:count, :count] + products[count:, count:]
    imag_part = products[:count, count:] - products[count:, :count]
    return (real_part, imag_part)


def exchange_rim(cells, axis, dim, width, strips=None, angle=None):
    count = lax.axis_size(axis)
    if strips is None:
        head = lax.slice_in_dim(cells, 0, width, axis=dim)
        tail = lax.slice_in_dim(cells, cells.shape[dim] - width, cells.shape[dim], axis=dim)
    else:
        head, tail = strips
    if count % 2:
        before = lax.ppermute(tail.reshape(-1), axis, [(i, (i + 1) % count) for i in range(count)])
        after = lax.ppermute(head.reshape(-1), axis, [((i + 1) % count, i) for i in range(count)])
    else:
        even = lax.axis_index(axis) % 2 == 0
        first = lax.ppermute(
            jnp.where(even, tail, head).reshape(-1), axis, [(i, i ^ 1) for i in range(count)]
        )
        second = lax.ppermute(
            jnp.where(even, head, tail).reshape(-1),
            axis,
            [(i, (i + 1) % count if i % 2 else (i - 1) % count) for i in range(count)],
        )
        before = jnp.where(even, second, first)
        after = jnp.where(even, first, second)
    if angle is not None:
        index = lax.axis_index(axis)
        before = turn_flat(before, jnp.where(index == 0, -angle, 0.0), cells.shape[0])
        after = turn_flat(after, jnp.where(index == count - 1, angle, 0.0), cells.shape[0])
    before = before.reshape(tail.shape)
    after = after.reshape(head.shape)
    return jnp.concatenate([before, cells, after], axis=dim)


def turn_flat(flat, phase_angle, channels):
    share = flat.shape[0] // channels
    half = (channels - 1) // 2 * share
    turned = rotate(jnp.stack([flat[:half], flat[half : 2 * half]]), phase_angle)
    return jnp.concatenate([turned[0], turned[1], flat[2 * half :]])


def tree_sum(value, axis):
    count = lax.axis_size(axis)
    if count & (count - 1):
        return lax.psum(value, axis)
    step = 1
    while step < count:
        value = value + lax.ppermute(value, axis, [(i, i ^ step) for i in range(count)])
        step *= 2
    return value


def pack_hermitian(real_part, imag_part):
    order_size = real_part.shape[0]
    upper = jnp.arange(order_size)[:, None] <= jnp.arange(order_size)[None, :]
    return jnp.where(upper, real_part, imag_part)


def unpack_hermitian(packed):
    order_size = packed.shape[0]
    upper = jnp.arange(order_size)[:, None] <= jnp.arange(order_size)[None, :]
    strict_upper = jnp.arange(order_size)[:, None] < jnp.arange(order_size)[None, :]
    real_upper = jnp.where(upper, packed, 0.0)
    real_part = real_upper + jnp.where(strict_upper, packed, 0.0).T
    imag_lower = jnp.where(upper, 0.0, packed)
    return (real_part, imag_lower - imag_lower.T)


def matrix_kernel(packed_ref, field_ref, basis_ref, red_ref, work_ref, *, band_count, scale):
    highest = lax.Precision.HIGHEST

    def dot(first, second):
        return jnp.dot(first, second, precision=highest, preferred_element_type=jnp.float32)

    size = work_ref.shape[-1]
    ext = packed_ref.shape[-1]
    raw = 3 * band_count
    half = size // 2
    work_ref[...] = jnp.zeros(work_ref.shape, jnp.float32)
    work_ref[0, :ext, :ext] = packed_ref[0]
    work_ref[1, :ext, :ext] = packed_ref[1]
    rows = lax.broadcasted_iota(jnp.int32, (size, size), 0)
    cols = lax.broadcasted_iota(jnp.int32, (size, size), 1)
    upper = rows <= cols
    strict = rows < cols
    eye = rows == cols
    corner = (rows < half) & (cols < half)

    def spread(value, axis):
        return pltpu.roll(value, half, axis)

    def embed(real_part, imag_part):
        return real_part + spread(spread(real_part, 0), 1) - spread(imag_part, 1) + spread(imag_part, 0)

    def unpack(packed):
        real_part = jnp.where(upper, packed, 0.0) + jnp.where(strict, packed, 0.0).T
        lower = jnp.where(upper, 0.0, packed)
        return real_part, lower - lower.T

    gram_re, gram_im = unpack(work_ref[0])
    ham_re, ham_im = unpack(work_ref[1])
    band_diag = eye & (rows < band_count)
    quotient = jnp.where(band_diag, ham_re, 0.0) / jnp.where(band_diag, gram_re, 1.0)
    to_row = ((rows == cols + 2 * band_count) & (cols < band_count)).astype(jnp.float32)
    to_col = ((cols == rows + band_count) & (rows < band_count)).astype(jnp.float32)
    shifted = dot(dot(to_row, quotient), to_col)
    kept = (eye & (cols < 2 * band_count)) | (
        (rows == cols + band_count) & (cols >= 2 * band_count) & (cols < raw)
    )
    mixing = kept.astype(jnp.float32) - shifted
    mixing = mixing + spread(spread(mixing, 0), 1)
    embedded = dot(mixing.T, dot(embed(gram_re, gram_im), mixing))
    active = (rows < raw) | ((rows >= half) & (rows < half + raw))
    identity = (eye & active).astype(jnp.float32)
    total = jnp.sum(jnp.sum(embedded * embedded, axis=0, keepdims=True), axis=1, keepdims=True)
    magnitude = jnp.sqrt(total)
    current = embedded / magnitude
    inverse = identity
    for _ in range(NS_STEPS):
        factor = 1.5 * identity - 0.5 * dot(inverse, current)
        current, inverse = dot(current, factor), dot(factor, inverse)
    root = inverse / jnp.sqrt(magnitude)
    root = embed(jnp.where(corner, root, 0.0), jnp.where(corner, spread(root, 0), 0.0))
    rotation = dot(mixing, root)
    work_ref[1] = dot(rotation.T, dot(embed(ham_re, ham_im), rotation))
    red_ref[:, 0, :] = work_ref[1, :raw, :raw]
    red_ref[:, 1, :] = work_ref[1, half : half + raw, :raw]
    rotation = jnp.where(corner | ~((rows < half) | (cols < half)), rotation, -rotation)
    pick_rows = ((rows < ext) & (cols == rows)) | (
        (rows >= ext) & (rows < 2 * ext) & (cols == rows - ext + half)
    )
    pick_cols = ((rows < raw) & (cols == rows)) | (
        (rows >= half) & (rows < half + raw) & (cols == rows - half + raw)
    )
    packed_rotation = dot(pick_rows.astype(jnp.float32), dot(rotation, pick_cols.astype(jnp.float32)))
    work_ref[0] = scale * packed_rotation.T
    rotation_t = work_ref[0, : 2 * raw, : 2 * ext]
    for row in range(field_ref.shape[1]):
        basis_ref[:, row, :] = dot(rotation_t, field_ref[:, row, :])


def matrix_stage(packed, fields, band_count, scale):
    size = 128
    raw = 3 * band_count
    vmem = pl.BlockSpec(memory_space=pltpu.VMEM)
    return pl.pallas_call(
        functools.partial(matrix_kernel, band_count=band_count, scale=scale),
        out_shape=(
            jax.ShapeDtypeStruct((2 * raw,) + fields.shape[1:], jnp.float32),
            jax.ShapeDtypeStruct((raw, 2, raw), jnp.float32),
        ),
        in_specs=[vmem, vmem],
        out_specs=(vmem, vmem),
        scratch_shapes=[pltpu.VMEM((2, size, size), jnp.float32)],
    )(packed, fields)


def body(bands, directions, materials, permittivity, wavevector):
    band_count = bands.shape[1]
    height = bands.shape[2]
    breadth = bands.shape[3]
    levels = jnp.arange(permittivity.shape[0], dtype=jnp.int32)

    def stiffness_of(cells):
        return jnp.sum(
            jnp.where(
                cells[None] == levels.astype(jnp.float32)[:, None, None],
                (1.0 / permittivity)[:, None, None],
                0.0,
            ),
            axis=0,
        )

    def strip_of(start, stop):
        field_rows = jnp.concatenate(
            [bands[:, :, start:stop], directions[:, :, start:stop]], axis=1
        ).reshape(4 * band_count, stop - start, breadth)
        return jnp.concatenate([field_rows, material_grid[None, start:stop]], axis=0)

    material_grid = materials.astype(jnp.float32)
    angle_row = 2.0 * math.pi * wavevector[0].astype(jnp.float32) / KDEN
    angle_col = 2.0 * math.pi * wavevector[1].astype(jnp.float32) / KDEN
    fields = jnp.concatenate([bands, directions], axis=1)
    packed = jnp.concatenate(
        [fields.reshape(4 * band_count, height, breadth), material_grid[None]], axis=0
    )
    padded = exchange_rim(
        packed, "row", 1, 2, (strip_of(0, 2), strip_of(height - 2, height)), angle_row
    )
    padded = exchange_rim(padded, "col", 2, 2, angle=angle_col)
    stiff_wide = stiffness_of(padded[-1])
    field_wide = padded[:-1].reshape(2, 2 * band_count, height + 4, breadth + 4)
    band_wide = field_wide[:, :band_count]
    applied_ring, diagonal_ring = stencil(band_wide, stiff_wide)
    stiff_ring = stiff_wide[1:-1, 1:-1]
    scaled_ring = jnp.concatenate(
        [
            applied_ring / diagonal_ring,
            band_wide[:, :, 1:-1, 1:-1] / diagonal_ring,
            field_wide[:, band_count:, 1:-1, 1:-1],
        ],
        axis=1,
    )
    extra_applied = stencil(scaled_ring, stiff_ring)[0]
    applied_cycle = applied_ring[:, :, 1:-1, 1:-1]
    scaled_image = scaled_ring[:, :band_count, 1:-1, 1:-1]
    scaled_bands = scaled_ring[:, band_count : 2 * band_count, 1:-1, 1:-1]
    extended = jnp.concatenate([bands, scaled_image, scaled_bands, directions], axis=1)
    extended_applied = jnp.concatenate([applied_cycle, extra_applied], axis=1)
    count = extended.shape[1]
    products = jnp.einsum(
        "jrc,krc->jk",
        extended.reshape((2 * count,) + extended.shape[2:]),
        jnp.concatenate([extended, extended_applied], axis=0).reshape(
            (4 * count,) + extended.shape[2:]
        ),
        precision=lax.Precision.HIGHEST,
    )
    local_gram = combine_parts(products[:, : 2 * count], count)
    local_ham = combine_parts(products[:, 2 * count :], count)
    summed = jnp.stack([pack_hermitian(*local_gram), pack_hermitian(*local_ham)])
    summed = tree_sum(tree_sum(summed.reshape(-1), "row"), "col").reshape(summed.shape)
    raw_count = 3 * band_count
    ext_count = 4 * band_count
    scale_factor = math.sqrt(height * breadth * lax.axis_size("row") * lax.axis_size("col"))
    basis, red = matrix_stage(
        summed, extended.reshape(2 * ext_count, height, breadth), band_count, scale_factor
    )
    reduced = jnp.transpose(red, (1, 0, 2))
    basis = basis.reshape(2, raw_count, height, breadth)
    return (basis, reduced)


def solution(mesh):
    placed = (P(None, None, "row", "col"), P(None, None, "row", "col"), P("row", "col"), P(), P())
    return jax.shard_map(
        body,
        mesh=mesh,
        in_specs=placed,
        out_specs=(P(None, None, "row", "col"), P()),
        check_vma=False,
    )
```

```python
import functools
import math

import jax
import jax.numpy as jnp
from jax import lax
from jax.experimental import pallas as pl
from jax.experimental.pallas import tpu as pltpu
from jax.sharding import PartitionSpec as P

KDEN = 16
NS_STEPS = 5


def rotate(values, phase_angle):
    cosine = jnp.cos(phase_angle)
    sine_part = jnp.sin(phase_angle)
    return jnp.stack(
        [values[0] * cosine - values[1] * sine_part, values[0] * sine_part + values[1] * cosine]
    )


def stencil(padded, stiff_pad):
    centre = stiff_pad[1:-1, 1:-1]
    upward = 0.5 * (centre + stiff_pad[:-2, 1:-1])
    downward = 0.5 * (centre + stiff_pad[2:, 1:-1])
    leftward = 0.5 * (centre + stiff_pad[1:-1, :-2])
    rightward = 0.5 * (centre + stiff_pad[1:-1, 2:])
    diagonal = upward + downward + leftward + rightward
    inner_cells = padded[:, :, 1:-1, 1:-1]
    neighbours = (
        upward * padded[:, :, :-2, 1:-1]
        + downward * padded[:, :, 2:, 1:-1]
        + leftward * padded[:, :, 1:-1, :-2]
        + rightward * padded[:, :, 1:-1, 2:]
    )
    return (diagonal * inner_cells - neighbours, diagonal)


def complex_gram(first_block, second_block):
    count = first_block.shape[1]
    first_flat = first_block.reshape((2 * count,) + first_block.shape[2:])
    second_flat = second_block.reshape((2 * count,) + second_block.shape[2:])
    products = jnp.einsum(
        "jrc,krc->jk", first_flat, second_flat, precision=lax.Precision.HIGHEST
    )
    real_part = products[:count, :count] + products[count:, count:]
    imag_part = products[:count, count:] - products[count:, :count]
    return (real_part, imag_part)


def inverse_root(gram_real, gram_imag):
    highest = lax.Precision.HIGHEST
    order_size = gram_real.shape[0]
    upper_half = jnp.concatenate([gram_real, -gram_imag], axis=1)
    lower_half = jnp.concatenate([gram_imag, gram_real], axis=1)
    embedded = jnp.concatenate([upper_half, lower_half], axis=0)
    magnitude = jnp.sqrt(jnp.sum(embedded * embedded))
    identity = jnp.eye(2 * order_size, dtype=embedded.dtype)

    def newton(turn_index, carried):
        current, inverse = carried
        factor = 1.5 * identity - 0.5 * jnp.dot(inverse, current, precision=highest)
        return (
            jnp.dot(current, factor, precision=highest),
            jnp.dot(factor, inverse, precision=highest),
        )

    current, inverse = lax.fori_loop(0, NS_STEPS, newton, (embedded / magnitude, identity))
    root_full = inverse / jnp.sqrt(magnitude)
    return (root_full[:order_size, :order_size], root_full[order_size:, :order_size])


def reduce_matrix(root_real, root_imag, ham_real, ham_imag):
    highest = lax.Precision.HIGHEST
    prod_real = jnp.dot(ham_real, root_real, precision=highest) - jnp.dot(
        ham_imag, root_imag, precision=highest
    )
    prod_imag = jnp.dot(ham_real, root_imag, precision=highest) + jnp.dot(
        ham_imag, root_real, precision=highest
    )
    red_real = jnp.dot(root_real.T, prod_real, precision=highest) + jnp.dot(
        root_imag.T, prod_imag, precision=highest
    )
    red_imag = jnp.dot(root_real.T, prod_imag, precision=highest) - jnp.dot(
        root_imag.T, prod_real, precision=highest
    )
    return jnp.stack([red_real, red_imag])


def rotate_basis(raw_basis, root_real, root_imag, scale_factor):
    highest = lax.Precision.HIGHEST
    basis_real = jnp.einsum("jrc,jk->krc", raw_basis[0], root_real, precision=highest) - jnp.einsum(
        "jrc,jk->krc", raw_basis[1], root_imag, precision=highest
    )
    basis_imag = jnp.einsum("jrc,jk->krc", raw_basis[0], root_imag, precision=highest) + jnp.einsum(
        "jrc,jk->krc", raw_basis[1], root_real, precision=highest
    )
    return scale_factor * jnp.stack([basis_real, basis_imag])


def project_mixing(mixing, matrix):
    highest = lax.Precision.HIGHEST
    return jnp.dot(mixing.T, jnp.dot(matrix, mixing, precision=highest), precision=highest)


def exchange_rim(cells, axis, dim, width, strips=None, angle=None):
    count = lax.axis_size(axis)
    if strips is None:
        head = lax.slice_in_dim(cells, 0, width, axis=dim)
        tail = lax.slice_in_dim(cells, cells.shape[dim] - width, cells.shape[dim], axis=dim)
    else:
        head, tail = strips
    if count % 2:
        before = lax.ppermute(tail.reshape(-1), axis, [(i, (i + 1) % count) for i in range(count)])
        after = lax.ppermute(head.reshape(-1), axis, [((i + 1) % count, i) for i in range(count)])
    else:
        even = lax.axis_index(axis) % 2 == 0
        first = lax.ppermute(
            jnp.where(even, tail, head).reshape(-1), axis, [(i, i ^ 1) for i in range(count)]
        )
        second = lax.ppermute(
            jnp.where(even, head, tail).reshape(-1),
            axis,
            [(i, (i + 1) % count if i % 2 else (i - 1) % count) for i in range(count)],
        )
        before = jnp.where(even, second, first)
        after = jnp.where(even, first, second)
    if angle is not None:
        index = lax.axis_index(axis)
        before = turn_flat(before, jnp.where(index == 0, -angle, 0.0), cells.shape[0])
        after = turn_flat(after, jnp.where(index == count - 1, angle, 0.0), cells.shape[0])
    before = before.reshape(tail.shape)
    after = after.reshape(head.shape)
    return jnp.concatenate([before, cells, after], axis=dim)


def turn_flat(flat, phase_angle, channels):
    share = flat.shape[0] // channels
    half = (channels - 1) // 2 * share
    turned = rotate(jnp.stack([flat[:half], flat[half : 2 * half]]), phase_angle)
    return jnp.concatenate([turned[0], turned[1], flat[2 * half :]])


def tree_sum(value, axis):
    count = lax.axis_size(axis)
    if count & (count - 1):
        return lax.psum(value, axis)
    step = 1
    while step < count:
        value = value + lax.ppermute(value, axis, [(i, i ^ step) for i in range(count)])
        step *= 2
    return value


def pack_hermitian(real_part, imag_part):
    order_size = real_part.shape[0]
    upper = jnp.arange(order_size)[:, None] <= jnp.arange(order_size)[None, :]
    return jnp.where(upper, real_part, imag_part)


def unpack_hermitian(packed):
    order_size = packed.shape[0]
    upper = jnp.arange(order_size)[:, None] <= jnp.arange(order_size)[None, :]
    strict_upper = jnp.arange(order_size)[:, None] < jnp.arange(order_size)[None, :]
    real_upper = jnp.where(upper, packed, 0.0)
    real_part = real_upper + jnp.where(strict_upper, packed, 0.0).T
    imag_lower = jnp.where(upper, 0.0, packed)
    return (real_part, imag_lower - imag_lower.T)


def matrix_kernel(packed_ref, field_ref, basis_ref, red_ref, work_ref, *, band_count, scale):
    highest = lax.Precision.HIGHEST

    def dot(first, second):
        return jnp.dot(first, second, precision=highest, preferred_element_type=jnp.float32)

    size = work_ref.shape[-1]
    ext = packed_ref.shape[-1]
    raw = 3 * band_count
    half = size // 2
    work_ref[...] = jnp.zeros(work_ref.shape, jnp.float32)
    work_ref[0, :ext, :ext] = packed_ref[0]
    work_ref[1, :ext, :ext] = packed_ref[1]
    rows = lax.broadcasted_iota(jnp.int32, (size, size), 0)
    cols = lax.broadcasted_iota(jnp.int32, (size, size), 1)
    upper = rows <= cols
    strict = rows < cols
    eye = rows == cols
    corner = (rows < half) & (cols < half)

    def spread(value, axis):
        return pltpu.roll(value, half, axis)

    def embed(real_part, imag_part):
        return real_part + spread(spread(real_part, 0), 1) - spread(imag_part, 1) + spread(imag_part, 0)

    def unpack(packed):
        real_part = jnp.where(upper, packed, 0.0) + jnp.where(strict, packed, 0.0).T
        lower = jnp.where(upper, 0.0, packed)
        return real_part, lower - lower.T

    gram_re, gram_im = unpack(work_ref[0])
    ham_re, ham_im = unpack(work_ref[1])
    band_diag = eye & (rows < band_count)
    quotient = jnp.where(band_diag, ham_re, 0.0) / jnp.where(band_diag, gram_re, 1.0)
    to_row = ((rows == cols + 2 * band_count) & (cols < band_count)).astype(jnp.float32)
    to_col = ((cols == rows + band_count) & (rows < band_count)).astype(jnp.float32)
    shifted = dot(dot(to_row, quotient), to_col)
    kept = (eye & (cols < 2 * band_count)) | (
        (rows == cols + band_count) & (cols >= 2 * band_count) & (cols < raw)
    )
    mixing = kept.astype(jnp.float32) - shifted
    mixing = mixing + spread(spread(mixing, 0), 1)
    embedded = dot(mixing.T, dot(embed(gram_re, gram_im), mixing))
    active = (rows < raw) | ((rows >= half) & (rows < half + raw))
    identity = (eye & active).astype(jnp.float32)
    total = jnp.sum(jnp.sum(embedded * embedded, axis=0, keepdims=True), axis=1, keepdims=True)
    magnitude = jnp.sqrt(total)
    current = embedded / magnitude
    inverse = identity
    for _ in range(NS_STEPS):
        factor = 1.5 * identity - 0.5 * dot(inverse, current)
        current, inverse = dot(current, factor), dot(factor, inverse)
    root = inverse / jnp.sqrt(magnitude)
    root = embed(jnp.where(corner, root, 0.0), jnp.where(corner, spread(root, 0), 0.0))
    rotation = dot(mixing, root)
    work_ref[1] = dot(rotation.T, dot(embed(ham_re, ham_im), rotation))
    red_ref[:, 0, :] = work_ref[1, :raw, :raw]
    red_ref[:, 1, :] = work_ref[1, half : half + raw, :raw]
    rotation = jnp.where(corner | ~((rows < half) | (cols < half)), rotation, -rotation)
    pick_rows = ((rows < ext) & (cols == rows)) | (
        (rows >= ext) & (rows < 2 * ext) & (cols == rows - ext + half)
    )
    pick_cols = ((rows < raw) & (cols == rows)) | (
        (rows >= half) & (rows < half + raw) & (cols == rows - half + raw)
    )
    packed_rotation = dot(pick_rows.astype(jnp.float32), dot(rotation, pick_cols.astype(jnp.float32)))
    work_ref[0] = scale * packed_rotation.T
    rotation_t = work_ref[0, : 2 * raw, : 2 * ext]
    for row in range(field_ref.shape[1]):
        basis_ref[:, row, :] = dot(rotation_t, field_ref[:, row, :])


def matrix_stage(packed, fields, band_count, scale):
    size = 128
    raw = 3 * band_count
    vmem = pl.BlockSpec(memory_space=pltpu.VMEM)
    return pl.pallas_call(
        functools.partial(matrix_kernel, band_count=band_count, scale=scale),
        out_shape=(
            jax.ShapeDtypeStruct((2 * raw,) + fields.shape[1:], jnp.float32),
            jax.ShapeDtypeStruct((raw, 2, raw), jnp.float32),
        ),
        in_specs=[vmem, vmem],
        out_specs=(vmem, vmem),
        scratch_shapes=[pltpu.VMEM((2, size, size), jnp.float32)],
    )(packed, fields)


def body(bands, directions, materials, permittivity, wavevector):
    band_count = bands.shape[1]
    height = bands.shape[2]
    breadth = bands.shape[3]
    levels = jnp.arange(permittivity.shape[0], dtype=jnp.int32)

    def stiffness_of(cells):
        return jnp.sum(
            jnp.where(
                cells[None] == levels.astype(jnp.float32)[:, None, None],
                (1.0 / permittivity)[:, None, None],
                0.0,
            ),
            axis=0,
        )

    def strip_of(start, stop):
        field_rows = jnp.concatenate(
            [bands[:, :, start:stop], directions[:, :, start:stop]], axis=1
        ).reshape(4 * band_count, stop - start, breadth)
        return jnp.concatenate([field_rows, material_grid[None, start:stop]], axis=0)

    material_grid = materials.astype(jnp.float32)
    angle_row = 2.0 * math.pi * wavevector[0].astype(jnp.float32) / KDEN
    angle_col = 2.0 * math.pi * wavevector[1].astype(jnp.float32) / KDEN
    fields = jnp.concatenate([bands, directions], axis=1)
    packed = jnp.concatenate(
        [fields.reshape(4 * band_count, height, breadth), material_grid[None]], axis=0
    )
    padded = exchange_rim(
        packed, "row", 1, 2, (strip_of(0, 2), strip_of(height - 2, height)), angle_row
    )
    padded = exchange_rim(padded, "col", 2, 2, angle=angle_col)
    stiff_wide = stiffness_of(padded[-1])
    field_wide = padded[:-1].reshape(2, 2 * band_count, height + 4, breadth + 4)
    band_wide = field_wide[:, :band_count]
    applied_ring, diagonal_ring = stencil(band_wide, stiff_wide)
    stiff_ring = stiff_wide[1:-1, 1:-1]
    scaled_ring = jnp.concatenate(
        [
            applied_ring / diagonal_ring,
            band_wide[:, :, 1:-1, 1:-1] / diagonal_ring,
            field_wide[:, band_count:, 1:-1, 1:-1],
        ],
        axis=1,
    )
    extra_applied = stencil(scaled_ring, stiff_ring)[0]
    applied_cycle = applied_ring[:, :, 1:-1, 1:-1]
    scaled_image = scaled_ring[:, :band_count, 1:-1, 1:-1]
    scaled_bands = scaled_ring[:, band_count : 2 * band_count, 1:-1, 1:-1]
    extended = jnp.concatenate([bands, scaled_image, scaled_bands, directions], axis=1)
    extended_applied = jnp.concatenate([applied_cycle, extra_applied], axis=1)
    local_gram = complex_gram(extended, extended)
    local_ham = complex_gram(extended, extended_applied)
    summed = jnp.stack([pack_hermitian(*local_gram), pack_hermitian(*local_ham)])
    summed = tree_sum(tree_sum(summed.reshape(-1), "col"), "row").reshape(summed.shape)
    raw_count = 3 * band_count
    ext_count = 4 * band_count
    scale_factor = math.sqrt(height * breadth * lax.axis_size("row") * lax.axis_size("col"))
    basis, red = matrix_stage(
        summed, extended.reshape(2 * ext_count, height, breadth), band_count, scale_factor
    )
    reduced = jnp.transpose(red, (1, 0, 2))
    basis = basis.reshape(2, raw_count, height, breadth)
    return (basis, reduced)


def solution(mesh):
    placed = (P(None, None, "row", "col"), P(None, None, "row", "col"), P("row", "col"), P(), P())
    return jax.shard_map(
        body,
        mesh=mesh,
        in_specs=placed,
        out_specs=(P(None, None, "row", "col"), P()),
        check_vma=False,
    )
```

```python
import functools
import math

import jax
import jax.numpy as jnp
from jax import lax
from jax.experimental import pallas as pl
from jax.experimental.pallas import tpu as pltpu
from jax.sharding import PartitionSpec as P

KDEN = 16
NS_STEPS = 5


def rotate(values, phase_angle):
    cosine = jnp.cos(phase_angle)
    sine_part = jnp.sin(phase_angle)
    return jnp.stack(
        [values[0] * cosine - values[1] * sine_part, values[0] * sine_part + values[1] * cosine]
    )


def stencil(padded, stiff_pad):
    centre = stiff_pad[1:-1, 1:-1]
    upward = 0.5 * (centre + stiff_pad[:-2, 1:-1])
    downward = 0.5 * (centre + stiff_pad[2:, 1:-1])
    leftward = 0.5 * (centre + stiff_pad[1:-1, :-2])
    rightward = 0.5 * (centre + stiff_pad[1:-1, 2:])
    diagonal = upward + downward + leftward + rightward
    inner_cells = padded[:, :, 1:-1, 1:-1]
    neighbours = (
        upward * padded[:, :, :-2, 1:-1]
        + downward * padded[:, :, 2:, 1:-1]
        + leftward * padded[:, :, 1:-1, :-2]
        + rightward * padded[:, :, 1:-1, 2:]
    )
    return (diagonal * inner_cells - neighbours, diagonal)


def complex_gram(first_block, second_block):
    count = first_block.shape[1]
    first_flat = first_block.reshape((2 * count,) + first_block.shape[2:])
    second_flat = second_block.reshape((2 * count,) + second_block.shape[2:])
    products = jnp.einsum(
        "jrc,krc->jk", first_flat, second_flat, precision=lax.Precision.HIGHEST
    )
    real_part = products[:count, :count] + products[count:, count:]
    imag_part = products[:count, count:] - products[count:, :count]
    return (real_part, imag_part)


def inverse_root(gram_real, gram_imag):
    highest = lax.Precision.HIGHEST
    order_size = gram_real.shape[0]
    upper_half = jnp.concatenate([gram_real, -gram_imag], axis=1)
    lower_half = jnp.concatenate([gram_imag, gram_real], axis=1)
    embedded = jnp.concatenate([upper_half, lower_half], axis=0)
    magnitude = jnp.sqrt(jnp.sum(embedded * embedded))
    identity = jnp.eye(2 * order_size, dtype=embedded.dtype)

    def newton(turn_index, carried):
        current, inverse = carried
        factor = 1.5 * identity - 0.5 * jnp.dot(inverse, current, precision=highest)
        return (
            jnp.dot(current, factor, precision=highest),
            jnp.dot(factor, inverse, precision=highest),
        )

    current, inverse = lax.fori_loop(0, NS_STEPS, newton, (embedded / magnitude, identity))
    root_full = inverse / jnp.sqrt(magnitude)
    return (root_full[:order_size, :order_size], root_full[order_size:, :order_size])


def reduce_matrix(root_real, root_imag, ham_real, ham_imag):
    highest = lax.Precision.HIGHEST
    prod_real = jnp.dot(ham_real, root_real, precision=highest) - jnp.dot(
        ham_imag, root_imag, precision=highest
    )
    prod_imag = jnp.dot(ham_real, root_imag, precision=highest) + jnp.dot(
        ham_imag, root_real, precision=highest
    )
    red_real = jnp.dot(root_real.T, prod_real, precision=highest) + jnp.dot(
        root_imag.T, prod_imag, precision=highest
    )
    red_imag = jnp.dot(root_real.T, prod_imag, precision=highest) - jnp.dot(
        root_imag.T, prod_real, precision=highest
    )
    return jnp.stack([red_real, red_imag])


def rotate_basis(raw_basis, root_real, root_imag, scale_factor):
    highest = lax.Precision.HIGHEST
    basis_real = jnp.einsum("jrc,jk->krc", raw_basis[0], root_real, precision=highest) - jnp.einsum(
        "jrc,jk->krc", raw_basis[1], root_imag, precision=highest
    )
    basis_imag = jnp.einsum("jrc,jk->krc", raw_basis[0], root_imag, precision=highest) + jnp.einsum(
        "jrc,jk->krc", raw_basis[1], root_real, precision=highest
    )
    return scale_factor * jnp.stack([basis_real, basis_imag])


def project_mixing(mixing, matrix):
    highest = lax.Precision.HIGHEST
    return jnp.dot(mixing.T, jnp.dot(matrix, mixing, precision=highest), precision=highest)


def exchange_rim(cells, axis, dim, width, strips=None, angle=None):
    count = lax.axis_size(axis)
    if strips is None:
        head = lax.slice_in_dim(cells, 0, width, axis=dim)
        tail = lax.slice_in_dim(cells, cells.shape[dim] - width, cells.shape[dim], axis=dim)
    else:
        head, tail = strips
    if count % 2:
        before = lax.ppermute(tail.reshape(-1), axis, [(i, (i + 1) % count) for i in range(count)])
        after = lax.ppermute(head.reshape(-1), axis, [((i + 1) % count, i) for i in range(count)])
    else:
        even = lax.axis_index(axis) % 2 == 0
        first = lax.ppermute(
            jnp.where(even, tail, head).reshape(-1), axis, [(i, i ^ 1) for i in range(count)]
        )
        second = lax.ppermute(
            jnp.where(even, head, tail).reshape(-1),
            axis,
            [(i, (i + 1) % count if i % 2 else (i - 1) % count) for i in range(count)],
        )
        before = jnp.where(even, second, first)
        after = jnp.where(even, first, second)
    if angle is not None:
        index = lax.axis_index(axis)
        before = turn_flat(before, jnp.where(index == 0, -angle, 0.0), cells.shape[0])
        after = turn_flat(after, jnp.where(index == count - 1, angle, 0.0), cells.shape[0])
    before = before.reshape(tail.shape)
    after = after.reshape(head.shape)
    return jnp.concatenate([before, cells, after], axis=dim)


def turn_flat(flat, phase_angle, channels):
    share = flat.shape[0] // channels
    half = (channels - 1) // 2 * share
    turned = rotate(jnp.stack([flat[:half], flat[half : 2 * half]]), phase_angle)
    return jnp.concatenate([turned[0], turned[1], flat[2 * half :]])


def tree_sum(value, axis):
    count = lax.axis_size(axis)
    if count & (count - 1):
        return lax.psum(value, axis)
    step = 1
    while step < count:
        value = value + lax.ppermute(value, axis, [(i, i ^ step) for i in range(count)])
        step *= 2
    return value


def pack_hermitian(real_part, imag_part):
    order_size = real_part.shape[0]
    upper = jnp.arange(order_size)[:, None] <= jnp.arange(order_size)[None, :]
    return jnp.where(upper, real_part, imag_part)


def unpack_hermitian(packed):
    order_size = packed.shape[0]
    upper = jnp.arange(order_size)[:, None] <= jnp.arange(order_size)[None, :]
    strict_upper = jnp.arange(order_size)[:, None] < jnp.arange(order_size)[None, :]
    real_upper = jnp.where(upper, packed, 0.0)
    real_part = real_upper + jnp.where(strict_upper, packed, 0.0).T
    imag_lower = jnp.where(upper, 0.0, packed)
    return (real_part, imag_lower - imag_lower.T)


def matrix_kernel(packed_ref, field_ref, basis_ref, red_ref, work_ref, *, band_count, scale):
    highest = lax.Precision.HIGHEST

    def dot(first, second):
        return jnp.dot(first, second, precision=highest, preferred_element_type=jnp.float32)

    size = work_ref.shape[-1]
    ext = packed_ref.shape[-1]
    raw = 3 * band_count
    half = size // 2
    work_ref[...] = jnp.zeros(work_ref.shape, jnp.float32)
    work_ref[0, :ext, :ext] = packed_ref[0]
    work_ref[1, :ext, :ext] = packed_ref[1]
    rows = lax.broadcasted_iota(jnp.int32, (size, size), 0)
    cols = lax.broadcasted_iota(jnp.int32, (size, size), 1)
    upper = rows <= cols
    strict = rows < cols
    eye = rows == cols
    corner = (rows < half) & (cols < half)

    def spread(value, axis):
        return pltpu.roll(value, half, axis)

    def embed(real_part, imag_part):
        return real_part + spread(spread(real_part, 0), 1) - spread(imag_part, 1) + spread(imag_part, 0)

    def unpack(packed):
        real_part = jnp.where(upper, packed, 0.0) + jnp.where(strict, packed, 0.0).T
        lower = jnp.where(upper, 0.0, packed)
        return real_part, lower - lower.T

    gram_re, gram_im = unpack(work_ref[0])
    ham_re, ham_im = unpack(work_ref[1])
    band_diag = eye & (rows < band_count)
    quotient = jnp.where(band_diag, ham_re, 0.0) / jnp.where(band_diag, gram_re, 1.0)
    shifted = pltpu.roll(pltpu.roll(quotient, 2 * band_count, 0), band_count, 1)
    kept = (eye & (cols < 2 * band_count)) | (
        (rows == cols + band_count) & (cols >= 2 * band_count) & (cols < raw)
    )
    mixing = kept.astype(jnp.float32) - shifted
    mixing = mixing + spread(spread(mixing, 0), 1)
    embedded = dot(mixing.T, dot(embed(gram_re, gram_im), mixing))
    active = (rows < raw) | ((rows >= half) & (rows < half + raw))
    identity = (eye & active).astype(jnp.float32)
    total = jnp.sum(jnp.sum(embedded * embedded, axis=0, keepdims=True), axis=1, keepdims=True)
    magnitude = jnp.sqrt(total)
    current = embedded / magnitude
    inverse = identity
    for _ in range(NS_STEPS):
        factor = 1.5 * identity - 0.5 * dot(inverse, current)
        current, inverse = dot(current, factor), dot(factor, inverse)
    root = inverse / jnp.sqrt(magnitude)
    root = embed(jnp.where(corner, root, 0.0), jnp.where(corner, spread(root, 0), 0.0))
    rotation = dot(mixing, root)
    work_ref[1] = dot(rotation.T, dot(embed(ham_re, ham_im), rotation))
    red_ref[:, 0, :] = work_ref[1, :raw, :raw]
    red_ref[:, 1, :] = work_ref[1, half : half + raw, :raw]
    rotation = jnp.where(corner | ~((rows < half) | (cols < half)), rotation, -rotation)
    packed_rotation = jnp.where(
        cols < raw,
        rotation,
        jnp.where(cols < 2 * raw, pltpu.roll(rotation, size - half + raw, 1), 0.0),
    )
    packed_rotation = jnp.where(
        rows < ext,
        packed_rotation,
        jnp.where(rows < 2 * ext, pltpu.roll(packed_rotation, size - half + ext, 0), 0.0),
    )
    work_ref[0] = scale * packed_rotation.T
    rotation_t = work_ref[0, : 2 * raw, : 2 * ext]
    for row in range(field_ref.shape[1]):
        basis_ref[:, row, :] = dot(rotation_t, field_ref[:, row, :])


def matrix_stage(packed, fields, band_count, scale):
    size = 128
    raw = 3 * band_count
    vmem = pl.BlockSpec(memory_space=pltpu.VMEM)
    return pl.pallas_call(
        functools.partial(matrix_kernel, band_count=band_count, scale=scale),
        out_shape=(
            jax.ShapeDtypeStruct((2 * raw,) + fields.shape[1:], jnp.float32),
            jax.ShapeDtypeStruct((raw, 2, raw), jnp.float32),
        ),
        in_specs=[vmem, vmem],
        out_specs=(vmem, vmem),
        scratch_shapes=[pltpu.VMEM((2, size, size), jnp.float32)],
    )(packed, fields)


def body(bands, directions, materials, permittivity, wavevector):
    band_count = bands.shape[1]
    height = bands.shape[2]
    breadth = bands.shape[3]
    levels = jnp.arange(permittivity.shape[0], dtype=jnp.int32)

    def stiffness_of(cells):
        return jnp.sum(
            jnp.where(
                cells[None] == levels.astype(jnp.float32)[:, None, None],
                (1.0 / permittivity)[:, None, None],
                0.0,
            ),
            axis=0,
        )

    def strip_of(start, stop):
        field_rows = jnp.concatenate(
            [bands[:, :, start:stop], directions[:, :, start:stop]], axis=1
        ).reshape(4 * band_count, stop - start, breadth)
        return jnp.concatenate([field_rows, material_grid[None, start:stop]], axis=0)

    material_grid = materials.astype(jnp.float32)
    angle_row = 2.0 * math.pi * wavevector[0].astype(jnp.float32) / KDEN
    angle_col = 2.0 * math.pi * wavevector[1].astype(jnp.float32) / KDEN
    fields = jnp.concatenate([bands, directions], axis=1)
    packed = jnp.concatenate(
        [fields.reshape(4 * band_count, height, breadth), material_grid[None]], axis=0
    )
    padded = exchange_rim(
        packed, "row", 1, 2, (strip_of(0, 2), strip_of(height - 2, height)), angle_row
    )
    padded = exchange_rim(padded, "col", 2, 2, angle=angle_col)
    stiff_wide = stiffness_of(padded[-1])
    field_wide = padded[:-1].reshape(2, 2 * band_count, height + 4, breadth + 4)
    band_wide = field_wide[:, :band_count]
    applied_ring, diagonal_ring = stencil(band_wide, stiff_wide)
    stiff_ring = stiff_wide[1:-1, 1:-1]
    scaled_ring = jnp.concatenate(
        [
            applied_ring / diagonal_ring,
            band_wide[:, :, 1:-1, 1:-1] / diagonal_ring,
            field_wide[:, band_count:, 1:-1, 1:-1],
        ],
        axis=1,
    )
    extra_applied = stencil(scaled_ring, stiff_ring)[0]
    applied_cycle = applied_ring[:, :, 1:-1, 1:-1]
    scaled_image = scaled_ring[:, :band_count, 1:-1, 1:-1]
    scaled_bands = scaled_ring[:, band_count : 2 * band_count, 1:-1, 1:-1]
    extended = jnp.concatenate([bands, scaled_image, scaled_bands, directions], axis=1)
    extended_applied = jnp.concatenate([applied_cycle, extra_applied], axis=1)
    local_gram = complex_gram(extended, extended)
    local_ham = complex_gram(extended, extended_applied)
    summed = jnp.stack([pack_hermitian(*local_gram), pack_hermitian(*local_ham)])
    summed = tree_sum(tree_sum(summed.reshape(-1), "row"), "col").reshape(summed.shape)
    raw_count = 3 * band_count
    ext_count = 4 * band_count
    scale_factor = math.sqrt(height * breadth * lax.axis_size("row") * lax.axis_size("col"))
    basis, red = matrix_stage(
        summed, extended.reshape(2 * ext_count, height, breadth), band_count, scale_factor
    )
    reduced = jnp.transpose(red, (1, 0, 2))
    basis = basis.reshape(2, raw_count, height, breadth)
    return (basis, reduced)


def solution(mesh):
    placed = (P(None, None, "row", "col"), P(None, None, "row", "col"), P("row", "col"), P(), P())
    return jax.shard_map(
        body,
        mesh=mesh,
        in_specs=placed,
        out_specs=(P(None, None, "row", "col"), P()),
        check_vma=False,
    )
```

```python
import functools
import math

import jax
import jax.numpy as jnp
from jax import lax
from jax.experimental import pallas as pl
from jax.experimental.pallas import tpu as pltpu
from jax.sharding import PartitionSpec as P

KDEN = 16
NS_STEPS = 5


def rotate(values, phase_angle):
    cosine = jnp.cos(phase_angle)
    sine_part = jnp.sin(phase_angle)
    return jnp.stack(
        [values[0] * cosine - values[1] * sine_part, values[0] * sine_part + values[1] * cosine]
    )


def stencil(padded, stiff_pad):
    centre = stiff_pad[1:-1, 1:-1]
    upward = 0.5 * (centre + stiff_pad[:-2, 1:-1])
    downward = 0.5 * (centre + stiff_pad[2:, 1:-1])
    leftward = 0.5 * (centre + stiff_pad[1:-1, :-2])
    rightward = 0.5 * (centre + stiff_pad[1:-1, 2:])
    diagonal = upward + downward + leftward + rightward
    inner_cells = padded[:, :, 1:-1, 1:-1]
    neighbours = (
        upward * padded[:, :, :-2, 1:-1]
        + downward * padded[:, :, 2:, 1:-1]
        + leftward * padded[:, :, 1:-1, :-2]
        + rightward * padded[:, :, 1:-1, 2:]
    )
    return (diagonal * inner_cells - neighbours, diagonal)


def complex_gram(first_block, second_block):
    count = first_block.shape[1]
    first_flat = first_block.reshape((2 * count,) + first_block.shape[2:])
    second_flat = second_block.reshape((2 * count,) + second_block.shape[2:])
    products = jnp.einsum(
        "jrc,krc->jk", first_flat, second_flat, precision=lax.Precision.HIGHEST
    )
    real_part = products[:count, :count] + products[count:, count:]
    imag_part = products[:count, count:] - products[count:, :count]
    return (real_part, imag_part)


def inverse_root(gram_real, gram_imag):
    highest = lax.Precision.HIGHEST
    order_size = gram_real.shape[0]
    upper_half = jnp.concatenate([gram_real, -gram_imag], axis=1)
    lower_half = jnp.concatenate([gram_imag, gram_real], axis=1)
    embedded = jnp.concatenate([upper_half, lower_half], axis=0)
    magnitude = jnp.sqrt(jnp.sum(embedded * embedded))
    identity = jnp.eye(2 * order_size, dtype=embedded.dtype)

    def newton(turn_index, carried):
        current, inverse = carried
        factor = 1.5 * identity - 0.5 * jnp.dot(inverse, current, precision=highest)
        return (
            jnp.dot(current, factor, precision=highest),
            jnp.dot(factor, inverse, precision=highest),
        )

    current, inverse = lax.fori_loop(0, NS_STEPS, newton, (embedded / magnitude, identity))
    root_full = inverse / jnp.sqrt(magnitude)
    return (root_full[:order_size, :order_size], root_full[order_size:, :order_size])


def reduce_matrix(root_real, root_imag, ham_real, ham_imag):
    highest = lax.Precision.HIGHEST
    prod_real = jnp.dot(ham_real, root_real, precision=highest) - jnp.dot(
        ham_imag, root_imag, precision=highest
    )
    prod_imag = jnp.dot(ham_real, root_imag, precision=highest) + jnp.dot(
        ham_imag, root_real, precision=highest
    )
    red_real = jnp.dot(root_real.T, prod_real, precision=highest) + jnp.dot(
        root_imag.T, prod_imag, precision=highest
    )
    red_imag = jnp.dot(root_real.T, prod_imag, precision=highest) - jnp.dot(
        root_imag.T, prod_real, precision=highest
    )
    return jnp.stack([red_real, red_imag])


def rotate_basis(raw_basis, root_real, root_imag, scale_factor):
    highest = lax.Precision.HIGHEST
    basis_real = jnp.einsum("jrc,jk->krc", raw_basis[0], root_real, precision=highest) - jnp.einsum(
        "jrc,jk->krc", raw_basis[1], root_imag, precision=highest
    )
    basis_imag = jnp.einsum("jrc,jk->krc", raw_basis[0], root_imag, precision=highest) + jnp.einsum(
        "jrc,jk->krc", raw_basis[1], root_real, precision=highest
    )
    return scale_factor * jnp.stack([basis_real, basis_imag])


def project_mixing(mixing, matrix):
    highest = lax.Precision.HIGHEST
    return jnp.dot(mixing.T, jnp.dot(matrix, mixing, precision=highest), precision=highest)


def exchange_rim(cells, axis, dim, width, strips=None, angle=None):
    count = lax.axis_size(axis)
    if strips is None:
        head = lax.slice_in_dim(cells, 0, width, axis=dim)
        tail = lax.slice_in_dim(cells, cells.shape[dim] - width, cells.shape[dim], axis=dim)
    else:
        head, tail = strips
    if count % 2:
        before = lax.ppermute(tail.reshape(-1), axis, [(i, (i + 1) % count) for i in range(count)])
        after = lax.ppermute(head.reshape(-1), axis, [((i + 1) % count, i) for i in range(count)])
    else:
        even = lax.axis_index(axis) % 2 == 0
        first = lax.ppermute(
            jnp.where(even, tail, head).reshape(-1), axis, [(i, i ^ 1) for i in range(count)]
        )
        second = lax.ppermute(
            jnp.where(even, head, tail).reshape(-1),
            axis,
            [(i, (i + 1) % count if i % 2 else (i - 1) % count) for i in range(count)],
        )
        before = jnp.where(even, second, first)
        after = jnp.where(even, first, second)
    if angle is not None:
        index = lax.axis_index(axis)
        before = turn_flat(before, jnp.where(index == 0, -angle, 0.0), cells.shape[0])
        after = turn_flat(after, jnp.where(index == count - 1, angle, 0.0), cells.shape[0])
    before = before.reshape(tail.shape)
    after = after.reshape(head.shape)
    return jnp.concatenate([before, cells, after], axis=dim)


def turn_flat(flat, phase_angle, channels):
    share = flat.shape[0] // channels
    half = (channels - 1) // 2 * share
    turned = rotate(jnp.stack([flat[:half], flat[half : 2 * half]]), phase_angle)
    return jnp.concatenate([turned[0], turned[1], flat[2 * half :]])


def tree_sum(value, axis):
    count = lax.axis_size(axis)
    if count & (count - 1):
        return lax.psum(value, axis)
    step = 1
    while step < count:
        value = value + lax.ppermute(value, axis, [(i, i ^ step) for i in range(count)])
        step *= 2
    return value


def pack_hermitian(real_part, imag_part):
    order_size = real_part.shape[0]
    upper = jnp.arange(order_size)[:, None] <= jnp.arange(order_size)[None, :]
    return jnp.where(upper, real_part, imag_part)


def unpack_hermitian(packed):
    order_size = packed.shape[0]
    upper = jnp.arange(order_size)[:, None] <= jnp.arange(order_size)[None, :]
    strict_upper = jnp.arange(order_size)[:, None] < jnp.arange(order_size)[None, :]
    real_upper = jnp.where(upper, packed, 0.0)
    real_part = real_upper + jnp.where(strict_upper, packed, 0.0).T
    imag_lower = jnp.where(upper, 0.0, packed)
    return (real_part, imag_lower - imag_lower.T)


def matrix_kernel(packed_ref, field_ref, basis_ref, red_ref, work_ref, *, band_count, scale):
    highest = lax.Precision.HIGHEST

    def dot(first, second):
        return jnp.dot(first, second, precision=highest, preferred_element_type=jnp.float32)

    size = work_ref.shape[-1]
    ext = packed_ref.shape[-1]
    raw = 3 * band_count
    half = size // 2
    work_ref[...] = jnp.zeros(work_ref.shape, jnp.float32)
    work_ref[0, :ext, :ext] = packed_ref[0]
    work_ref[1, :ext, :ext] = packed_ref[1]
    rows = lax.broadcasted_iota(jnp.int32, (size, size), 0)
    cols = lax.broadcasted_iota(jnp.int32, (size, size), 1)
    upper = rows <= cols
    strict = rows < cols
    eye = rows == cols
    corner = (rows < half) & (cols < half)

    def spread(value, axis):
        return pltpu.roll(value, half, axis)

    def embed(real_part, imag_part):
        return real_part + spread(spread(real_part, 0), 1) - spread(imag_part, 1) + spread(imag_part, 0)

    def unpack(packed):
        real_part = jnp.where(upper, packed, 0.0) + jnp.where(strict, packed, 0.0).T
        lower = jnp.where(upper, 0.0, packed)
        return real_part, lower - lower.T

    gram_re, gram_im = unpack(work_ref[0])
    ham_re, ham_im = unpack(work_ref[1])
    band_diag = eye & (rows < band_count)
    quotient = jnp.where(band_diag, ham_re, 0.0) / jnp.where(band_diag, gram_re, 1.0)
    shifted = pltpu.roll(pltpu.roll(quotient, 2 * band_count, 0), band_count, 1)
    kept = (eye & (cols < 2 * band_count)) | (
        (rows == cols + band_count) & (cols >= 2 * band_count) & (cols < raw)
    )
    mixing = kept.astype(jnp.float32) - shifted
    mixing = mixing + spread(spread(mixing, 0), 1)
    embedded = dot(mixing.T, dot(embed(gram_re, gram_im), mixing))
    active = (rows < raw) | ((rows >= half) & (rows < half + raw))
    identity = (eye & active).astype(jnp.float32)
    total = jnp.sum(jnp.sum(embedded * embedded, axis=0, keepdims=True), axis=1, keepdims=True)
    magnitude = jnp.sqrt(total)
    current = embedded / magnitude
    inverse = identity
    for step in range(NS_STEPS):
        if step == 0:
            factor = 1.5 * identity - 0.5 * current
            current, inverse = dot(current, factor), factor
        else:
            factor = 1.5 * identity - 0.5 * dot(inverse, current)
            current, inverse = dot(current, factor), dot(factor, inverse)
    root = inverse / jnp.sqrt(magnitude)
    root = embed(jnp.where(corner, root, 0.0), jnp.where(corner, spread(root, 0), 0.0))
    rotation = dot(mixing, root)
    work_ref[1] = dot(rotation.T, dot(embed(ham_re, ham_im), rotation))
    red_ref[:, 0, :] = work_ref[1, :raw, :raw]
    red_ref[:, 1, :] = work_ref[1, half : half + raw, :raw]
    rotation = jnp.where(corner | ~((rows < half) | (cols < half)), rotation, -rotation)
    packed_rotation = jnp.where(
        cols < raw,
        rotation,
        jnp.where(cols < 2 * raw, pltpu.roll(rotation, size - half + raw, 1), 0.0),
    )
    packed_rotation = jnp.where(
        rows < ext,
        packed_rotation,
        jnp.where(rows < 2 * ext, pltpu.roll(packed_rotation, size - half + ext, 0), 0.0),
    )
    work_ref[0] = scale * packed_rotation.T
    rotation_t = work_ref[0, : 2 * raw, : 2 * ext]
    for row in range(field_ref.shape[1]):
        basis_ref[:, row, :] = dot(rotation_t, field_ref[:, row, :])


def matrix_stage(packed, fields, band_count, scale):
    size = 128
    raw = 3 * band_count
    vmem = pl.BlockSpec(memory_space=pltpu.VMEM)
    return pl.pallas_call(
        functools.partial(matrix_kernel, band_count=band_count, scale=scale),
        out_shape=(
            jax.ShapeDtypeStruct((2 * raw,) + fields.shape[1:], jnp.float32),
            jax.ShapeDtypeStruct((raw, 2, raw), jnp.float32),
        ),
        in_specs=[vmem, vmem],
        out_specs=(vmem, vmem),
        scratch_shapes=[pltpu.VMEM((2, size, size), jnp.float32)],
    )(packed, fields)


def body(bands, directions, materials, permittivity, wavevector):
    band_count = bands.shape[1]
    height = bands.shape[2]
    breadth = bands.shape[3]
    levels = jnp.arange(permittivity.shape[0], dtype=jnp.int32)

    def stiffness_of(cells):
        return jnp.sum(
            jnp.where(
                cells[None] == levels.astype(jnp.float32)[:, None, None],
                (1.0 / permittivity)[:, None, None],
                0.0,
            ),
            axis=0,
        )

    def strip_of(start, stop):
        field_rows = jnp.concatenate(
            [bands[:, :, start:stop], directions[:, :, start:stop]], axis=1
        ).reshape(4 * band_count, stop - start, breadth)
        return jnp.concatenate([field_rows, material_grid[None, start:stop]], axis=0)

    material_grid = materials.astype(jnp.float32)
    angle_row = 2.0 * math.pi * wavevector[0].astype(jnp.float32) / KDEN
    angle_col = 2.0 * math.pi * wavevector[1].astype(jnp.float32) / KDEN
    fields = jnp.concatenate([bands, directions], axis=1)
    packed = jnp.concatenate(
        [fields.reshape(4 * band_count, height, breadth), material_grid[None]], axis=0
    )
    padded = exchange_rim(
        packed, "row", 1, 2, (strip_of(0, 2), strip_of(height - 2, height)), angle_row
    )
    padded = exchange_rim(padded, "col", 2, 2, angle=angle_col)
    stiff_wide = stiffness_of(padded[-1])
    field_wide = padded[:-1].reshape(2, 2 * band_count, height + 4, breadth + 4)
    band_wide = field_wide[:, :band_count]
    applied_ring, diagonal_ring = stencil(band_wide, stiff_wide)
    stiff_ring = stiff_wide[1:-1, 1:-1]
    scaled_ring = jnp.concatenate(
        [
            applied_ring / diagonal_ring,
            band_wide[:, :, 1:-1, 1:-1] / diagonal_ring,
            field_wide[:, band_count:, 1:-1, 1:-1],
        ],
        axis=1,
    )
    extra_applied = stencil(scaled_ring, stiff_ring)[0]
    applied_cycle = applied_ring[:, :, 1:-1, 1:-1]
    scaled_image = scaled_ring[:, :band_count, 1:-1, 1:-1]
    scaled_bands = scaled_ring[:, band_count : 2 * band_count, 1:-1, 1:-1]
    extended = jnp.concatenate([bands, scaled_image, scaled_bands, directions], axis=1)
    extended_applied = jnp.concatenate([applied_cycle, extra_applied], axis=1)
    local_gram = complex_gram(extended, extended)
    local_ham = complex_gram(extended, extended_applied)
    summed = jnp.stack([pack_hermitian(*local_gram), pack_hermitian(*local_ham)])
    summed = tree_sum(tree_sum(summed.reshape(-1), "row"), "col").reshape(summed.shape)
    raw_count = 3 * band_count
    ext_count = 4 * band_count
    scale_factor = math.sqrt(height * breadth * lax.axis_size("row") * lax.axis_size("col"))
    basis, red = matrix_stage(
        summed, extended.reshape(2 * ext_count, height, breadth), band_count, scale_factor
    )
    reduced = jnp.transpose(red, (1, 0, 2))
    basis = basis.reshape(2, raw_count, height, breadth)
    return (basis, reduced)


def solution(mesh):
    placed = (P(None, None, "row", "col"), P(None, None, "row", "col"), P("row", "col"), P(), P())
    return jax.shard_map(
        body,
        mesh=mesh,
        in_specs=placed,
        out_specs=(P(None, None, "row", "col"), P()),
        check_vma=False,
    )
```

```python
import functools
import math

import jax
import jax.numpy as jnp
from jax import lax
from jax.experimental import pallas as pl
from jax.experimental.pallas import tpu as pltpu
from jax.sharding import PartitionSpec as P

KDEN = 16
NS_STEPS = 5


def rotate(values, phase_angle):
    cosine = jnp.cos(phase_angle)
    sine_part = jnp.sin(phase_angle)
    return jnp.stack(
        [values[0] * cosine - values[1] * sine_part, values[0] * sine_part + values[1] * cosine]
    )


def stencil(padded, stiff_pad):
    centre = stiff_pad[1:-1, 1:-1]
    upward = 0.5 * (centre + stiff_pad[:-2, 1:-1])
    downward = 0.5 * (centre + stiff_pad[2:, 1:-1])
    leftward = 0.5 * (centre + stiff_pad[1:-1, :-2])
    rightward = 0.5 * (centre + stiff_pad[1:-1, 2:])
    diagonal = upward + downward + leftward + rightward
    inner_cells = padded[:, :, 1:-1, 1:-1]
    neighbours = (
        upward * padded[:, :, :-2, 1:-1]
        + downward * padded[:, :, 2:, 1:-1]
        + leftward * padded[:, :, 1:-1, :-2]
        + rightward * padded[:, :, 1:-1, 2:]
    )
    return (diagonal * inner_cells - neighbours, diagonal)


def complex_gram(first_block, second_block):
    count = first_block.shape[1]
    first_flat = first_block.reshape((2 * count,) + first_block.shape[2:])
    second_flat = second_block.reshape((2 * count,) + second_block.shape[2:])
    products = jnp.einsum(
        "jrc,krc->jk", first_flat, second_flat, precision=lax.Precision.HIGHEST
    )
    real_part = products[:count, :count] + products[count:, count:]
    imag_part = products[:count, count:] - products[count:, :count]
    return (real_part, imag_part)


def inverse_root(gram_real, gram_imag):
    highest = lax.Precision.HIGHEST
    order_size = gram_real.shape[0]
    upper_half = jnp.concatenate([gram_real, -gram_imag], axis=1)
    lower_half = jnp.concatenate([gram_imag, gram_real], axis=1)
    embedded = jnp.concatenate([upper_half, lower_half], axis=0)
    magnitude = jnp.sqrt(jnp.sum(embedded * embedded))
    identity = jnp.eye(2 * order_size, dtype=embedded.dtype)

    def newton(turn_index, carried):
        current, inverse = carried
        factor = 1.5 * identity - 0.5 * jnp.dot(inverse, current, precision=highest)
        return (
            jnp.dot(current, factor, precision=highest),
            jnp.dot(factor, inverse, precision=highest),
        )

    current, inverse = lax.fori_loop(0, NS_STEPS, newton, (embedded / magnitude, identity))
    root_full = inverse / jnp.sqrt(magnitude)
    return (root_full[:order_size, :order_size], root_full[order_size:, :order_size])


def reduce_matrix(root_real, root_imag, ham_real, ham_imag):
    highest = lax.Precision.HIGHEST
    prod_real = jnp.dot(ham_real, root_real, precision=highest) - jnp.dot(
        ham_imag, root_imag, precision=highest
    )
    prod_imag = jnp.dot(ham_real, root_imag, precision=highest) + jnp.dot(
        ham_imag, root_real, precision=highest
    )
    red_real = jnp.dot(root_real.T, prod_real, precision=highest) + jnp.dot(
        root_imag.T, prod_imag, precision=highest
    )
    red_imag = jnp.dot(root_real.T, prod_imag, precision=highest) - jnp.dot(
        root_imag.T, prod_real, precision=highest
    )
    return jnp.stack([red_real, red_imag])


def rotate_basis(raw_basis, root_real, root_imag, scale_factor):
    highest = lax.Precision.HIGHEST
    basis_real = jnp.einsum("jrc,jk->krc", raw_basis[0], root_real, precision=highest) - jnp.einsum(
        "jrc,jk->krc", raw_basis[1], root_imag, precision=highest
    )
    basis_imag = jnp.einsum("jrc,jk->krc", raw_basis[0], root_imag, precision=highest) + jnp.einsum(
        "jrc,jk->krc", raw_basis[1], root_real, precision=highest
    )
    return scale_factor * jnp.stack([basis_real, basis_imag])


def project_mixing(mixing, matrix):
    highest = lax.Precision.HIGHEST
    return jnp.dot(mixing.T, jnp.dot(matrix, mixing, precision=highest), precision=highest)


def exchange_rim(cells, axis, dim, width, strips=None, angle=None):
    count = lax.axis_size(axis)
    if strips is None:
        head = lax.slice_in_dim(cells, 0, width, axis=dim)
        tail = lax.slice_in_dim(cells, cells.shape[dim] - width, cells.shape[dim], axis=dim)
    else:
        head, tail = strips
    if count % 2:
        before = lax.ppermute(tail.reshape(-1), axis, [(i, (i + 1) % count) for i in range(count)])
        after = lax.ppermute(head.reshape(-1), axis, [((i + 1) % count, i) for i in range(count)])
    else:
        even = lax.axis_index(axis) % 2 == 0
        first = lax.ppermute(
            jnp.where(even, tail, head).reshape(-1), axis, [(i, i ^ 1) for i in range(count)]
        )
        second = lax.ppermute(
            jnp.where(even, head, tail).reshape(-1),
            axis,
            [(i, (i + 1) % count if i % 2 else (i - 1) % count) for i in range(count)],
        )
        before = jnp.where(even, second, first)
        after = jnp.where(even, first, second)
    if angle is not None:
        index = lax.axis_index(axis)
        before = turn_flat(before, jnp.where(index == 0, -angle, 0.0), cells.shape[0])
        after = turn_flat(after, jnp.where(index == count - 1, angle, 0.0), cells.shape[0])
    before = before.reshape(tail.shape)
    after = after.reshape(head.shape)
    return jnp.concatenate([before, cells, after], axis=dim)


def turn_flat(flat, phase_angle, channels):
    share = flat.shape[0] // channels
    half = (channels - 1) // 2 * share
    turned = rotate(jnp.stack([flat[:half], flat[half : 2 * half]]), phase_angle)
    return jnp.concatenate([turned[0], turned[1], flat[2 * half :]])


def tree_sum(value, axis):
    count = lax.axis_size(axis)
    if count & (count - 1):
        return lax.psum(value, axis)
    step = 1
    while step < count:
        value = value + lax.ppermute(value, axis, [(i, i ^ step) for i in range(count)])
        step *= 2
    return value


def pack_hermitian(real_part, imag_part):
    order_size = real_part.shape[0]
    upper = jnp.arange(order_size)[:, None] <= jnp.arange(order_size)[None, :]
    return jnp.where(upper, real_part, imag_part)


def unpack_hermitian(packed):
    order_size = packed.shape[0]
    upper = jnp.arange(order_size)[:, None] <= jnp.arange(order_size)[None, :]
    strict_upper = jnp.arange(order_size)[:, None] < jnp.arange(order_size)[None, :]
    real_upper = jnp.where(upper, packed, 0.0)
    real_part = real_upper + jnp.where(strict_upper, packed, 0.0).T
    imag_lower = jnp.where(upper, 0.0, packed)
    return (real_part, imag_lower - imag_lower.T)


def matrix_kernel(packed_ref, field_ref, basis_ref, red_ref, work_ref, *, band_count, scale):
    highest = lax.Precision.HIGHEST

    def dot(first, second):
        return jnp.dot(first, second, precision=highest, preferred_element_type=jnp.float32)

    size = work_ref.shape[-1]
    ext = packed_ref.shape[-1]
    raw = 3 * band_count
    half = size // 2
    work_ref[...] = jnp.zeros(work_ref.shape, jnp.float32)
    work_ref[0, :ext, :ext] = packed_ref[0]
    work_ref[1, :ext, :ext] = packed_ref[1]
    rows = lax.broadcasted_iota(jnp.int32, (size, size), 0)
    cols = lax.broadcasted_iota(jnp.int32, (size, size), 1)
    upper = rows <= cols
    strict = rows < cols
    eye = rows == cols
    corner = (rows < half) & (cols < half)

    def spread(value, axis):
        return pltpu.roll(value, half, axis)

    def embed(real_part, imag_part):
        return real_part + spread(spread(real_part, 0), 1) - spread(imag_part, 1) + spread(imag_part, 0)

    def unpack(packed):
        mirrored = packed.T
        real_part = jnp.where(upper, packed, mirrored)
        imag_part = jnp.where(upper, jnp.where(strict, -mirrored, 0.0), packed)
        return real_part, imag_part

    gram_re, gram_im = unpack(work_ref[0])
    ham_re, ham_im = unpack(work_ref[1])
    band_diag = eye & (rows < band_count)
    quotient = jnp.where(band_diag, ham_re, 0.0) / jnp.where(band_diag, gram_re, 1.0)
    shifted = pltpu.roll(pltpu.roll(quotient, 2 * band_count, 0), band_count, 1)
    kept = (eye & (cols < 2 * band_count)) | (
        (rows == cols + band_count) & (cols >= 2 * band_count) & (cols < raw)
    )
    mixing = kept.astype(jnp.float32) - shifted
    mixing = mixing + spread(spread(mixing, 0), 1)
    embedded = dot(mixing.T, dot(embed(gram_re, gram_im), mixing))
    active = (rows < raw) | ((rows >= half) & (rows < half + raw))
    identity = (eye & active).astype(jnp.float32)
    total = jnp.sum(jnp.sum(embedded * embedded, axis=0, keepdims=True), axis=1, keepdims=True)
    magnitude = jnp.sqrt(total)
    current = embedded / magnitude
    inverse = identity
    for step in range(NS_STEPS):
        if step == 0:
            factor = 1.5 * identity - 0.5 * current
            current, inverse = dot(current, factor), factor
        else:
            factor = 1.5 * identity - 0.5 * dot(inverse, current)
            current, inverse = dot(current, factor), dot(factor, inverse)
    root = inverse / jnp.sqrt(magnitude)
    root = embed(jnp.where(corner, root, 0.0), jnp.where(corner, spread(root, 0), 0.0))
    rotation = dot(mixing, root)
    work_ref[1] = dot(rotation.T, dot(embed(ham_re, ham_im), rotation))
    red_ref[:, 0, :] = work_ref[1, :raw, :raw]
    red_ref[:, 1, :] = work_ref[1, half : half + raw, :raw]
    rotation = jnp.where(corner | ~((rows < half) | (cols < half)), rotation, -rotation)
    packed_rotation = jnp.where(
        cols < raw,
        rotation,
        jnp.where(cols < 2 * raw, pltpu.roll(rotation, size - half + raw, 1), 0.0),
    )
    packed_rotation = jnp.where(
        rows < ext,
        packed_rotation,
        jnp.where(rows < 2 * ext, pltpu.roll(packed_rotation, size - half + ext, 0), 0.0),
    )
    work_ref[0] = scale * packed_rotation.T
    rotation_t = work_ref[0, : 2 * raw, : 2 * ext]
    for row in range(field_ref.shape[1]):
        basis_ref[:, row, :] = dot(rotation_t, field_ref[:, row, :])


def matrix_stage(packed, fields, band_count, scale):
    size = 128
    raw = 3 * band_count
    vmem = pl.BlockSpec(memory_space=pltpu.VMEM)
    return pl.pallas_call(
        functools.partial(matrix_kernel, band_count=band_count, scale=scale),
        out_shape=(
            jax.ShapeDtypeStruct((2 * raw,) + fields.shape[1:], jnp.float32),
            jax.ShapeDtypeStruct((raw, 2, raw), jnp.float32),
        ),
        in_specs=[vmem, vmem],
        out_specs=(vmem, vmem),
        scratch_shapes=[pltpu.VMEM((2, size, size), jnp.float32)],
    )(packed, fields)


def body(bands, directions, materials, permittivity, wavevector):
    band_count = bands.shape[1]
    height = bands.shape[2]
    breadth = bands.shape[3]
    levels = jnp.arange(permittivity.shape[0], dtype=jnp.int32)

    def stiffness_of(cells):
        return jnp.sum(
            jnp.where(
                cells[None] == levels.astype(jnp.float32)[:, None, None],
                (1.0 / permittivity)[:, None, None],
                0.0,
            ),
            axis=0,
        )

    def strip_of(start, stop):
        field_rows = jnp.concatenate(
            [bands[:, :, start:stop], directions[:, :, start:stop]], axis=1
        ).reshape(4 * band_count, stop - start, breadth)
        return jnp.concatenate([field_rows, material_grid[None, start:stop]], axis=0)

    material_grid = materials.astype(jnp.float32)
    angle_row = 2.0 * math.pi * wavevector[0].astype(jnp.float32) / KDEN
    angle_col = 2.0 * math.pi * wavevector[1].astype(jnp.float32) / KDEN
    fields = jnp.concatenate([bands, directions], axis=1)
    packed = jnp.concatenate(
        [fields.reshape(4 * band_count, height, breadth), material_grid[None]], axis=0
    )
    padded = exchange_rim(
        packed, "row", 1, 2, (strip_of(0, 2), strip_of(height - 2, height)), angle_row
    )
    padded = exchange_rim(padded, "col", 2, 2, angle=angle_col)
    stiff_wide = stiffness_of(padded[-1])
    field_wide = padded[:-1].reshape(2, 2 * band_count, height + 4, breadth + 4)
    band_wide = field_wide[:, :band_count]
    applied_ring, diagonal_ring = stencil(band_wide, stiff_wide)
    stiff_ring = stiff_wide[1:-1, 1:-1]
    scaled_ring = jnp.concatenate(
        [
            applied_ring / diagonal_ring,
            band_wide[:, :, 1:-1, 1:-1] / diagonal_ring,
            field_wide[:, band_count:, 1:-1, 1:-1],
        ],
        axis=1,
    )
    extra_applied = stencil(scaled_ring, stiff_ring)[0]
    applied_cycle = applied_ring[:, :, 1:-1, 1:-1]
    scaled_image = scaled_ring[:, :band_count, 1:-1, 1:-1]
    scaled_bands = scaled_ring[:, band_count : 2 * band_count, 1:-1, 1:-1]
    extended = jnp.concatenate([bands, scaled_image, scaled_bands, directions], axis=1)
    extended_applied = jnp.concatenate([applied_cycle, extra_applied], axis=1)
    local_gram = complex_gram(extended, extended)
    local_ham = complex_gram(extended, extended_applied)
    summed = jnp.stack([pack_hermitian(*local_gram), pack_hermitian(*local_ham)])
    summed = tree_sum(tree_sum(summed.reshape(-1), "row"), "col").reshape(summed.shape)
    raw_count = 3 * band_count
    ext_count = 4 * band_count
    scale_factor = math.sqrt(height * breadth * lax.axis_size("row") * lax.axis_size("col"))
    basis, red = matrix_stage(
        summed, extended.reshape(2 * ext_count, height, breadth), band_count, scale_factor
    )
    reduced = jnp.transpose(red, (1, 0, 2))
    basis = basis.reshape(2, raw_count, height, breadth)
    return (basis, reduced)


def solution(mesh):
    placed = (P(None, None, "row", "col"), P(None, None, "row", "col"), P("row", "col"), P(), P())
    return jax.shard_map(
        body,
        mesh=mesh,
        in_specs=placed,
        out_specs=(P(None, None, "row", "col"), P()),
        check_vma=False,
    )
```

```python
import functools
import math

import jax
import jax.numpy as jnp
from jax import lax
from jax.experimental import pallas as pl
from jax.experimental.pallas import tpu as pltpu
from jax.sharding import PartitionSpec as P

KDEN = 16
NS_STEPS = 5


def rotate(values, phase_angle):
    cosine = jnp.cos(phase_angle)
    sine_part = jnp.sin(phase_angle)
    return jnp.stack(
        [values[0] * cosine - values[1] * sine_part, values[0] * sine_part + values[1] * cosine]
    )


def stencil(padded, stiff_pad):
    centre = stiff_pad[1:-1, 1:-1]
    upward = 0.5 * (centre + stiff_pad[:-2, 1:-1])
    downward = 0.5 * (centre + stiff_pad[2:, 1:-1])
    leftward = 0.5 * (centre + stiff_pad[1:-1, :-2])
    rightward = 0.5 * (centre + stiff_pad[1:-1, 2:])
    diagonal = upward + downward + leftward + rightward
    inner_cells = padded[:, :, 1:-1, 1:-1]
    neighbours = (
        upward * padded[:, :, :-2, 1:-1]
        + downward * padded[:, :, 2:, 1:-1]
        + leftward * padded[:, :, 1:-1, :-2]
        + rightward * padded[:, :, 1:-1, 2:]
    )
    return (diagonal * inner_cells - neighbours, diagonal)


def complex_gram(first_block, second_block):
    count = first_block.shape[1]
    first_flat = first_block.reshape((2 * count,) + first_block.shape[2:])
    second_flat = second_block.reshape((2 * count,) + second_block.shape[2:])
    products = jnp.einsum(
        "jrc,krc->jk", first_flat, second_flat, precision=lax.Precision.HIGHEST
    )
    real_part = products[:count, :count] + products[count:, count:]
    imag_part = products[:count, count:] - products[count:, :count]
    return (real_part, imag_part)


def inverse_root(gram_real, gram_imag):
    highest = lax.Precision.HIGHEST
    order_size = gram_real.shape[0]
    upper_half = jnp.concatenate([gram_real, -gram_imag], axis=1)
    lower_half = jnp.concatenate([gram_imag, gram_real], axis=1)
    embedded = jnp.concatenate([upper_half, lower_half], axis=0)
    magnitude = jnp.sqrt(jnp.sum(embedded * embedded))
    identity = jnp.eye(2 * order_size, dtype=embedded.dtype)

    def newton(turn_index, carried):
        current, inverse = carried
        factor = 1.5 * identity - 0.5 * jnp.dot(inverse, current, precision=highest)
        return (
            jnp.dot(current, factor, precision=highest),
            jnp.dot(factor, inverse, precision=highest),
        )

    current, inverse = lax.fori_loop(0, NS_STEPS, newton, (embedded / magnitude, identity))
    root_full = inverse / jnp.sqrt(magnitude)
    return (root_full[:order_size, :order_size], root_full[order_size:, :order_size])


def reduce_matrix(root_real, root_imag, ham_real, ham_imag):
    highest = lax.Precision.HIGHEST
    prod_real = jnp.dot(ham_real, root_real, precision=highest) - jnp.dot(
        ham_imag, root_imag, precision=highest
    )
    prod_imag = jnp.dot(ham_real, root_imag, precision=highest) + jnp.dot(
        ham_imag, root_real, precision=highest
    )
    red_real = jnp.dot(root_real.T, prod_real, precision=highest) + jnp.dot(
        root_imag.T, prod_imag, precision=highest
    )
    red_imag = jnp.dot(root_real.T, prod_imag, precision=highest) - jnp.dot(
        root_imag.T, prod_real, precision=highest
    )
    return jnp.stack([red_real, red_imag])


def rotate_basis(raw_basis, root_real, root_imag, scale_factor):
    highest = lax.Precision.HIGHEST
    basis_real = jnp.einsum("jrc,jk->krc", raw_basis[0], root_real, precision=highest) - jnp.einsum(
        "jrc,jk->krc", raw_basis[1], root_imag, precision=highest
    )
    basis_imag = jnp.einsum("jrc,jk->krc", raw_basis[0], root_imag, precision=highest) + jnp.einsum(
        "jrc,jk->krc", raw_basis[1], root_real, precision=highest
    )
    return scale_factor * jnp.stack([basis_real, basis_imag])


def project_mixing(mixing, matrix):
    highest = lax.Precision.HIGHEST
    return jnp.dot(mixing.T, jnp.dot(matrix, mixing, precision=highest), precision=highest)


def exchange_rim(cells, axis, dim, width, strips=None, angle=None):
    count = lax.axis_size(axis)
    if strips is None:
        head = lax.slice_in_dim(cells, 0, width, axis=dim)
        tail = lax.slice_in_dim(cells, cells.shape[dim] - width, cells.shape[dim], axis=dim)
    else:
        head, tail = strips
    if count % 2:
        before = lax.ppermute(tail.reshape(-1), axis, [(i, (i + 1) % count) for i in range(count)])
        after = lax.ppermute(head.reshape(-1), axis, [((i + 1) % count, i) for i in range(count)])
    else:
        even = lax.axis_index(axis) % 2 == 0
        first = lax.ppermute(
            jnp.where(even, tail, head).reshape(-1), axis, [(i, i ^ 1) for i in range(count)]
        )
        second = lax.ppermute(
            jnp.where(even, head, tail).reshape(-1),
            axis,
            [(i, (i + 1) % count if i % 2 else (i - 1) % count) for i in range(count)],
        )
        before = jnp.where(even, second, first)
        after = jnp.where(even, first, second)
    if angle is not None:
        index = lax.axis_index(axis)
        before = turn_flat(before, jnp.where(index == 0, -angle, 0.0), cells.shape[0])
        after = turn_flat(after, jnp.where(index == count - 1, angle, 0.0), cells.shape[0])
    before = before.reshape(tail.shape)
    after = after.reshape(head.shape)
    return jnp.concatenate([before, cells, after], axis=dim)


def turn_flat(flat, phase_angle, channels):
    share = flat.shape[0] // channels
    half = (channels - 1) // 2 * share
    turned = rotate(jnp.stack([flat[:half], flat[half : 2 * half]]), phase_angle)
    return jnp.concatenate([turned[0], turned[1], flat[2 * half :]])


def tree_sum(value, axis):
    count = lax.axis_size(axis)
    if count & (count - 1):
        return lax.psum(value, axis)
    step = 1
    while step < count:
        value = value + lax.ppermute(value, axis, [(i, i ^ step) for i in range(count)])
        step *= 2
    return value


def pack_hermitian(real_part, imag_part):
    order_size = real_part.shape[0]
    upper = jnp.arange(order_size)[:, None] <= jnp.arange(order_size)[None, :]
    return jnp.where(upper, real_part, imag_part)


def unpack_hermitian(packed):
    order_size = packed.shape[0]
    upper = jnp.arange(order_size)[:, None] <= jnp.arange(order_size)[None, :]
    strict_upper = jnp.arange(order_size)[:, None] < jnp.arange(order_size)[None, :]
    real_upper = jnp.where(upper, packed, 0.0)
    real_part = real_upper + jnp.where(strict_upper, packed, 0.0).T
    imag_lower = jnp.where(upper, 0.0, packed)
    return (real_part, imag_lower - imag_lower.T)


def matrix_kernel(packed_ref, field_ref, basis_ref, red_ref, work_ref, *, band_count, scale):
    highest = lax.Precision.HIGHEST

    def dot(first, second):
        return jnp.dot(first, second, precision=highest, preferred_element_type=jnp.float32)

    size = work_ref.shape[-1]
    ext = packed_ref.shape[-1]
    raw = 3 * band_count
    half = size // 2
    work_ref[...] = jnp.zeros(work_ref.shape, jnp.float32)
    work_ref[0, :ext, :ext] = packed_ref[0]
    work_ref[1, :ext, :ext] = packed_ref[1]
    rows = lax.broadcasted_iota(jnp.int32, (size, size), 0)
    cols = lax.broadcasted_iota(jnp.int32, (size, size), 1)
    upper = rows <= cols
    strict = rows < cols
    eye = rows == cols
    corner = (rows < half) & (cols < half)

    def spread(value, axis):
        return pltpu.roll(value, half, axis)

    def embed(real_part, imag_part):
        return real_part + spread(spread(real_part, 0), 1) - spread(imag_part, 1) + spread(imag_part, 0)

    def unpack(packed):
        real_part = jnp.where(upper, packed, 0.0) + jnp.where(strict, packed, 0.0).T
        lower = jnp.where(upper, 0.0, packed)
        return real_part, lower - lower.T

    gram_re, gram_im = unpack(work_ref[0])
    ham_re, ham_im = unpack(work_ref[1])
    band_diag = eye & (rows < band_count)
    quotient = jnp.where(band_diag, ham_re, 0.0) / jnp.where(band_diag, gram_re, 1.0)
    shifted = pltpu.roll(pltpu.roll(quotient, 2 * band_count, 0), band_count, 1)
    kept = (eye & (cols < 2 * band_count)) | (
        (rows == cols + band_count) & (cols >= 2 * band_count) & (cols < raw)
    )
    mixing = kept.astype(jnp.float32) - shifted
    mixing = mixing + spread(spread(mixing, 0), 1)
    kept_t = (eye & (rows < 2 * band_count)) | (
        (cols == rows + band_count) & (rows >= 2 * band_count) & (rows < raw)
    )
    shifted_t = pltpu.roll(pltpu.roll(quotient, band_count, 0), 2 * band_count, 1)
    mixing_t = kept_t.astype(jnp.float32) - shifted_t
    mixing_t = mixing_t + spread(spread(mixing_t, 0), 1)
    embedded = dot(mixing_t, dot(embed(gram_re, gram_im), mixing))
    active = (rows < raw) | ((rows >= half) & (rows < half + raw))
    identity = (eye & active).astype(jnp.float32)
    total = jnp.sum(jnp.sum(embedded * embedded, axis=0, keepdims=True), axis=1, keepdims=True)
    magnitude = jnp.sqrt(total)
    current = embedded / magnitude
    inverse = identity
    for step in range(NS_STEPS):
        if step == 0:
            factor = 1.5 * identity - 0.5 * current
            current, inverse = dot(current, factor), factor
        else:
            factor = 1.5 * identity - 0.5 * dot(inverse, current)
            current, inverse = dot(current, factor), dot(factor, inverse)
    root = inverse / jnp.sqrt(magnitude)
    root = embed(jnp.where(corner, root, 0.0), jnp.where(corner, spread(root, 0), 0.0))
    rotation = dot(mixing, root)
    work_ref[1] = dot(rotation.T, dot(embed(ham_re, ham_im), rotation))
    red_ref[:, 0, :] = work_ref[1, :raw, :raw]
    red_ref[:, 1, :] = work_ref[1, half : half + raw, :raw]
    rotation = jnp.where(corner | ~((rows < half) | (cols < half)), rotation, -rotation)
    packed_rotation = jnp.where(
        cols < raw,
        rotation,
        jnp.where(cols < 2 * raw, pltpu.roll(rotation, size - half + raw, 1), 0.0),
    )
    packed_rotation = jnp.where(
        rows < ext,
        packed_rotation,
        jnp.where(rows < 2 * ext, pltpu.roll(packed_rotation, size - half + ext, 0), 0.0),
    )
    work_ref[0] = scale * packed_rotation.T
    rotation_t = work_ref[0, : 2 * raw, : 2 * ext]
    for row in range(field_ref.shape[1]):
        basis_ref[:, row, :] = dot(rotation_t, field_ref[:, row, :])


def matrix_stage(packed, fields, band_count, scale):
    size = 128
    raw = 3 * band_count
    vmem = pl.BlockSpec(memory_space=pltpu.VMEM)
    return pl.pallas_call(
        functools.partial(matrix_kernel, band_count=band_count, scale=scale),
        out_shape=(
            jax.ShapeDtypeStruct((2 * raw,) + fields.shape[1:], jnp.float32),
            jax.ShapeDtypeStruct((raw, 2, raw), jnp.float32),
        ),
        in_specs=[vmem, vmem],
        out_specs=(vmem, vmem),
        scratch_shapes=[pltpu.VMEM((2, size, size), jnp.float32)],
    )(packed, fields)


def body(bands, directions, materials, permittivity, wavevector):
    band_count = bands.shape[1]
    height = bands.shape[2]
    breadth = bands.shape[3]
    levels = jnp.arange(permittivity.shape[0], dtype=jnp.int32)

    def stiffness_of(cells):
        return jnp.sum(
            jnp.where(
                cells[None] == levels.astype(jnp.float32)[:, None, None],
                (1.0 / permittivity)[:, None, None],
                0.0,
            ),
            axis=0,
        )

    def strip_of(start, stop):
        field_rows = jnp.concatenate(
            [bands[:, :, start:stop], directions[:, :, start:stop]], axis=1
        ).reshape(4 * band_count, stop - start, breadth)
        return jnp.concatenate([field_rows, material_grid[None, start:stop]], axis=0)

    material_grid = materials.astype(jnp.float32)
    angle_row = 2.0 * math.pi * wavevector[0].astype(jnp.float32) / KDEN
    angle_col = 2.0 * math.pi * wavevector[1].astype(jnp.float32) / KDEN
    fields = jnp.concatenate([bands, directions], axis=1)
    packed = jnp.concatenate(
        [fields.reshape(4 * band_count, height, breadth), material_grid[None]], axis=0
    )
    padded = exchange_rim(
        packed, "row", 1, 2, (strip_of(0, 2), strip_of(height - 2, height)), angle_row
    )
    padded = exchange_rim(padded, "col", 2, 2, angle=angle_col)
    stiff_wide = stiffness_of(padded[-1])
    field_wide = padded[:-1].reshape(2, 2 * band_count, height + 4, breadth + 4)
    band_wide = field_wide[:, :band_count]
    applied_ring, diagonal_ring = stencil(band_wide, stiff_wide)
    stiff_ring = stiff_wide[1:-1, 1:-1]
    scaled_ring = jnp.concatenate(
        [
            applied_ring / diagonal_ring,
            band_wide[:, :, 1:-1, 1:-1] / diagonal_ring,
            field_wide[:, band_count:, 1:-1, 1:-1],
        ],
        axis=1,
    )
    extra_applied = stencil(scaled_ring, stiff_ring)[0]
    applied_cycle = applied_ring[:, :, 1:-1, 1:-1]
    scaled_image = scaled_ring[:, :band_count, 1:-1, 1:-1]
    scaled_bands = scaled_ring[:, band_count : 2 * band_count, 1:-1, 1:-1]
    extended = jnp.concatenate([bands, scaled_image, scaled_bands, directions], axis=1)
    extended_applied = jnp.concatenate([applied_cycle, extra_applied], axis=1)
    local_gram = complex_gram(extended, extended)
    local_ham = complex_gram(extended, extended_applied)
    summed = jnp.stack([pack_hermitian(*local_gram), pack_hermitian(*local_ham)])
    summed = tree_sum(tree_sum(summed.reshape(-1), "row"), "col").reshape(summed.shape)
    raw_count = 3 * band_count
    ext_count = 4 * band_count
    scale_factor = math.sqrt(height * breadth * lax.axis_size("row") * lax.axis_size("col"))
    basis, red = matrix_stage(
        summed, extended.reshape(2 * ext_count, height, breadth), band_count, scale_factor
    )
    reduced = jnp.transpose(red, (1, 0, 2))
    basis = basis.reshape(2, raw_count, height, breadth)
    return (basis, reduced)


def solution(mesh):
    placed = (P(None, None, "row", "col"), P(None, None, "row", "col"), P("row", "col"), P(), P())
    return jax.shard_map(
        body,
        mesh=mesh,
        in_specs=placed,
        out_specs=(P(None, None, "row", "col"), P()),
        check_vma=False,
    )
```

```python
import functools
import math

import jax
import jax.numpy as jnp
from jax import lax
from jax.experimental import pallas as pl
from jax.experimental.pallas import tpu as pltpu
from jax.sharding import PartitionSpec as P

KDEN = 16
NS_STEPS = 5


def rotate(values, phase_angle):
    cosine = jnp.cos(phase_angle)
    sine_part = jnp.sin(phase_angle)
    return jnp.stack(
        [values[0] * cosine - values[1] * sine_part, values[0] * sine_part + values[1] * cosine]
    )


def stencil(padded, stiff_pad):
    centre = stiff_pad[1:-1, 1:-1]
    upward = 0.5 * (centre + stiff_pad[:-2, 1:-1])
    downward = 0.5 * (centre + stiff_pad[2:, 1:-1])
    leftward = 0.5 * (centre + stiff_pad[1:-1, :-2])
    rightward = 0.5 * (centre + stiff_pad[1:-1, 2:])
    diagonal = upward + downward + leftward + rightward
    inner_cells = padded[:, :, 1:-1, 1:-1]
    neighbours = (
        upward * padded[:, :, :-2, 1:-1]
        + downward * padded[:, :, 2:, 1:-1]
        + leftward * padded[:, :, 1:-1, :-2]
        + rightward * padded[:, :, 1:-1, 2:]
    )
    return (diagonal * inner_cells - neighbours, diagonal)


def complex_gram(first_block, second_block):
    count = first_block.shape[1]
    first_flat = first_block.reshape((2 * count,) + first_block.shape[2:])
    second_flat = second_block.reshape((2 * count,) + second_block.shape[2:])
    products = jnp.einsum(
        "jrc,krc->jk", first_flat, second_flat, precision=lax.Precision.HIGHEST
    )
    real_part = products[:count, :count] + products[count:, count:]
    imag_part = products[:count, count:] - products[count:, :count]
    return (real_part, imag_part)


def inverse_root(gram_real, gram_imag):
    highest = lax.Precision.HIGHEST
    order_size = gram_real.shape[0]
    upper_half = jnp.concatenate([gram_real, -gram_imag], axis=1)
    lower_half = jnp.concatenate([gram_imag, gram_real], axis=1)
    embedded = jnp.concatenate([upper_half, lower_half], axis=0)
    magnitude = jnp.sqrt(jnp.sum(embedded * embedded))
    identity = jnp.eye(2 * order_size, dtype=embedded.dtype)

    def newton(turn_index, carried):
        current, inverse = carried
        factor = 1.5 * identity - 0.5 * jnp.dot(inverse, current, precision=highest)
        return (
            jnp.dot(current, factor, precision=highest),
            jnp.dot(factor, inverse, precision=highest),
        )

    current, inverse = lax.fori_loop(0, NS_STEPS, newton, (embedded / magnitude, identity))
    root_full = inverse / jnp.sqrt(magnitude)
    return (root_full[:order_size, :order_size], root_full[order_size:, :order_size])


def reduce_matrix(root_real, root_imag, ham_real, ham_imag):
    highest = lax.Precision.HIGHEST
    prod_real = jnp.dot(ham_real, root_real, precision=highest) - jnp.dot(
        ham_imag, root_imag, precision=highest
    )
    prod_imag = jnp.dot(ham_real, root_imag, precision=highest) + jnp.dot(
        ham_imag, root_real, precision=highest
    )
    red_real = jnp.dot(root_real.T, prod_real, precision=highest) + jnp.dot(
        root_imag.T, prod_imag, precision=highest
    )
    red_imag = jnp.dot(root_real.T, prod_imag, precision=highest) - jnp.dot(
        root_imag.T, prod_real, precision=highest
    )
    return jnp.stack([red_real, red_imag])


def rotate_basis(raw_basis, root_real, root_imag, scale_factor):
    highest = lax.Precision.HIGHEST
    basis_real = jnp.einsum("jrc,jk->krc", raw_basis[0], root_real, precision=highest) - jnp.einsum(
        "jrc,jk->krc", raw_basis[1], root_imag, precision=highest
    )
    basis_imag = jnp.einsum("jrc,jk->krc", raw_basis[0], root_imag, precision=highest) + jnp.einsum(
        "jrc,jk->krc", raw_basis[1], root_real, precision=highest
    )
    return scale_factor * jnp.stack([basis_real, basis_imag])


def project_mixing(mixing, matrix):
    highest = lax.Precision.HIGHEST
    return jnp.dot(mixing.T, jnp.dot(matrix, mixing, precision=highest), precision=highest)


def exchange_rim(cells, axis, dim, width, strips=None, angle=None):
    count = lax.axis_size(axis)
    if strips is None:
        head = lax.slice_in_dim(cells, 0, width, axis=dim)
        tail = lax.slice_in_dim(cells, cells.shape[dim] - width, cells.shape[dim], axis=dim)
    else:
        head, tail = strips
    if count % 2:
        before = lax.ppermute(tail.reshape(-1), axis, [(i, (i + 1) % count) for i in range(count)])
        after = lax.ppermute(head.reshape(-1), axis, [((i + 1) % count, i) for i in range(count)])
    else:
        even = lax.axis_index(axis) % 2 == 0
        first = lax.ppermute(
            jnp.where(even, tail, head).reshape(-1), axis, [(i, i ^ 1) for i in range(count)]
        )
        second = lax.ppermute(
            jnp.where(even, head, tail).reshape(-1),
            axis,
            [(i, (i + 1) % count if i % 2 else (i - 1) % count) for i in range(count)],
        )
        before = jnp.where(even, second, first)
        after = jnp.where(even, first, second)
    if angle is not None:
        index = lax.axis_index(axis)
        before = turn_flat(before, jnp.where(index == 0, -angle, 0.0), cells.shape[0])
        after = turn_flat(after, jnp.where(index == count - 1, angle, 0.0), cells.shape[0])
    before = before.reshape(tail.shape)
    after = after.reshape(head.shape)
    return jnp.concatenate([before, cells, after], axis=dim)


def turn_flat(flat, phase_angle, channels):
    share = flat.shape[0] // channels
    half = (channels - 1) // 2 * share
    turned = rotate(jnp.stack([flat[:half], flat[half : 2 * half]]), phase_angle)
    return jnp.concatenate([turned[0], turned[1], flat[2 * half :]])


def tree_sum(value, axis, radix=2):
    count = lax.axis_size(axis)
    if count & (count - 1):
        return lax.psum(value, axis)

    def swap(part, step):
        return lax.ppermute(part, axis, [(i, i ^ step) for i in range(count)])

    step = 1
    while step < count:
        if radix == 4 and 4 * step <= count:
            value = (value + swap(value, step)) + (swap(value, 2 * step) + swap(value, 3 * step))
            step *= 4
        else:
            value = value + swap(value, step)
            step *= 2
    return value


def pack_hermitian(real_part, imag_part):
    order_size = real_part.shape[0]
    upper = jnp.arange(order_size)[:, None] <= jnp.arange(order_size)[None, :]
    return jnp.where(upper, real_part, imag_part)


def unpack_hermitian(packed):
    order_size = packed.shape[0]
    upper = jnp.arange(order_size)[:, None] <= jnp.arange(order_size)[None, :]
    strict_upper = jnp.arange(order_size)[:, None] < jnp.arange(order_size)[None, :]
    real_upper = jnp.where(upper, packed, 0.0)
    real_part = real_upper + jnp.where(strict_upper, packed, 0.0).T
    imag_lower = jnp.where(upper, 0.0, packed)
    return (real_part, imag_lower - imag_lower.T)


def matrix_kernel(packed_ref, field_ref, basis_ref, red_ref, work_ref, *, band_count, scale):
    highest = lax.Precision.HIGHEST

    def dot(first, second):
        return jnp.dot(first, second, precision=highest, preferred_element_type=jnp.float32)

    size = work_ref.shape[-1]
    ext = packed_ref.shape[-1]
    raw = 3 * band_count
    half = size // 2
    work_ref[...] = jnp.zeros(work_ref.shape, jnp.float32)
    work_ref[0, :ext, :ext] = packed_ref[0]
    work_ref[1, :ext, :ext] = packed_ref[1]
    rows = lax.broadcasted_iota(jnp.int32, (size, size), 0)
    cols = lax.broadcasted_iota(jnp.int32, (size, size), 1)
    upper = rows <= cols
    strict = rows < cols
    eye = rows == cols
    corner = (rows < half) & (cols < half)

    def spread(value, axis):
        return pltpu.roll(value, half, axis)

    def embed(real_part, imag_part):
        return real_part + spread(spread(real_part, 0), 1) - spread(imag_part, 1) + spread(imag_part, 0)

    def unpack(packed):
        real_part = jnp.where(upper, packed, 0.0) + jnp.where(strict, packed, 0.0).T
        lower = jnp.where(upper, 0.0, packed)
        return real_part, lower - lower.T

    gram_re, gram_im = unpack(work_ref[0])
    ham_re, ham_im = unpack(work_ref[1])
    band_diag = eye & (rows < band_count)
    quotient = jnp.where(band_diag, ham_re, 0.0) / jnp.where(band_diag, gram_re, 1.0)
    shifted = pltpu.roll(pltpu.roll(quotient, 2 * band_count, 0), band_count, 1)
    kept = (eye & (cols < 2 * band_count)) | (
        (rows == cols + band_count) & (cols >= 2 * band_count) & (cols < raw)
    )
    mixing = kept.astype(jnp.float32) - shifted
    mixing = mixing + spread(spread(mixing, 0), 1)
    embedded = dot(mixing.T, dot(embed(gram_re, gram_im), mixing))
    active = (rows < raw) | ((rows >= half) & (rows < half + raw))
    identity = (eye & active).astype(jnp.float32)
    total = jnp.sum(jnp.sum(embedded * embedded, axis=0, keepdims=True), axis=1, keepdims=True)
    magnitude = jnp.sqrt(total)
    current = embedded / magnitude
    inverse = identity
    for step in range(NS_STEPS):
        if step == 0:
            factor = 1.5 * identity - 0.5 * current
            current, inverse = dot(current, factor), factor
        else:
            factor = 1.5 * identity - 0.5 * dot(inverse, current)
            current, inverse = dot(current, factor), dot(factor, inverse)
    root = inverse / jnp.sqrt(magnitude)
    root = embed(jnp.where(corner, root, 0.0), jnp.where(corner, spread(root, 0), 0.0))
    rotation = dot(mixing, root)
    work_ref[1] = dot(rotation.T, dot(embed(ham_re, ham_im), rotation))
    red_ref[:, 0, :] = work_ref[1, :raw, :raw]
    red_ref[:, 1, :] = work_ref[1, half : half + raw, :raw]
    rotation = jnp.where(corner | ~((rows < half) | (cols < half)), rotation, -rotation)
    packed_rotation = jnp.where(
        cols < raw,
        rotation,
        jnp.where(cols < 2 * raw, pltpu.roll(rotation, size - half + raw, 1), 0.0),
    )
    packed_rotation = jnp.where(
        rows < ext,
        packed_rotation,
        jnp.where(rows < 2 * ext, pltpu.roll(packed_rotation, size - half + ext, 0), 0.0),
    )
    work_ref[0] = scale * packed_rotation.T
    rotation_t = work_ref[0, : 2 * raw, : 2 * ext]
    for row in range(field_ref.shape[1]):
        basis_ref[:, row, :] = dot(rotation_t, field_ref[:, row, :])


def matrix_stage(packed, fields, band_count, scale):
    size = 128
    raw = 3 * band_count
    vmem = pl.BlockSpec(memory_space=pltpu.VMEM)
    return pl.pallas_call(
        functools.partial(matrix_kernel, band_count=band_count, scale=scale),
        out_shape=(
            jax.ShapeDtypeStruct((2 * raw,) + fields.shape[1:], jnp.float32),
            jax.ShapeDtypeStruct((raw, 2, raw), jnp.float32),
        ),
        in_specs=[vmem, vmem],
        out_specs=(vmem, vmem),
        scratch_shapes=[pltpu.VMEM((2, size, size), jnp.float32)],
    )(packed, fields)


def body(bands, directions, materials, permittivity, wavevector):
    band_count = bands.shape[1]
    height = bands.shape[2]
    breadth = bands.shape[3]
    levels = jnp.arange(permittivity.shape[0], dtype=jnp.int32)

    def stiffness_of(cells):
        return jnp.sum(
            jnp.where(
                cells[None] == levels.astype(jnp.float32)[:, None, None],
                (1.0 / permittivity)[:, None, None],
                0.0,
            ),
            axis=0,
        )

    def strip_of(start, stop):
        field_rows = jnp.concatenate(
            [bands[:, :, start:stop], directions[:, :, start:stop]], axis=1
        ).reshape(4 * band_count, stop - start, breadth)
        return jnp.concatenate([field_rows, material_grid[None, start:stop]], axis=0)

    material_grid = materials.astype(jnp.float32)
    angle_row = 2.0 * math.pi * wavevector[0].astype(jnp.float32) / KDEN
    angle_col = 2.0 * math.pi * wavevector[1].astype(jnp.float32) / KDEN
    fields = jnp.concatenate([bands, directions], axis=1)
    packed = jnp.concatenate(
        [fields.reshape(4 * band_count, height, breadth), material_grid[None]], axis=0
    )
    padded = exchange_rim(
        packed, "row", 1, 2, (strip_of(0, 2), strip_of(height - 2, height)), angle_row
    )
    padded = exchange_rim(padded, "col", 2, 2, angle=angle_col)
    stiff_wide = stiffness_of(padded[-1])
    field_wide = padded[:-1].reshape(2, 2 * band_count, height + 4, breadth + 4)
    band_wide = field_wide[:, :band_count]
    applied_ring, diagonal_ring = stencil(band_wide, stiff_wide)
    stiff_ring = stiff_wide[1:-1, 1:-1]
    scaled_ring = jnp.concatenate(
        [
            applied_ring / diagonal_ring,
            band_wide[:, :, 1:-1, 1:-1] / diagonal_ring,
            field_wide[:, band_count:, 1:-1, 1:-1],
        ],
        axis=1,
    )
    extra_applied = stencil(scaled_ring, stiff_ring)[0]
    applied_cycle = applied_ring[:, :, 1:-1, 1:-1]
    scaled_image = scaled_ring[:, :band_count, 1:-1, 1:-1]
    scaled_bands = scaled_ring[:, band_count : 2 * band_count, 1:-1, 1:-1]
    extended = jnp.concatenate([bands, scaled_image, scaled_bands, directions], axis=1)
    extended_applied = jnp.concatenate([applied_cycle, extra_applied], axis=1)
    local_gram = complex_gram(extended, extended)
    local_ham = complex_gram(extended, extended_applied)
    summed = jnp.stack([pack_hermitian(*local_gram), pack_hermitian(*local_ham)])
    summed = tree_sum(tree_sum(summed.reshape(-1), "row", radix=4), "col").reshape(summed.shape)
    raw_count = 3 * band_count
    ext_count = 4 * band_count
    scale_factor = math.sqrt(height * breadth * lax.axis_size("row") * lax.axis_size("col"))
    basis, red = matrix_stage(
        summed, extended.reshape(2 * ext_count, height, breadth), band_count, scale_factor
    )
    reduced = jnp.transpose(red, (1, 0, 2))
    basis = basis.reshape(2, raw_count, height, breadth)
    return (basis, reduced)


def solution(mesh):
    placed = (P(None, None, "row", "col"), P(None, None, "row", "col"), P("row", "col"), P(), P())
    return jax.shard_map(
        body,
        mesh=mesh,
        in_specs=placed,
        out_specs=(P(None, None, "row", "col"), P()),
        check_vma=False,
    )
```

```python
import functools
import math

import jax
import jax.numpy as jnp
from jax import lax
from jax.experimental import pallas as pl
from jax.experimental.pallas import tpu as pltpu
from jax.sharding import PartitionSpec as P

KDEN = 16
NS_STEPS = 5


def rotate(values, phase_angle):
    cosine = jnp.cos(phase_angle)
    sine_part = jnp.sin(phase_angle)
    return jnp.stack(
        [values[0] * cosine - values[1] * sine_part, values[0] * sine_part + values[1] * cosine]
    )


def stencil(padded, stiff_pad):
    centre = stiff_pad[1:-1, 1:-1]
    upward = 0.5 * (centre + stiff_pad[:-2, 1:-1])
    downward = 0.5 * (centre + stiff_pad[2:, 1:-1])
    leftward = 0.5 * (centre + stiff_pad[1:-1, :-2])
    rightward = 0.5 * (centre + stiff_pad[1:-1, 2:])
    diagonal = upward + downward + leftward + rightward
    inner_cells = padded[:, :, 1:-1, 1:-1]
    neighbours = (
        upward * padded[:, :, :-2, 1:-1]
        + downward * padded[:, :, 2:, 1:-1]
        + leftward * padded[:, :, 1:-1, :-2]
        + rightward * padded[:, :, 1:-1, 2:]
    )
    return (diagonal * inner_cells - neighbours, diagonal)


def complex_gram(first_block, second_block):
    count = first_block.shape[1]
    first_flat = first_block.reshape((2 * count,) + first_block.shape[2:])
    second_flat = second_block.reshape((2 * count,) + second_block.shape[2:])
    products = jnp.einsum(
        "jrc,krc->jk", first_flat, second_flat, precision=lax.Precision.HIGHEST
    )
    real_part = products[:count, :count] + products[count:, count:]
    imag_part = products[:count, count:] - products[count:, :count]
    return (real_part, imag_part)


def inverse_root(gram_real, gram_imag):
    highest = lax.Precision.HIGHEST
    order_size = gram_real.shape[0]
    upper_half = jnp.concatenate([gram_real, -gram_imag], axis=1)
    lower_half = jnp.concatenate([gram_imag, gram_real], axis=1)
    embedded = jnp.concatenate([upper_half, lower_half], axis=0)
    magnitude = jnp.sqrt(jnp.sum(embedded * embedded))
    identity = jnp.eye(2 * order_size, dtype=embedded.dtype)

    def newton(turn_index, carried):
        current, inverse = carried
        factor = 1.5 * identity - 0.5 * jnp.dot(inverse, current, precision=highest)
        return (
            jnp.dot(current, factor, precision=highest),
            jnp.dot(factor, inverse, precision=highest),
        )

    current, inverse = lax.fori_loop(0, NS_STEPS, newton, (embedded / magnitude, identity))
    root_full = inverse / jnp.sqrt(magnitude)
    return (root_full[:order_size, :order_size], root_full[order_size:, :order_size])


def reduce_matrix(root_real, root_imag, ham_real, ham_imag):
    highest = lax.Precision.HIGHEST
    prod_real = jnp.dot(ham_real, root_real, precision=highest) - jnp.dot(
        ham_imag, root_imag, precision=highest
    )
    prod_imag = jnp.dot(ham_real, root_imag, precision=highest) + jnp.dot(
        ham_imag, root_real, precision=highest
    )
    red_real = jnp.dot(root_real.T, prod_real, precision=highest) + jnp.dot(
        root_imag.T, prod_imag, precision=highest
    )
    red_imag = jnp.dot(root_real.T, prod_imag, precision=highest) - jnp.dot(
        root_imag.T, prod_real, precision=highest
    )
    return jnp.stack([red_real, red_imag])


def rotate_basis(raw_basis, root_real, root_imag, scale_factor):
    highest = lax.Precision.HIGHEST
    basis_real = jnp.einsum("jrc,jk->krc", raw_basis[0], root_real, precision=highest) - jnp.einsum(
        "jrc,jk->krc", raw_basis[1], root_imag, precision=highest
    )
    basis_imag = jnp.einsum("jrc,jk->krc", raw_basis[0], root_imag, precision=highest) + jnp.einsum(
        "jrc,jk->krc", raw_basis[1], root_real, precision=highest
    )
    return scale_factor * jnp.stack([basis_real, basis_imag])


def project_mixing(mixing, matrix):
    highest = lax.Precision.HIGHEST
    return jnp.dot(mixing.T, jnp.dot(matrix, mixing, precision=highest), precision=highest)


def exchange_rim(cells, axis, dim, width, strips=None, angle=None):
    count = lax.axis_size(axis)
    if strips is None:
        head = lax.slice_in_dim(cells, 0, width, axis=dim)
        tail = lax.slice_in_dim(cells, cells.shape[dim] - width, cells.shape[dim], axis=dim)
    else:
        head, tail = strips
    if count % 2:
        before = lax.ppermute(tail.reshape(-1), axis, [(i, (i + 1) % count) for i in range(count)])
        after = lax.ppermute(head.reshape(-1), axis, [((i + 1) % count, i) for i in range(count)])
    else:
        even = lax.axis_index(axis) % 2 == 0
        first = lax.ppermute(
            jnp.where(even, tail, head).reshape(-1), axis, [(i, i ^ 1) for i in range(count)]
        )
        second = lax.ppermute(
            jnp.where(even, head, tail).reshape(-1),
            axis,
            [(i, (i + 1) % count if i % 2 else (i - 1) % count) for i in range(count)],
        )
        before = jnp.where(even, second, first)
        after = jnp.where(even, first, second)
    if angle is not None:
        index = lax.axis_index(axis)
        before = turn_flat(before, jnp.where(index == 0, -angle, 0.0), cells.shape[0])
        after = turn_flat(after, jnp.where(index == count - 1, angle, 0.0), cells.shape[0])
    before = before.reshape(tail.shape)
    after = after.reshape(head.shape)
    return jnp.concatenate([before, cells, after], axis=dim)


def turn_flat(flat, phase_angle, channels):
    share = flat.shape[0] // channels
    half = (channels - 1) // 2 * share
    turned = rotate(jnp.stack([flat[:half], flat[half : 2 * half]]), phase_angle)
    return jnp.concatenate([turned[0], turned[1], flat[2 * half :]])


def tree_sum(value, axis, radix=2):
    count = lax.axis_size(axis)
    if count & (count - 1):
        return lax.psum(value, axis)

    def swap(part, step):
        return lax.ppermute(part, axis, [(i, i ^ step) for i in range(count)])

    step = 1
    while step < count:
        if radix == 4 and 4 * step <= count:
            value = (value + swap(value, step)) + (swap(value, 2 * step) + swap(value, 3 * step))
            step *= 4
        else:
            value = value + swap(value, step)
            step *= 2
    return value


def pack_hermitian(real_part, imag_part):
    order_size = real_part.shape[0]
    upper = jnp.arange(order_size)[:, None] <= jnp.arange(order_size)[None, :]
    return jnp.where(upper, real_part, imag_part)


def unpack_hermitian(packed):
    order_size = packed.shape[0]
    upper = jnp.arange(order_size)[:, None] <= jnp.arange(order_size)[None, :]
    strict_upper = jnp.arange(order_size)[:, None] < jnp.arange(order_size)[None, :]
    real_upper = jnp.where(upper, packed, 0.0)
    real_part = real_upper + jnp.where(strict_upper, packed, 0.0).T
    imag_lower = jnp.where(upper, 0.0, packed)
    return (real_part, imag_lower - imag_lower.T)


def matrix_kernel(packed_ref, field_ref, basis_ref, red_ref, work_ref, *, band_count, scale):
    highest = lax.Precision.HIGHEST

    def dot(first, second):
        return jnp.dot(first, second, precision=highest, preferred_element_type=jnp.float32)

    size = work_ref.shape[-1]
    ext = packed_ref.shape[-1]
    raw = 3 * band_count
    half = size // 2
    work_ref[...] = jnp.zeros(work_ref.shape, jnp.float32)
    work_ref[0, :ext, :ext] = packed_ref[0]
    work_ref[1, :ext, :ext] = packed_ref[1]
    rows = lax.broadcasted_iota(jnp.int32, (size, size), 0)
    cols = lax.broadcasted_iota(jnp.int32, (size, size), 1)
    upper = rows <= cols
    strict = rows < cols
    eye = rows == cols
    corner = (rows < half) & (cols < half)

    def spread(value, axis):
        return pltpu.roll(value, half, axis)

    def embed(real_part, imag_part):
        return real_part + spread(spread(real_part, 0), 1) - spread(imag_part, 1) + spread(imag_part, 0)

    def unpack(packed):
        real_part = jnp.where(upper, packed, 0.0) + jnp.where(strict, packed, 0.0).T
        lower = jnp.where(upper, 0.0, packed)
        return real_part, lower - lower.T

    gram_re, gram_im = unpack(work_ref[0])
    ham_re, ham_im = unpack(work_ref[1])
    band_diag = eye & (rows < band_count)
    quotient = jnp.where(band_diag, ham_re, 0.0) / jnp.where(band_diag, gram_re, 1.0)
    shifted = pltpu.roll(pltpu.roll(quotient, 2 * band_count, 0), band_count, 1)
    kept = (eye & (cols < 2 * band_count)) | (
        (rows == cols + band_count) & (cols >= 2 * band_count) & (cols < raw)
    )
    mixing = kept.astype(jnp.float32) - shifted
    mixing = mixing + spread(spread(mixing, 0), 1)
    embedded = dot(mixing.T, dot(embed(gram_re, gram_im), mixing))
    active = (rows < raw) | ((rows >= half) & (rows < half + raw))
    identity = (eye & active).astype(jnp.float32)
    total = jnp.sum(jnp.sum(embedded * embedded, axis=0, keepdims=True), axis=1, keepdims=True)
    magnitude = jnp.sqrt(total)
    current = embedded / magnitude
    inverse = identity
    for step in range(NS_STEPS):
        if step == 0:
            factor = 1.5 * identity - 0.5 * current
            current, inverse = dot(current, factor), factor
        else:
            factor = 1.5 * identity - 0.5 * dot(inverse, current)
            current, inverse = dot(current, factor), dot(factor, inverse)
    root = inverse / jnp.sqrt(magnitude)
    root = embed(jnp.where(corner, root, 0.0), jnp.where(corner, spread(root, 0), 0.0))
    rotation = dot(mixing, root)
    work_ref[1] = dot(rotation.T, dot(embed(ham_re, ham_im), rotation))
    red_ref[:, 0, :] = work_ref[1, :raw, :raw]
    red_ref[:, 1, :] = work_ref[1, half : half + raw, :raw]
    rotation = jnp.where(corner | ~((rows < half) | (cols < half)), rotation, -rotation)
    packed_rotation = jnp.where(
        cols < raw,
        rotation,
        jnp.where(cols < 2 * raw, pltpu.roll(rotation, size - half + raw, 1), 0.0),
    )
    packed_rotation = jnp.where(
        rows < ext,
        packed_rotation,
        jnp.where(rows < 2 * ext, pltpu.roll(packed_rotation, size - half + ext, 0), 0.0),
    )
    work_ref[0] = scale * packed_rotation.T
    rotation_t = work_ref[0, : 2 * raw, : 2 * ext]
    for row in range(field_ref.shape[1]):
        basis_ref[:, row, :] = dot(rotation_t, field_ref[:, row, :])


def matrix_stage(packed, fields, band_count, scale):
    size = 128
    raw = 3 * band_count
    vmem = pl.BlockSpec(memory_space=pltpu.VMEM)
    return pl.pallas_call(
        functools.partial(matrix_kernel, band_count=band_count, scale=scale),
        out_shape=(
            jax.ShapeDtypeStruct((2 * raw,) + fields.shape[1:], jnp.float32),
            jax.ShapeDtypeStruct((raw, 2, raw), jnp.float32),
        ),
        in_specs=[vmem, vmem],
        out_specs=(vmem, vmem),
        scratch_shapes=[pltpu.VMEM((2, size, size), jnp.float32)],
    )(packed, fields)


def body(bands, directions, materials, permittivity, wavevector):
    band_count = bands.shape[1]
    height = bands.shape[2]
    breadth = bands.shape[3]
    levels = jnp.arange(permittivity.shape[0], dtype=jnp.int32)

    def stiffness_of(cells):
        return jnp.sum(
            jnp.where(
                cells[None] == levels.astype(jnp.float32)[:, None, None],
                (1.0 / permittivity)[:, None, None],
                0.0,
            ),
            axis=0,
        )

    def strip_of(start, stop):
        field_rows = jnp.concatenate(
            [bands[:, :, start:stop], directions[:, :, start:stop]], axis=1
        ).reshape(4 * band_count, stop - start, breadth)
        return jnp.concatenate([field_rows, material_grid[None, start:stop]], axis=0)

    material_grid = materials.astype(jnp.float32)
    angle_row = 2.0 * math.pi * wavevector[0].astype(jnp.float32) / KDEN
    angle_col = 2.0 * math.pi * wavevector[1].astype(jnp.float32) / KDEN
    fields = jnp.concatenate([bands, directions], axis=1)
    packed = jnp.concatenate(
        [fields.reshape(4 * band_count, height, breadth), material_grid[None]], axis=0
    )
    padded = exchange_rim(
        packed, "row", 1, 2, (strip_of(0, 2), strip_of(height - 2, height)), angle_row
    )
    padded = exchange_rim(padded, "col", 2, 2, angle=angle_col)
    stiff_wide = stiffness_of(padded[-1])
    field_wide = padded[:-1].reshape(2, 2 * band_count, height + 4, breadth + 4)
    band_wide = field_wide[:, :band_count]
    applied_ring, diagonal_ring = stencil(band_wide, stiff_wide)
    stiff_ring = stiff_wide[1:-1, 1:-1]
    scaled_ring = jnp.concatenate(
        [
            applied_ring / diagonal_ring,
            band_wide[:, :, 1:-1, 1:-1] / diagonal_ring,
            field_wide[:, band_count:, 1:-1, 1:-1],
        ],
        axis=1,
    )
    extra_applied = stencil(scaled_ring, stiff_ring)[0]
    applied_cycle = applied_ring[:, :, 1:-1, 1:-1]
    scaled_image = scaled_ring[:, :band_count, 1:-1, 1:-1]
    scaled_bands = scaled_ring[:, band_count : 2 * band_count, 1:-1, 1:-1]
    extended = jnp.concatenate([bands, scaled_image, scaled_bands, directions], axis=1)
    extended_applied = jnp.concatenate([applied_cycle, extra_applied], axis=1)
    local_gram = complex_gram(extended, extended)
    local_ham = complex_gram(extended, extended_applied)
    summed = jnp.stack([pack_hermitian(*local_gram), pack_hermitian(*local_ham)])
    summed = tree_sum(tree_sum(summed.reshape(-1), "row", radix=4), "col", radix=4).reshape(summed.shape)
    raw_count = 3 * band_count
    ext_count = 4 * band_count
    scale_factor = math.sqrt(height * breadth * lax.axis_size("row") * lax.axis_size("col"))
    basis, red = matrix_stage(
        summed, extended.reshape(2 * ext_count, height, breadth), band_count, scale_factor
    )
    reduced = jnp.transpose(red, (1, 0, 2))
    basis = basis.reshape(2, raw_count, height, breadth)
    return (basis, reduced)


def solution(mesh):
    placed = (P(None, None, "row", "col"), P(None, None, "row", "col"), P("row", "col"), P(), P())
    return jax.shard_map(
        body,
        mesh=mesh,
        in_specs=placed,
        out_specs=(P(None, None, "row", "col"), P()),
        check_vma=False,
    )
```

```python
import functools
import math

import jax
import jax.numpy as jnp
from jax import lax
from jax.experimental import pallas as pl
from jax.experimental.pallas import tpu as pltpu
from jax.sharding import PartitionSpec as P

KDEN = 16
NS_STEPS = 5


def rotate(values, phase_angle):
    cosine = jnp.cos(phase_angle)
    sine_part = jnp.sin(phase_angle)
    return jnp.stack(
        [values[0] * cosine - values[1] * sine_part, values[0] * sine_part + values[1] * cosine]
    )


def stencil(padded, stiff_pad):
    centre = stiff_pad[1:-1, 1:-1]
    upward = 0.5 * (centre + stiff_pad[:-2, 1:-1])
    downward = 0.5 * (centre + stiff_pad[2:, 1:-1])
    leftward = 0.5 * (centre + stiff_pad[1:-1, :-2])
    rightward = 0.5 * (centre + stiff_pad[1:-1, 2:])
    diagonal = upward + downward + leftward + rightward
    inner_cells = padded[:, :, 1:-1, 1:-1]
    neighbours = (
        upward * padded[:, :, :-2, 1:-1]
        + downward * padded[:, :, 2:, 1:-1]
        + leftward * padded[:, :, 1:-1, :-2]
        + rightward * padded[:, :, 1:-1, 2:]
    )
    return (diagonal * inner_cells - neighbours, diagonal)


def complex_gram(first_block, second_block):
    count = first_block.shape[1]
    first_flat = first_block.reshape((2 * count,) + first_block.shape[2:])
    second_flat = second_block.reshape((2 * count,) + second_block.shape[2:])
    products = jnp.einsum(
        "jrc,krc->jk", first_flat, second_flat, precision=lax.Precision.HIGHEST
    )
    real_part = products[:count, :count] + products[count:, count:]
    imag_part = products[:count, count:] - products[count:, :count]
    return (real_part, imag_part)


def inverse_root(gram_real, gram_imag):
    highest = lax.Precision.HIGHEST
    order_size = gram_real.shape[0]
    upper_half = jnp.concatenate([gram_real, -gram_imag], axis=1)
    lower_half = jnp.concatenate([gram_imag, gram_real], axis=1)
    embedded = jnp.concatenate([upper_half, lower_half], axis=0)
    magnitude = jnp.sqrt(jnp.sum(embedded * embedded))
    identity = jnp.eye(2 * order_size, dtype=embedded.dtype)

    def newton(turn_index, carried):
        current, inverse = carried
        factor = 1.5 * identity - 0.5 * jnp.dot(inverse, current, precision=highest)
        return (
            jnp.dot(current, factor, precision=highest),
            jnp.dot(factor, inverse, precision=highest),
        )

    current, inverse = lax.fori_loop(0, NS_STEPS, newton, (embedded / magnitude, identity))
    root_full = inverse / jnp.sqrt(magnitude)
    return (root_full[:order_size, :order_size], root_full[order_size:, :order_size])


def reduce_matrix(root_real, root_imag, ham_real, ham_imag):
    highest = lax.Precision.HIGHEST
    prod_real = jnp.dot(ham_real, root_real, precision=highest) - jnp.dot(
        ham_imag, root_imag, precision=highest
    )
    prod_imag = jnp.dot(ham_real, root_imag, precision=highest) + jnp.dot(
        ham_imag, root_real, precision=highest
    )
    red_real = jnp.dot(root_real.T, prod_real, precision=highest) + jnp.dot(
        root_imag.T, prod_imag, precision=highest
    )
    red_imag = jnp.dot(root_real.T, prod_imag, precision=highest) - jnp.dot(
        root_imag.T, prod_real, precision=highest
    )
    return jnp.stack([red_real, red_imag])


def rotate_basis(raw_basis, root_real, root_imag, scale_factor):
    highest = lax.Precision.HIGHEST
    basis_real = jnp.einsum("jrc,jk->krc", raw_basis[0], root_real, precision=highest) - jnp.einsum(
        "jrc,jk->krc", raw_basis[1], root_imag, precision=highest
    )
    basis_imag = jnp.einsum("jrc,jk->krc", raw_basis[0], root_imag, precision=highest) + jnp.einsum(
        "jrc,jk->krc", raw_basis[1], root_real, precision=highest
    )
    return scale_factor * jnp.stack([basis_real, basis_imag])


def project_mixing(mixing, matrix):
    highest = lax.Precision.HIGHEST
    return jnp.dot(mixing.T, jnp.dot(matrix, mixing, precision=highest), precision=highest)


def exchange_rim(cells, axis, dim, width, strips=None, angle=None):
    count = lax.axis_size(axis)
    if strips is None:
        head = lax.slice_in_dim(cells, 0, width, axis=dim)
        tail = lax.slice_in_dim(cells, cells.shape[dim] - width, cells.shape[dim], axis=dim)
    else:
        head, tail = strips
    if count % 2:
        before = lax.ppermute(tail.reshape(-1), axis, [(i, (i + 1) % count) for i in range(count)])
        after = lax.ppermute(head.reshape(-1), axis, [((i + 1) % count, i) for i in range(count)])
    else:
        even = lax.axis_index(axis) % 2 == 0
        first = lax.ppermute(
            jnp.where(even, tail, head).reshape(-1), axis, [(i, i ^ 1) for i in range(count)]
        )
        second = lax.ppermute(
            jnp.where(even, head, tail).reshape(-1),
            axis,
            [(i, (i + 1) % count if i % 2 else (i - 1) % count) for i in range(count)],
        )
        before = jnp.where(even, second, first)
        after = jnp.where(even, first, second)
    if angle is not None:
        index = lax.axis_index(axis)
        before = turn_flat(before, jnp.where(index == 0, -angle, 0.0), cells.shape[0])
        after = turn_flat(after, jnp.where(index == count - 1, angle, 0.0), cells.shape[0])
    before = before.reshape(tail.shape)
    after = after.reshape(head.shape)
    return jnp.concatenate([before, cells, after], axis=dim)


def turn_flat(flat, phase_angle, channels):
    share = flat.shape[0] // channels
    half = (channels - 1) // 2 * share
    turned = rotate(jnp.stack([flat[:half], flat[half : 2 * half]]), phase_angle)
    return jnp.concatenate([turned[0], turned[1], flat[2 * half :]])


def tree_sum(value, axis, radix=2, late=False):
    count = lax.axis_size(axis)
    if count & (count - 1):
        return lax.psum(value, axis)

    def swap(part, step):
        return lax.ppermute(part, axis, [(i, i ^ step) for i in range(count)])

    step = 1
    while step < count:
        if radix == 4 and 4 * step <= count and not (late and step == 1):
            value = (value + swap(value, step)) + (swap(value, 2 * step) + swap(value, 3 * step))
            step *= 4
        else:
            value = value + swap(value, step)
            step *= 2
    return value


def pack_hermitian(real_part, imag_part):
    order_size = real_part.shape[0]
    upper = jnp.arange(order_size)[:, None] <= jnp.arange(order_size)[None, :]
    return jnp.where(upper, real_part, imag_part)


def unpack_hermitian(packed):
    order_size = packed.shape[0]
    upper = jnp.arange(order_size)[:, None] <= jnp.arange(order_size)[None, :]
    strict_upper = jnp.arange(order_size)[:, None] < jnp.arange(order_size)[None, :]
    real_upper = jnp.where(upper, packed, 0.0)
    real_part = real_upper + jnp.where(strict_upper, packed, 0.0).T
    imag_lower = jnp.where(upper, 0.0, packed)
    return (real_part, imag_lower - imag_lower.T)


def matrix_kernel(packed_ref, field_ref, basis_ref, red_ref, work_ref, *, band_count, scale):
    highest = lax.Precision.HIGHEST

    def dot(first, second):
        return jnp.dot(first, second, precision=highest, preferred_element_type=jnp.float32)

    size = work_ref.shape[-1]
    ext = packed_ref.shape[-1]
    raw = 3 * band_count
    half = size // 2
    work_ref[...] = jnp.zeros(work_ref.shape, jnp.float32)
    work_ref[0, :ext, :ext] = packed_ref[0]
    work_ref[1, :ext, :ext] = packed_ref[1]
    rows = lax.broadcasted_iota(jnp.int32, (size, size), 0)
    cols = lax.broadcasted_iota(jnp.int32, (size, size), 1)
    upper = rows <= cols
    strict = rows < cols
    eye = rows == cols
    corner = (rows < half) & (cols < half)

    def spread(value, axis):
        return pltpu.roll(value, half, axis)

    def embed(real_part, imag_part):
        return real_part + spread(spread(real_part, 0), 1) - spread(imag_part, 1) + spread(imag_part, 0)

    def unpack(packed):
        real_part = jnp.where(upper, packed, 0.0) + jnp.where(strict, packed, 0.0).T
        lower = jnp.where(upper, 0.0, packed)
        return real_part, lower - lower.T

    gram_re, gram_im = unpack(work_ref[0])
    ham_re, ham_im = unpack(work_ref[1])
    band_diag = eye & (rows < band_count)
    quotient = jnp.where(band_diag, ham_re, 0.0) / jnp.where(band_diag, gram_re, 1.0)
    shifted = pltpu.roll(pltpu.roll(quotient, 2 * band_count, 0), band_count, 1)
    kept = (eye & (cols < 2 * band_count)) | (
        (rows == cols + band_count) & (cols >= 2 * band_count) & (cols < raw)
    )
    mixing = kept.astype(jnp.float32) - shifted
    mixing = mixing + spread(spread(mixing, 0), 1)
    embedded = dot(mixing.T, dot(embed(gram_re, gram_im), mixing))
    active = (rows < raw) | ((rows >= half) & (rows < half + raw))
    identity = (eye & active).astype(jnp.float32)
    total = jnp.sum(jnp.sum(embedded * embedded, axis=0, keepdims=True), axis=1, keepdims=True)
    magnitude = jnp.sqrt(total)
    current = embedded / magnitude
    inverse = identity
    for step in range(NS_STEPS):
        if step == 0:
            factor = 1.5 * identity - 0.5 * current
            current, inverse = dot(current, factor), factor
        else:
            factor = 1.5 * identity - 0.5 * dot(inverse, current)
            current, inverse = dot(current, factor), dot(factor, inverse)
    root = inverse / jnp.sqrt(magnitude)
    root = embed(jnp.where(corner, root, 0.0), jnp.where(corner, spread(root, 0), 0.0))
    rotation = dot(mixing, root)
    work_ref[1] = dot(rotation.T, dot(embed(ham_re, ham_im), rotation))
    red_ref[:, 0, :] = work_ref[1, :raw, :raw]
    red_ref[:, 1, :] = work_ref[1, half : half + raw, :raw]
    rotation = jnp.where(corner | ~((rows < half) | (cols < half)), rotation, -rotation)
    packed_rotation = jnp.where(
        cols < raw,
        rotation,
        jnp.where(cols < 2 * raw, pltpu.roll(rotation, size - half + raw, 1), 0.0),
    )
    packed_rotation = jnp.where(
        rows < ext,
        packed_rotation,
        jnp.where(rows < 2 * ext, pltpu.roll(packed_rotation, size - half + ext, 0), 0.0),
    )
    work_ref[0] = scale * packed_rotation.T
    rotation_t = work_ref[0, : 2 * raw, : 2 * ext]
    for row in range(field_ref.shape[1]):
        basis_ref[:, row, :] = dot(rotation_t, field_ref[:, row, :])


def matrix_stage(packed, fields, band_count, scale):
    size = 128
    raw = 3 * band_count
    vmem = pl.BlockSpec(memory_space=pltpu.VMEM)
    return pl.pallas_call(
        functools.partial(matrix_kernel, band_count=band_count, scale=scale),
        out_shape=(
            jax.ShapeDtypeStruct((2 * raw,) + fields.shape[1:], jnp.float32),
            jax.ShapeDtypeStruct((raw, 2, raw), jnp.float32),
        ),
        in_specs=[vmem, vmem],
        out_specs=(vmem, vmem),
        scratch_shapes=[pltpu.VMEM((2, size, size), jnp.float32)],
    )(packed, fields)


def body(bands, directions, materials, permittivity, wavevector):
    band_count = bands.shape[1]
    height = bands.shape[2]
    breadth = bands.shape[3]
    levels = jnp.arange(permittivity.shape[0], dtype=jnp.int32)

    def stiffness_of(cells):
        return jnp.sum(
            jnp.where(
                cells[None] == levels.astype(jnp.float32)[:, None, None],
                (1.0 / permittivity)[:, None, None],
                0.0,
            ),
            axis=0,
        )

    def strip_of(start, stop):
        field_rows = jnp.concatenate(
            [bands[:, :, start:stop], directions[:, :, start:stop]], axis=1
        ).reshape(4 * band_count, stop - start, breadth)
        return jnp.concatenate([field_rows, material_grid[None, start:stop]], axis=0)

    material_grid = materials.astype(jnp.float32)
    angle_row = 2.0 * math.pi * wavevector[0].astype(jnp.float32) / KDEN
    angle_col = 2.0 * math.pi * wavevector[1].astype(jnp.float32) / KDEN
    fields = jnp.concatenate([bands, directions], axis=1)
    packed = jnp.concatenate(
        [fields.reshape(4 * band_count, height, breadth), material_grid[None]], axis=0
    )
    padded = exchange_rim(
        packed, "row", 1, 2, (strip_of(0, 2), strip_of(height - 2, height)), angle_row
    )
    padded = exchange_rim(padded, "col", 2, 2, angle=angle_col)
    stiff_wide = stiffness_of(padded[-1])
    field_wide = padded[:-1].reshape(2, 2 * band_count, height + 4, breadth + 4)
    band_wide = field_wide[:, :band_count]
    applied_ring, diagonal_ring = stencil(band_wide, stiff_wide)
    stiff_ring = stiff_wide[1:-1, 1:-1]
    scaled_ring = jnp.concatenate(
        [
            applied_ring / diagonal_ring,
            band_wide[:, :, 1:-1, 1:-1] / diagonal_ring,
            field_wide[:, band_count:, 1:-1, 1:-1],
        ],
        axis=1,
    )
    extra_applied = stencil(scaled_ring, stiff_ring)[0]
    applied_cycle = applied_ring[:, :, 1:-1, 1:-1]
    scaled_image = scaled_ring[:, :band_count, 1:-1, 1:-1]
    scaled_bands = scaled_ring[:, band_count : 2 * band_count, 1:-1, 1:-1]
    extended = jnp.concatenate([bands, scaled_image, scaled_bands, directions], axis=1)
    extended_applied = jnp.concatenate([applied_cycle, extra_applied], axis=1)
    local_gram = complex_gram(extended, extended)
    local_ham = complex_gram(extended, extended_applied)
    summed = jnp.stack([pack_hermitian(*local_gram), pack_hermitian(*local_ham)])
    summed = tree_sum(tree_sum(summed.reshape(-1), "row", radix=4), "col", radix=4, late=True).reshape(summed.shape)
    raw_count = 3 * band_count
    ext_count = 4 * band_count
    scale_factor = math.sqrt(height * breadth * lax.axis_size("row") * lax.axis_size("col"))
    basis, red = matrix_stage(
        summed, extended.reshape(2 * ext_count, height, breadth), band_count, scale_factor
    )
    reduced = jnp.transpose(red, (1, 0, 2))
    basis = basis.reshape(2, raw_count, height, breadth)
    return (basis, reduced)


def solution(mesh):
    placed = (P(None, None, "row", "col"), P(None, None, "row", "col"), P("row", "col"), P(), P())
    return jax.shard_map(
        body,
        mesh=mesh,
        in_specs=placed,
        out_specs=(P(None, None, "row", "col"), P()),
        check_vma=False,
    )
```
